32 devices in a mesh: dp: 8 (over z, y), seq: 4 (over x, core).
Axes of the slice: x: 2, y: 2, z: 4, core: 2. Of those that a mesh axis runs over, the one named last changes fastest.
Arguments:
- frames: bfloat16 [8, 512, 1536], P('dp', 'seq'), may hold values from -6 to 6
- lengths: int32 [8, 4], P('dp'), may hold values from 1 to 256, 512 in all within a row
- ln1_gain: float32 [1536], replicated, may hold values from 0.5 to 12
- ln2_gain: float32 [1536], replicated, may hold values from 0.5 to 1.5
- w_qkv: bfloat16 [1536, 3, 1536], P('dp', None, 'seq'), may hold values from -0.15625 to 0.15625
- w_out: bfloat16 [1536, 1536], P('seq', 'dp'), may hold values from -0.15625 to 0.15625
- w_glu: bfloat16 [1536, 2, 1536], P('dp', None, 'seq'), may hold values from -0.15625 to 0.15625
- dw_kernel: bfloat16 [31, 1536], P(None, 'seq'), may hold values from -1 to 1
- w_proj: bfloat16 [1536, 1536], P('seq', 'dp'), may hold values from -0.15625 to 0.15625
Outputs:
- block_out: bfloat16 [8, 512, 1536], P('dp', 'seq')
The draws below stay inside these ranges and needn't reach their ends.
Inputs may be any that keep to these rules, and one draw needn't show every extreme that they name: `lengths`: each row sums to 512, and its largest entry is 256.
All inputs are finite; a program needn't handle non-finite values.
Results may differ from the reference program's by a relative error of at most 0.013.
The reference program's roundings to bfloat16 on the way count: a program that leaves them out, or rounds other values in their place, can miss the bound.
Values may be sent and summed in bfloat16 or wider, within the bound.
No kernel may reach another device: no remote copies, remote signals or barrier semaphores. Data moves between devices by JAX's collectives and lax.ppermute only.
A program may use at most 64 MiB of HBM per device.

```python
import math
import jax
import jax.numpy as jnp
import numpy as np
from jax import lax

D = 1536
HD = 96
KW = 31
REC = 4
FRAMES = 512
GROUPS = 8
N_SEQ = 4


def draw_ln1_gain(key, part):
    logs = jax.random.uniform(key, (D,), jnp.float32, math.log(0.5), math.log(2.0))
    return jnp.exp(logs)


def steps_of(stream_key, extent, pieces, low, largest):
    factor_of = 1.0
    for axis_at, shards_of in pieces:
        steps = jax.random.uniform(jax.random.fold_in(jax.random.fold_in(stream_key, 6), axis_at), (shards_of,), jnp.float32, low / len(pieces), largest / len(pieces))
        factor_of = factor_of * jnp.repeat(jnp.exp(steps), extent[axis_at] // shards_of).reshape((-1,) + (1,) * (len(extent) - 1 - axis_at))
    return factor_of


def length_profile(count, total, bound, slope):
    portions = [(1 << 20) // math.isqrt(rank ** slope) + 1 for rank in range(2, count + 1)]
    surplus, given = total - bound - (count - 1), [1] * (count - 1)
    while surplus > 0:
        free = [i for i in range(count - 1) if given[i] < bound]
        mass, left = sum([portions[i] for i in free]), surplus
        for i in free:
            addition = min(bound - given[i], max(1, left * portions[i] // mass), surplus)
            given[i] = given[i] + addition
            surplus = surplus - addition
    return np.array([bound] + given)


def ragged(rng, number_of, total, limit, skew):
    if number_of == 2:
        one = jax.random.randint(rng, (), max(1, total - limit), min(limit, total - 1) + 1)
        return jnp.stack([one, total - one])
    sizes = jnp.asarray(length_profile(number_of, total, limit, skew), jnp.int32)
    pairs = (number_of - 1) // 2
    giver, sink = sizes[1:1 + 2 * pairs:2], sizes[2:2 + 2 * pairs:2]
    room = jnp.minimum(giver - 1, limit - sink)
    moved = jax.random.randint(jax.random.fold_in(rng, 1), (pairs,), 0, 1 << 20) % (room + 1)
    sizes = sizes.at[1:1 + 2 * pairs:2].set(giver - moved).at[2:2 + 2 * pairs:2].set(sink + moved)
    return sizes[jax.random.permutation(jax.random.fold_in(rng, 2), number_of)]


def scatter_about(stream_key, extent, scale, limit, cuts=(), kind=jnp.bfloat16):
    array = jax.random.normal(stream_key, extent, jnp.float32) * scale
    if len(cuts) > 0:
        array = steps_of(stream_key, extent, cuts, -0.22, 0.18) * array
    return jnp.clip(array, min=-limit, max=limit).astype(kind)


def setup_inputs(seed: int = 0) -> dict:
    key_list = jax.random.split(jax.random.key(seed), 10)
    frames = scatter_about(key_list[0], (GROUPS, FRAMES, D), 1.0, 6.0, ((0, 8), (1, 4)))
    lengths = jax.vmap(lambda own: ragged(own, REC, FRAMES, FRAMES // 2, 2))(jax.random.split(key_list[1], GROUPS)).reshape((GROUPS, REC)).astype(jnp.int32)
    ln1_gain = draw_ln1_gain(jax.random.fold_in(key_list[9], 71), 0)
    ln2_gain = jnp.clip(1.0 + 0.1 * jax.random.normal(key_list[3], (D,), jnp.float32), 0.5, 1.5)
    w_qkv = scatter_about(key_list[4], (D, 3, D), D ** -0.5, 0.15625, ((0, 8), (2, 4)))
    w_out = scatter_about(key_list[5], (D, D), D ** -0.5, 0.15625, ((0, 4), (1, 8)))
    w_glu = scatter_about(key_list[6], (D, 2, D), D ** -0.5, 0.15625, ((0, 8), (2, 4)))
    dw_kernel = scatter_about(key_list[7], (KW, D), KW ** -0.5, 1.0, ((1, 4),))
    w_proj = scatter_about(key_list[8], (D, D), D ** -0.5, 0.15625, ((0, 4), (1, 8)))
    return {"frames": frames, "lengths": lengths, "ln1_gain": ln1_gain, "ln2_gain": ln2_gain, "w_qkv": w_qkv, "w_out": w_out, "w_glu": w_glu, "dw_kernel": dw_kernel, "w_proj": w_proj}


def layer_norm(values, gain_vec):
    mean_value = lax.optimization_barrier(jnp.mean(values, axis=-1, keepdims=True))
    centered = values - mean_value
    variance = lax.optimization_barrier(jnp.mean(centered * centered, axis=-1, keepdims=True))
    return (centered * lax.rsqrt(variance + 1e-05) * gain_vec).astype(jnp.bfloat16)

def segment_of(record_ends, positions):
    return lax.optimization_barrier(jnp.sum((positions[:, None] >= record_ends[None, :]).astype(jnp.int32), axis=1)).astype(jnp.int32)

def attend(projected, seg_all, head_size):
    group_rows = projected.shape[0]
    block_rows = 512 if group_rows % 512 == 0 else group_rows
    heads_here = projected.shape[2] // head_size
    split = projected.reshape(group_rows, 3, heads_here, head_size)
    queries = split[:, 0]
    keys = split[:, 1].astype(jnp.float32)
    values = split[:, 2].astype(jnp.float32)
    blocks = group_rows // block_rows
    scale = 1.0 / head_size ** 0.5

    def one_block(block_data):
        query_block, seg_block = block_data
        scores = jnp.einsum('qhe,khe->hqk', query_block.astype(jnp.float32), keys) * scale
        allowed = seg_block[:, None] == seg_all[None, :]
        scores = jnp.where(allowed[None], scores, -1e+30)
        top_score = lax.optimization_barrier(jnp.max(scores, axis=-1, keepdims=True))
        weights = jnp.exp(scores - top_score)
        probs = (weights / lax.optimization_barrier(jnp.sum(weights, axis=-1, keepdims=True))).astype(jnp.bfloat16)
        mixed = jnp.einsum('hqk,khe->qhe', probs.astype(jnp.float32), values)
        return mixed.astype(jnp.bfloat16).reshape(block_rows, heads_here * head_size)
    result = lax.map(one_block, (queries.reshape(blocks, block_rows, heads_here, head_size), seg_all.reshape(blocks, block_rows)))
    return result.reshape(group_rows, heads_here * head_size)

def depthwise(padded, kernel, seg_here, seg_near, count):
    total_acc = jnp.zeros((count, padded.shape[1]), jnp.float32)
    for tap_index in range(kernel.shape[0]):
        window = padded[tap_index:tap_index + count].astype(jnp.float32)
        same = (seg_near[tap_index:tap_index + count] == seg_here)[:, None]
        total_acc = total_acc + jnp.where(same, window * kernel[tap_index].astype(jnp.float32), 0.0)
    return jax.nn.silu(total_acc).astype(jnp.bfloat16)

def blocked_product(left, right, blocks_count):
    block_width = left.shape[1] // blocks_count
    summed = jnp.zeros((left.shape[0], right.shape[1]), jnp.float32)
    for block_index in range(blocks_count):
        lo_col = block_index * block_width
        partial_sum = jnp.dot(left[:, lo_col:lo_col + block_width], right[lo_col:lo_col + block_width], preferred_element_type=jnp.float32)
        summed = summed + partial_sum.astype(jnp.bfloat16).astype(jnp.float32)
    return summed

def reference(frames, lengths, ln1_gain, ln2_gain, w_qkv, w_out, w_glu, dw_kernel, w_proj):
    reach = KW // 2

    def one_group(group_data):
        frames_group, lengths_group = group_data
        inputs = frames_group.astype(jnp.float32)
        record_ends = jnp.cumsum(lengths_group).astype(jnp.int32)
        positions = jnp.arange(FRAMES, dtype=jnp.int32)
        seg_all = segment_of(record_ends, positions)
        normed1 = layer_norm(inputs, ln1_gain)
        projected = jnp.dot(normed1, w_qkv.reshape(D, 3 * D), preferred_element_type=jnp.float32).astype(jnp.bfloat16).reshape(FRAMES, 3, D)
        attended = attend(projected, seg_all, HD)
        middle = (inputs + blocked_product(attended, w_out, N_SEQ)).astype(jnp.bfloat16)
        normed2 = layer_norm(middle.astype(jnp.float32), ln2_gain)
        paired = jnp.dot(normed2, w_glu.reshape(D, 2 * D), preferred_element_type=jnp.float32).reshape(FRAMES, 2, D)
        gated = (paired[:, 0] * jax.nn.sigmoid(paired[:, 1])).astype(jnp.bfloat16)
        padded = jnp.pad(gated, ((reach, reach), (0, 0)))
        near_positions = jnp.arange(-reach, FRAMES + reach, dtype=jnp.int32)
        activated = depthwise(padded, dw_kernel, seg_all, segment_of(record_ends, near_positions), FRAMES)
        conv_out = blocked_product(activated, w_proj, N_SEQ)
        return (middle.astype(jnp.float32) + conv_out).astype(jnp.bfloat16)
    return lax.map(one_group, (frames, lengths))
```

```python
import jax
import jax.numpy as jnp
from jax import lax
from jax.sharding import PartitionSpec as P

HD = 96


def layer_norm(values, gain_vec):
    mean_value = jnp.mean(values, axis=-1, keepdims=True)
    centered = values - mean_value
    variance = jnp.mean(centered * centered, axis=-1, keepdims=True)
    return (centered * lax.rsqrt(variance + 1e-05) * gain_vec).astype(jnp.bfloat16)


def segment_of(record_ends, positions):
    return jnp.sum((positions[:, None] >= record_ends[None, :]).astype(jnp.int32), axis=1)


def seq_gather(block):
    count = lax.axis_size("seq")
    me = lax.axis_index("seq")
    parts = [block]
    for shift in range(1, count):
        parts.append(
            lax.ppermute(block, "seq", [(i, (i - shift) % count) for i in range(count)])
        )
    ring = jnp.concatenate(parts + parts, axis=0)
    rows = block.shape[0]
    return lax.dynamic_slice_in_dim(ring, ((count - me) % count) * rows, count * rows, axis=0)


def seq_scatter_sum(full):
    count = lax.axis_size("seq")
    me = lax.axis_index("seq")
    rows = full.shape[0] // count
    total = lax.dynamic_slice_in_dim(full, me * rows, rows, axis=0).astype(jnp.float32)
    for shift in range(1, count):
        piece = lax.dynamic_slice_in_dim(full, ((me + shift) % count) * rows, rows, axis=0)
        got = lax.ppermute(piece, "seq", [(i, (i + shift) % count) for i in range(count)])
        total = total + got.astype(jnp.float32)
    return total


def attend(projected, seg_all, head_size):
    group_rows = projected.shape[0]
    block_rows = 512
    heads_here = projected.shape[2] // head_size
    split = projected.reshape(group_rows, 3, heads_here, head_size)
    queries = split[:, 0]
    keys = split[:, 1]
    values = split[:, 2]
    blocks = group_rows // block_rows
    scale = 1.0 / head_size**0.5

    def one_block(block_data):
        query_block, seg_block = block_data
        scores = (
            jnp.einsum("qhe,khe->hqk", query_block, keys, preferred_element_type=jnp.float32)
            * scale
        )
        allowed = seg_block[:, None] == seg_all[None, :]
        scores = jnp.where(allowed[None], scores, -1e30)
        top_score = jnp.max(scores, axis=-1, keepdims=True)
        weights = jnp.exp(scores - top_score)
        probs = (weights / jnp.sum(weights, axis=-1, keepdims=True)).astype(jnp.bfloat16)
        mixed = jnp.einsum("hqk,khe->qhe", probs, values, preferred_element_type=jnp.float32)
        return mixed.astype(jnp.bfloat16).reshape(block_rows, heads_here * head_size)

    result = lax.map(
        one_block,
        (
            queries.reshape(blocks, block_rows, heads_here, head_size),
            seg_all.reshape(blocks, block_rows),
        ),
    )
    return result.reshape(group_rows, heads_here * head_size)


def depthwise(padded, kernel, seg_here, seg_near, count):
    total_acc = jnp.zeros((count, padded.shape[1]), jnp.float32)
    for tap_index in range(kernel.shape[0]):
        window = padded[tap_index : tap_index + count].astype(jnp.float32)
        same = (seg_near[tap_index : tap_index + count] == seg_here)[:, None]
        total_acc = total_acc + jnp.where(same, window * kernel[tap_index].astype(jnp.float32), 0.0)
    return jax.nn.silu(total_acc).astype(jnp.bfloat16)


def on_device(frames, lengths, ln1_gain, ln2_gain, w_qkv, w_out, w_glu, dw_kernel, w_proj):
    frame_rows = frames.shape[1]
    model_width = frames.shape[2]
    seq_count = lax.axis_size("seq")
    group_rows = frame_rows * seq_count
    group_width = model_width // seq_count
    kernel_reach = dw_kernel.shape[0] // 2
    qkv_matrix = lax.all_gather(
        w_qkv.reshape(w_qkv.shape[0], 3 * group_width), "dp", axis=0, tiled=True
    )
    out_local = lax.all_gather(w_out, "dp", axis=1, tiled=True)
    glu_matrix = lax.all_gather(
        w_glu.reshape(w_glu.shape[0], 2 * group_width), "dp", axis=0, tiled=True
    )
    proj_local = lax.all_gather(w_proj, "dp", axis=1, tiled=True)
    inputs = frames[0].astype(jnp.float32)
    record_ends = jnp.cumsum(lengths[0])
    seg_all = segment_of(record_ends, jnp.arange(group_rows, dtype=jnp.int32))
    normed1 = layer_norm(inputs, ln1_gain)
    projected = (
        jnp.dot(seq_gather(normed1), qkv_matrix, preferred_element_type=jnp.float32)
        .astype(jnp.bfloat16)
        .reshape(group_rows, 3, group_width)
    )
    attended = attend(projected, seg_all, HD)
    attn_sum = seq_scatter_sum(
        jnp.dot(attended, out_local, preferred_element_type=jnp.float32).astype(jnp.bfloat16)
    )
    middle = (inputs + attn_sum).astype(jnp.bfloat16)
    normed2 = layer_norm(middle.astype(jnp.float32), ln2_gain)
    shard_piece = seq_gather(normed2)
    paired = jnp.dot(shard_piece, glu_matrix, preferred_element_type=jnp.float32).reshape(
        shard_piece.shape[0], 2, group_width
    )
    gated = (paired[:, 0] * jax.nn.sigmoid(paired[:, 1])).astype(jnp.bfloat16)
    padded = jnp.pad(gated, ((kernel_reach, kernel_reach), (0, 0)))
    near_positions = jnp.arange(-kernel_reach, group_rows + kernel_reach, dtype=jnp.int32)
    activated = depthwise(
        padded, dw_kernel, seg_all, segment_of(record_ends, near_positions), group_rows
    )
    conv_out = seq_scatter_sum(
        jnp.dot(activated, proj_local, preferred_element_type=jnp.float32).astype(jnp.bfloat16)
    )
    results = [(middle.astype(jnp.float32) + conv_out).astype(jnp.bfloat16)]
    return jnp.stack(results, axis=0)


def solution(mesh):
    in_specs = (
        P("dp", "seq", None),
        P("dp", None),
        P(),
        P(),
        P("dp", None, "seq"),
        P("seq", "dp"),
        P("dp", None, "seq"),
        P(None, "seq"),
        P("seq", "dp"),
    )
    out_specs = P("dp", "seq", None)
    return jax.shard_map(
        on_device, mesh=mesh, in_specs=in_specs, out_specs=out_specs, check_vma=False
    )
```

```python
import functools

import jax
import jax.numpy as jnp
from jax import lax
from jax.sharding import PartitionSpec as P

HD = 96


def layer_norm(values, gain_vec):
    mean_value = jnp.mean(values, axis=-1, keepdims=True)
    centered = values - mean_value
    variance = jnp.mean(centered * centered, axis=-1, keepdims=True)
    return (centered * lax.rsqrt(variance + 1e-05) * gain_vec).astype(jnp.bfloat16)


def segment_of(record_ends, positions):
    return jnp.sum((positions[:, None] >= record_ends[None, :]).astype(jnp.int32), axis=1)


def seq_gather(block):
    count = lax.axis_size("seq")
    me = lax.axis_index("seq")
    parts = [block]
    for shift in range(1, count):
        parts.append(
            lax.ppermute(block, "seq", [(i, (i - shift) % count) for i in range(count)])
        )
    ring = jnp.concatenate(parts + parts, axis=0)
    rows = block.shape[0]
    return lax.dynamic_slice_in_dim(ring, ((count - me) % count) * rows, count * rows, axis=0)


def seq_scatter_sum(full):
    count = lax.axis_size("seq")
    me = lax.axis_index("seq")
    rows = full.shape[0] // count
    total = lax.dynamic_slice_in_dim(full, me * rows, rows, axis=0).astype(jnp.float32)
    for shift in range(1, count):
        piece = lax.dynamic_slice_in_dim(full, ((me + shift) % count) * rows, rows, axis=0)
        got = lax.ppermute(piece, "seq", [(i, (i + shift) % count) for i in range(count)])
        total = total + got.astype(jnp.float32)
    return total


def dp_ring(mesh):
    count = mesh.shape["dp"]
    plain = list(range(count))
    try:
        coords = [tuple(int(c) for c in d.coords) for d in mesh.devices[:, 0]]
    except (AttributeError, TypeError, IndexError):
        return plain
    axes = [k for k in range(len(coords[0])) if len({c[k] for c in coords}) > 1]
    if len(axes) != 2:
        return plain
    low = [min(c[k] for c in coords) for k in axes]
    spots = {(c[axes[0]] - low[0], c[axes[1]] - low[1]): i for i, c in enumerate(coords)}
    sizes = [len({c[k] for c in coords}) for k in axes]
    if sizes[0] * sizes[1] != count or len(spots) != count:
        return plain
    if sizes[0] % 2 == 0:
        first, second, swap = sizes[0], sizes[1], False
    elif sizes[1] % 2 == 0:
        first, second, swap = sizes[1], sizes[0], True
    else:
        return plain
    path = [(0, 0)]
    for a in range(first):
        cols = range(1, second) if a % 2 == 0 else range(second - 1, 0, -1)
        path += [(a, b) for b in cols]
    path += [(a, 0) for a in range(first - 1, 0, -1)]
    if swap:
        path = [(b, a) for a, b in path]
    cycle = [spots.get(p) for p in path]
    if None in cycle or sorted(cycle) != plain:
        return plain
    return cycle


def ring_gather(block, ring):
    count = len(ring)
    me = lax.axis_index("dp")
    my_pos = jnp.asarray([ring.index(i) for i in range(count)], jnp.int32)[me]
    order = jnp.asarray(ring, jnp.int32)
    forward = [(ring[p], ring[(p + 1) % count]) for p in range(count)]
    backward = [(ring[p], ring[(p - 1) % count]) for p in range(count)]
    out = jnp.zeros((count,) + block.shape, block.dtype)
    out = lax.dynamic_update_index_in_dim(out, block, me, 0)
    ahead = behind = block
    for step in range(1, count // 2 + 1):
        ahead = lax.ppermute(ahead, "dp", forward)
        out = lax.dynamic_update_index_in_dim(out, ahead, order[(my_pos - step) % count], 0)
        if step <= count - 1 - count // 2:
            behind = lax.ppermute(behind, "dp", backward)
            out = lax.dynamic_update_index_in_dim(out, behind, order[(my_pos + step) % count], 0)
    return out


def after(token, value):
    return lax.optimization_barrier((token, value))[1]


def attend(projected, seg_all, head_size):
    group_rows = projected.shape[0]
    block_rows = 512
    heads_here = projected.shape[2] // head_size
    split = projected.reshape(group_rows, 3, heads_here, head_size)
    queries = split[:, 0]
    keys = split[:, 1]
    values = split[:, 2]
    blocks = group_rows // block_rows
    scale = 1.0 / head_size**0.5

    def one_block(block_data):
        query_block, seg_block = block_data
        scores = (
            jnp.einsum("qhe,khe->hqk", query_block, keys, preferred_element_type=jnp.float32)
            * scale
        )
        allowed = seg_block[:, None] == seg_all[None, :]
        scores = jnp.where(allowed[None], scores, -1e30)
        top_score = jnp.max(scores, axis=-1, keepdims=True)
        weights = jnp.exp(scores - top_score)
        probs = (weights / jnp.sum(weights, axis=-1, keepdims=True)).astype(jnp.bfloat16)
        mixed = jnp.einsum("hqk,khe->qhe", probs, values, preferred_element_type=jnp.float32)
        return mixed.astype(jnp.bfloat16).reshape(block_rows, heads_here * head_size)

    result = lax.map(
        one_block,
        (
            queries.reshape(blocks, block_rows, heads_here, head_size),
            seg_all.reshape(blocks, block_rows),
        ),
    )
    return result.reshape(group_rows, heads_here * head_size)


def depthwise(padded, kernel, seg_here, seg_near, count):
    total_acc = jnp.zeros((count, padded.shape[1]), jnp.float32)
    for tap_index in range(kernel.shape[0]):
        window = padded[tap_index : tap_index + count].astype(jnp.float32)
        same = (seg_near[tap_index : tap_index + count] == seg_here)[:, None]
        total_acc = total_acc + jnp.where(same, window * kernel[tap_index].astype(jnp.float32), 0.0)
    return jax.nn.silu(total_acc).astype(jnp.bfloat16)


def on_device(ring, frames, lengths, ln1_gain, ln2_gain, w_qkv, w_out, w_glu, dw_kernel, w_proj):
    frame_rows = frames.shape[1]
    model_width = frames.shape[2]
    seq_count = lax.axis_size("seq")
    group_rows = frame_rows * seq_count
    group_width = model_width // seq_count
    kernel_reach = dw_kernel.shape[0] // 2
    qkv_parts = ring_gather(w_qkv.reshape(w_qkv.shape[0], 3 * group_width), ring)
    qkv_matrix = qkv_parts.reshape(model_width, 3 * group_width)
    out_parts = ring_gather(after(qkv_parts, w_out), ring)
    out_local = jnp.einsum("nrc->rnc", out_parts).reshape(w_out.shape[0], model_width)
    glu_parts = ring_gather(after(out_parts, w_glu.reshape(w_glu.shape[0], 2 * group_width)), ring)
    glu_matrix = glu_parts.reshape(model_width, 2 * group_width)
    proj_parts = ring_gather(after(glu_parts, w_proj), ring)
    proj_local = jnp.einsum("nrc->rnc", proj_parts).reshape(w_proj.shape[0], model_width)
    inputs = frames[0].astype(jnp.float32)
    record_ends = jnp.cumsum(lengths[0])
    seg_all = segment_of(record_ends, jnp.arange(group_rows, dtype=jnp.int32))
    normed1 = layer_norm(inputs, ln1_gain)
    projected = (
        jnp.dot(seq_gather(normed1), qkv_matrix, preferred_element_type=jnp.float32)
        .astype(jnp.bfloat16)
        .reshape(group_rows, 3, group_width)
    )
    attended = attend(projected, seg_all, HD)
    attn_sum = seq_scatter_sum(
        jnp.dot(attended, out_local, preferred_element_type=jnp.float32).astype(jnp.bfloat16)
    )
    middle = (inputs + attn_sum).astype(jnp.bfloat16)
    normed2 = layer_norm(middle.astype(jnp.float32), ln2_gain)
    shard_piece = seq_gather(normed2)
    paired = jnp.dot(shard_piece, glu_matrix, preferred_element_type=jnp.float32).reshape(
        shard_piece.shape[0], 2, group_width
    )
    gated = (paired[:, 0] * jax.nn.sigmoid(paired[:, 1])).astype(jnp.bfloat16)
    padded = jnp.pad(gated, ((kernel_reach, kernel_reach), (0, 0)))
    near_positions = jnp.arange(-kernel_reach, group_rows + kernel_reach, dtype=jnp.int32)
    activated = depthwise(
        padded, dw_kernel, seg_all, segment_of(record_ends, near_positions), group_rows
    )
    conv_out = seq_scatter_sum(
        jnp.dot(activated, proj_local, preferred_element_type=jnp.float32).astype(jnp.bfloat16)
    )
    results = [(middle.astype(jnp.float32) + conv_out).astype(jnp.bfloat16)]
    return jnp.stack(results, axis=0)


def solution(mesh):
    in_specs = (
        P("dp", "seq", None),
        P("dp", None),
        P(),
        P(),
        P("dp", None, "seq"),
        P("seq", "dp"),
        P("dp", None, "seq"),
        P(None, "seq"),
        P("seq", "dp"),
    )
    out_specs = P("dp", "seq", None)
    return jax.shard_map(
        functools.partial(on_device, dp_ring(mesh)), mesh=mesh, in_specs=in_specs, out_specs=out_specs, check_vma=False
    )
```

```python
import functools

import jax
import jax.numpy as jnp
from jax import lax
from jax.sharding import PartitionSpec as P

HD = 96


def layer_norm(values, gain_vec):
    mean_value = jnp.mean(values, axis=-1, keepdims=True)
    centered = values - mean_value
    variance = jnp.mean(centered * centered, axis=-1, keepdims=True)
    return (centered * lax.rsqrt(variance + 1e-05) * gain_vec).astype(jnp.bfloat16)


def segment_of(record_ends, positions):
    return jnp.sum((positions[:, None] >= record_ends[None, :]).astype(jnp.int32), axis=1)


def seq_gather(block, paired):
    count = lax.axis_size("seq")
    me = lax.axis_index("seq")
    out = jnp.zeros((count,) + block.shape, block.dtype)
    out = lax.dynamic_update_index_in_dim(out, block, me, 0)
    if not paired:
        for shift in range(1, count):
            got = lax.ppermute(block, "seq", [(i, (i + shift) % count) for i in range(count)])
            out = lax.dynamic_update_index_in_dim(out, got, (me - shift) % count, 0)
        return out
    half = count // 2
    mine = jnp.zeros((half,) + block.shape, block.dtype)
    mine = lax.dynamic_update_index_in_dim(mine, block, me // 2, 0)
    for shift in range(1, half):
        got = lax.ppermute(
            block, "seq", [(i, (i + 2 * shift) % count) for i in range(count)]
        )
        src_dev = (me - 2 * shift) % count
        mine = lax.dynamic_update_index_in_dim(mine, got, src_dev // 2, 0)
        out = lax.dynamic_update_index_in_dim(out, got, src_dev, 0)
    other = lax.ppermute(mine, "seq", [(i, i ^ 1) for i in range(count)])
    partner = me ^ 1
    for k in range(half):
        out = lax.dynamic_update_index_in_dim(out, other[k], 2 * k + partner % 2, 0)
    return out


def cores_paired(mesh):
    count = mesh.shape["seq"]
    if count % 2:
        return False
    try:
        row = mesh.devices[0]
        return all(
            tuple(row[2 * k].coords) == tuple(row[2 * k + 1].coords) for k in range(count // 2)
        )
    except (AttributeError, TypeError, IndexError):
        return False


def seq_scatter_sum(full):
    count = lax.axis_size("seq")
    me = lax.axis_index("seq")
    rows = full.shape[0] // count
    total = lax.dynamic_slice_in_dim(full, me * rows, rows, axis=0).astype(jnp.float32)
    for shift in range(1, count):
        piece = lax.dynamic_slice_in_dim(full, ((me + shift) % count) * rows, rows, axis=0)
        got = lax.ppermute(piece, "seq", [(i, (i + shift) % count) for i in range(count)])
        total = total + got.astype(jnp.float32)
    return total


def dp_ring(mesh):
    count = mesh.shape["dp"]
    plain = list(range(count))
    try:
        coords = [tuple(int(c) for c in d.coords) for d in mesh.devices[:, 0]]
    except (AttributeError, TypeError, IndexError):
        return plain
    axes = [k for k in range(len(coords[0])) if len({c[k] for c in coords}) > 1]
    if len(axes) != 2:
        return plain
    low = [min(c[k] for c in coords) for k in axes]
    spots = {(c[axes[0]] - low[0], c[axes[1]] - low[1]): i for i, c in enumerate(coords)}
    sizes = [len({c[k] for c in coords}) for k in axes]
    if sizes[0] * sizes[1] != count or len(spots) != count:
        return plain
    if sizes[0] % 2 == 0:
        first, second, swap = sizes[0], sizes[1], False
    elif sizes[1] % 2 == 0:
        first, second, swap = sizes[1], sizes[0], True
    else:
        return plain
    path = [(0, 0)]
    for a in range(first):
        cols = range(1, second) if a % 2 == 0 else range(second - 1, 0, -1)
        path += [(a, b) for b in cols]
    path += [(a, 0) for a in range(first - 1, 0, -1)]
    if swap:
        path = [(b, a) for a, b in path]
    cycle = [spots.get(p) for p in path]
    if None in cycle or sorted(cycle) != plain:
        return plain
    return cycle


def ring_gather(block, ring):
    count = len(ring)
    me = lax.axis_index("dp")
    my_pos = jnp.asarray([ring.index(i) for i in range(count)], jnp.int32)[me]
    order = jnp.asarray(ring, jnp.int32)
    forward = [(ring[p], ring[(p + 1) % count]) for p in range(count)]
    backward = [(ring[p], ring[(p - 1) % count]) for p in range(count)]
    out = jnp.zeros((count,) + block.shape, block.dtype)
    out = lax.dynamic_update_index_in_dim(out, block, me, 0)
    ahead = behind = block
    for step in range(1, count // 2 + 1):
        ahead = lax.ppermute(ahead, "dp", forward)
        out = lax.dynamic_update_index_in_dim(out, ahead, order[(my_pos - step) % count], 0)
        if step <= count - 1 - count // 2:
            behind = lax.ppermute(behind, "dp", backward)
            out = lax.dynamic_update_index_in_dim(out, behind, order[(my_pos + step) % count], 0)
    return out


def after(token, value):
    return lax.optimization_barrier((token, value))[1]


def attend(projected, seg_all, head_size):
    group_rows = projected.shape[0]
    block_rows = 512
    heads_here = projected.shape[2] // head_size
    split = projected.reshape(group_rows, 3, heads_here, head_size)
    queries = split[:, 0]
    keys = split[:, 1]
    values = split[:, 2]
    blocks = group_rows // block_rows
    scale = 1.0 / head_size**0.5

    def one_block(block_data):
        query_block, seg_block = block_data
        scores = (
            jnp.einsum("qhe,khe->hqk", query_block, keys, preferred_element_type=jnp.float32)
            * scale
        )
        allowed = seg_block[:, None] == seg_all[None, :]
        scores = jnp.where(allowed[None], scores, -1e30)
        top_score = jnp.max(scores, axis=-1, keepdims=True)
        weights = jnp.exp(scores - top_score)
        probs = (weights / jnp.sum(weights, axis=-1, keepdims=True)).astype(jnp.bfloat16)
        mixed = jnp.einsum("hqk,khe->qhe", probs, values, preferred_element_type=jnp.float32)
        return mixed.astype(jnp.bfloat16).reshape(block_rows, heads_here * head_size)

    result = lax.map(
        one_block,
        (
            queries.reshape(blocks, block_rows, heads_here, head_size),
            seg_all.reshape(blocks, block_rows),
        ),
    )
    return result.reshape(group_rows, heads_here * head_size)


def depthwise(padded, kernel, seg_here, seg_near, count):
    total_acc = jnp.zeros((count, padded.shape[1]), jnp.float32)
    for tap_index in range(kernel.shape[0]):
        window = padded[tap_index : tap_index + count].astype(jnp.float32)
        same = (seg_near[tap_index : tap_index + count] == seg_here)[:, None]
        total_acc = total_acc + jnp.where(same, window * kernel[tap_index].astype(jnp.float32), 0.0)
    return jax.nn.silu(total_acc).astype(jnp.bfloat16)


def on_device(ring, paired, frames, lengths, ln1_gain, ln2_gain, w_qkv, w_out, w_glu, dw_kernel, w_proj):
    frame_rows = frames.shape[1]
    model_width = frames.shape[2]
    seq_count = lax.axis_size("seq")
    group_rows = frame_rows * seq_count
    group_width = model_width // seq_count
    kernel_reach = dw_kernel.shape[0] // 2
    qkv_parts = ring_gather(w_qkv.reshape(w_qkv.shape[0], 3 * group_width), ring)
    qkv_matrix = qkv_parts.reshape(model_width, 3 * group_width)
    out_parts = ring_gather(after(qkv_parts, w_out), ring)
    out_local = jnp.einsum("nrc->rnc", out_parts).reshape(w_out.shape[0], model_width)
    glu_parts = ring_gather(after(out_parts, w_glu.reshape(w_glu.shape[0], 2 * group_width)), ring)
    glu_matrix = glu_parts.reshape(model_width, 2 * group_width)
    proj_parts = ring_gather(after(glu_parts, w_proj), ring)
    proj_local = jnp.einsum("nrc->rnc", proj_parts).reshape(w_proj.shape[0], model_width)
    inputs = frames[0].astype(jnp.float32)
    record_ends = jnp.cumsum(lengths[0])
    seg_all = segment_of(record_ends, jnp.arange(group_rows, dtype=jnp.int32))
    normed1 = layer_norm(inputs, ln1_gain)
    projected = (
        jnp.dot(seq_gather(normed1, paired).reshape(group_rows, model_width), qkv_matrix, preferred_element_type=jnp.float32)
        .astype(jnp.bfloat16)
        .reshape(group_rows, 3, group_width)
    )
    attended = attend(projected, seg_all, HD)
    attn_sum = seq_scatter_sum(
        jnp.dot(attended, out_local, preferred_element_type=jnp.float32).astype(jnp.bfloat16)
    )
    middle = (inputs + attn_sum).astype(jnp.bfloat16)
    normed2 = layer_norm(middle.astype(jnp.float32), ln2_gain)
    shard_piece = seq_gather(normed2, paired).reshape(group_rows, model_width)
    glu_pair = jnp.dot(shard_piece, glu_matrix, preferred_element_type=jnp.float32).reshape(
        shard_piece.shape[0], 2, group_width
    )
    gated = (glu_pair[:, 0] * jax.nn.sigmoid(glu_pair[:, 1])).astype(jnp.bfloat16)
    padded = jnp.pad(gated, ((kernel_reach, kernel_reach), (0, 0)))
    near_positions = jnp.arange(-kernel_reach, group_rows + kernel_reach, dtype=jnp.int32)
    activated = depthwise(
        padded, dw_kernel, seg_all, segment_of(record_ends, near_positions), group_rows
    )
    conv_out = seq_scatter_sum(
        jnp.dot(activated, proj_local, preferred_element_type=jnp.float32).astype(jnp.bfloat16)
    )
    results = [(middle.astype(jnp.float32) + conv_out).astype(jnp.bfloat16)]
    return jnp.stack(results, axis=0)


def solution(mesh):
    in_specs = (
        P("dp", "seq", None),
        P("dp", None),
        P(),
        P(),
        P("dp", None, "seq"),
        P("seq", "dp"),
        P("dp", None, "seq"),
        P(None, "seq"),
        P("seq", "dp"),
    )
    out_specs = P("dp", "seq", None)
    return jax.shard_map(
        functools.partial(on_device, dp_ring(mesh), cores_paired(mesh)), mesh=mesh, in_specs=in_specs, out_specs=out_specs, check_vma=False
    )
```

```python
import functools

import jax
import jax.numpy as jnp
from jax import lax
from jax.sharding import PartitionSpec as P

HD = 96


def layer_norm(values, gain_vec):
    mean_value = jnp.mean(values, axis=-1, keepdims=True)
    centered = values - mean_value
    variance = jnp.mean(centered * centered, axis=-1, keepdims=True)
    return (centered * lax.rsqrt(variance + 1e-05) * gain_vec).astype(jnp.bfloat16)


def segment_of(record_ends, positions):
    return jnp.sum((positions[:, None] >= record_ends[None, :]).astype(jnp.int32), axis=1)


def seq_gather(block, paired):
    count = lax.axis_size("seq")
    me = lax.axis_index("seq")
    out = jnp.zeros((count,) + block.shape, block.dtype)
    out = lax.dynamic_update_index_in_dim(out, block, me, 0)
    if not paired:
        for shift in range(1, count):
            got = lax.ppermute(block, "seq", [(i, (i + shift) % count) for i in range(count)])
            out = lax.dynamic_update_index_in_dim(out, got, (me - shift) % count, 0)
        return out
    half = count // 2
    mine = jnp.zeros((half,) + block.shape, block.dtype)
    mine = lax.dynamic_update_index_in_dim(mine, block, me // 2, 0)
    for shift in range(1, half):
        got = lax.ppermute(
            block, "seq", [(i, (i + 2 * shift) % count) for i in range(count)]
        )
        src_dev = (me - 2 * shift) % count
        mine = lax.dynamic_update_index_in_dim(mine, got, src_dev // 2, 0)
        out = lax.dynamic_update_index_in_dim(out, got, src_dev, 0)
    other = lax.ppermute(mine, "seq", [(i, i ^ 1) for i in range(count)])
    partner = me ^ 1
    for k in range(half):
        out = lax.dynamic_update_index_in_dim(out, other[k], 2 * k + partner % 2, 0)
    return out


def cores_paired(mesh):
    count = mesh.shape["seq"]
    if count % 2:
        return False
    try:
        row = mesh.devices[0]
        return all(
            tuple(row[2 * k].coords) == tuple(row[2 * k + 1].coords) for k in range(count // 2)
        )
    except (AttributeError, TypeError, IndexError):
        return False


def seq_scatter_sum(full):
    count = lax.axis_size("seq")
    me = lax.axis_index("seq")
    rows = full.shape[0] // count
    total = lax.dynamic_slice_in_dim(full, me * rows, rows, axis=0).astype(jnp.float32)
    for shift in range(1, count):
        piece = lax.dynamic_slice_in_dim(full, ((me + shift) % count) * rows, rows, axis=0)
        got = lax.ppermute(piece, "seq", [(i, (i + shift) % count) for i in range(count)])
        total = total + got.astype(jnp.float32)
    return total


def dp_ring(mesh):
    count = mesh.shape["dp"]
    plain = list(range(count))
    try:
        coords = [tuple(int(c) for c in d.coords) for d in mesh.devices[:, 0]]
    except (AttributeError, TypeError, IndexError):
        return plain
    axes = [k for k in range(len(coords[0])) if len({c[k] for c in coords}) > 1]
    if len(axes) != 2:
        return plain
    low = [min(c[k] for c in coords) for k in axes]
    spots = {(c[axes[0]] - low[0], c[axes[1]] - low[1]): i for i, c in enumerate(coords)}
    sizes = [len({c[k] for c in coords}) for k in axes]
    if sizes[0] * sizes[1] != count or len(spots) != count:
        return plain
    if sizes[0] % 2 == 0:
        first, second, swap = sizes[0], sizes[1], False
    elif sizes[1] % 2 == 0:
        first, second, swap = sizes[1], sizes[0], True
    else:
        return plain
    path = [(0, 0)]
    for a in range(first):
        cols = range(1, second) if a % 2 == 0 else range(second - 1, 0, -1)
        path += [(a, b) for b in cols]
    path += [(a, 0) for a in range(first - 1, 0, -1)]
    if swap:
        path = [(b, a) for a, b in path]
    cycle = [spots.get(p) for p in path]
    if None in cycle or sorted(cycle) != plain:
        return plain
    return cycle


def ring_gather(block, ring):
    count = len(ring)
    me = lax.axis_index("dp")
    my_pos = jnp.asarray([ring.index(i) for i in range(count)], jnp.int32)[me]
    order = jnp.asarray(ring, jnp.int32)
    forward = [(ring[p], ring[(p + 1) % count]) for p in range(count)]
    backward = [(ring[p], ring[(p - 1) % count]) for p in range(count)]
    out = jnp.zeros((count,) + block.shape, block.dtype)
    out = lax.dynamic_update_index_in_dim(out, block, me, 0)
    ahead = behind = block
    for step in range(1, count // 2 + 1):
        ahead = lax.ppermute(ahead, "dp", forward)
        out = lax.dynamic_update_index_in_dim(out, ahead, order[(my_pos - step) % count], 0)
        if step <= count - 1 - count // 2:
            behind = lax.ppermute(behind, "dp", backward)
            out = lax.dynamic_update_index_in_dim(out, behind, order[(my_pos + step) % count], 0)
    return out


def after(token, value):
    return lax.optimization_barrier((token, value))[1]


def attend(query_rows, kv_rows, seg_all, head_size):
    group_rows = query_rows.shape[0]
    block_rows = 512
    heads_here = query_rows.shape[1] // head_size
    queries = query_rows.reshape(group_rows, heads_here, head_size)
    split = kv_rows.reshape(group_rows, 2, heads_here, head_size)
    keys = split[:, 0]
    values = split[:, 1]
    blocks = group_rows // block_rows
    scale = 1.0 / head_size**0.5

    def one_block(block_data):
        query_block, seg_block = block_data
        scores = (
            jnp.einsum("qhe,khe->hqk", query_block, keys, preferred_element_type=jnp.float32)
            * scale
        )
        allowed = seg_block[:, None] == seg_all[None, :]
        scores = jnp.where(allowed[None], scores, -1e30)
        top_score = jnp.max(scores, axis=-1, keepdims=True)
        weights = jnp.exp(scores - top_score)
        probs = (weights / jnp.sum(weights, axis=-1, keepdims=True)).astype(jnp.bfloat16)
        mixed = jnp.einsum("hqk,khe->qhe", probs, values, preferred_element_type=jnp.float32)
        return mixed.astype(jnp.bfloat16).reshape(block_rows, heads_here * head_size)

    result = lax.map(
        one_block,
        (
            queries.reshape(blocks, block_rows, heads_here, head_size),
            seg_all.reshape(blocks, block_rows),
        ),
    )
    return result.reshape(group_rows, heads_here * head_size)


def depthwise(padded, kernel, seg_here, seg_near, count):
    total_acc = jnp.zeros((count, padded.shape[1]), jnp.float32)
    for tap_index in range(kernel.shape[0]):
        window = padded[tap_index : tap_index + count].astype(jnp.float32)
        same = (seg_near[tap_index : tap_index + count] == seg_here)[:, None]
        total_acc = total_acc + jnp.where(same, window * kernel[tap_index].astype(jnp.float32), 0.0)
    return jax.nn.silu(total_acc).astype(jnp.bfloat16)


def on_device(ring, paired, frames, lengths, ln1_gain, ln2_gain, w_qkv, w_out, w_glu, dw_kernel, w_proj):
    frame_rows = frames.shape[1]
    model_width = frames.shape[2]
    seq_count = lax.axis_size("seq")
    group_rows = frame_rows * seq_count
    group_width = model_width // seq_count
    kernel_reach = dw_kernel.shape[0] // 2
    query_matrix = lax.all_gather(w_qkv[:, 0], "dp", axis=0, tiled=True)
    kv_parts = ring_gather(w_qkv[:, 1:].reshape(w_qkv.shape[0], 2 * group_width), ring)
    kv_matrix = kv_parts.reshape(model_width, 2 * group_width)
    out_parts = ring_gather(after(kv_parts, w_out), ring)
    out_local = jnp.einsum("nrc->rnc", out_parts).reshape(w_out.shape[0], model_width)
    glu_parts = ring_gather(after(out_parts, w_glu.reshape(w_glu.shape[0], 2 * group_width)), ring)
    glu_matrix = glu_parts.reshape(model_width, 2 * group_width)
    proj_parts = ring_gather(after(glu_parts, w_proj), ring)
    proj_local = jnp.einsum("nrc->rnc", proj_parts).reshape(w_proj.shape[0], model_width)
    inputs = frames[0].astype(jnp.float32)
    record_ends = jnp.cumsum(lengths[0])
    seg_all = segment_of(record_ends, jnp.arange(group_rows, dtype=jnp.int32))
    normed1 = layer_norm(inputs, ln1_gain)
    group_normed = seq_gather(normed1, paired).reshape(group_rows, model_width)
    query_rows = jnp.dot(
        group_normed, query_matrix, preferred_element_type=jnp.float32
    ).astype(jnp.bfloat16)
    kv_rows = jnp.dot(group_normed, kv_matrix, preferred_element_type=jnp.float32).astype(
        jnp.bfloat16
    )
    attended = attend(query_rows, kv_rows, seg_all, HD)
    attn_sum = seq_scatter_sum(
        jnp.dot(attended, out_local, preferred_element_type=jnp.float32).astype(jnp.bfloat16)
    )
    middle = (inputs + attn_sum).astype(jnp.bfloat16)
    normed2 = layer_norm(middle.astype(jnp.float32), ln2_gain)
    shard_piece = seq_gather(normed2, paired).reshape(group_rows, model_width)
    glu_pair = jnp.dot(shard_piece, glu_matrix, preferred_element_type=jnp.float32).reshape(
        shard_piece.shape[0], 2, group_width
    )
    gated = (glu_pair[:, 0] * jax.nn.sigmoid(glu_pair[:, 1])).astype(jnp.bfloat16)
    padded = jnp.pad(gated, ((kernel_reach, kernel_reach), (0, 0)))
    near_positions = jnp.arange(-kernel_reach, group_rows + kernel_reach, dtype=jnp.int32)
    activated = depthwise(
        padded, dw_kernel, seg_all, segment_of(record_ends, near_positions), group_rows
    )
    activated = lax.optimization_barrier(activated)
    conv_out = seq_scatter_sum(
        jnp.dot(activated, proj_local, preferred_element_type=jnp.float32).astype(jnp.bfloat16)
    )
    results = [(middle.astype(jnp.float32) + conv_out).astype(jnp.bfloat16)]
    return jnp.stack(results, axis=0)


def solution(mesh):
    in_specs = (
        P("dp", "seq", None),
        P("dp", None),
        P(),
        P(),
        P("dp", None, "seq"),
        P("seq", "dp"),
        P("dp", None, "seq"),
        P(None, "seq"),
        P("seq", "dp"),
    )
    out_specs = P("dp", "seq", None)
    return jax.shard_map(
        functools.partial(on_device, dp_ring(mesh), cores_paired(mesh)), mesh=mesh, in_specs=in_specs, out_specs=out_specs, check_vma=False
    )
```

```python
import functools

import jax
import jax.numpy as jnp
from jax import lax
from jax.sharding import PartitionSpec as P

HD = 96


def layer_norm(values, gain_vec):
    mean_value = jnp.mean(values, axis=-1, keepdims=True)
    centered = values - mean_value
    variance = jnp.mean(centered * centered, axis=-1, keepdims=True)
    return (centered * lax.rsqrt(variance + 1e-05) * gain_vec).astype(jnp.bfloat16)


def segment_of(record_ends, positions):
    return jnp.sum((positions[:, None] >= record_ends[None, :]).astype(jnp.int32), axis=1)


def seq_gather(block, paired):
    count = lax.axis_size("seq")
    me = lax.axis_index("seq")
    out = jnp.zeros((count,) + block.shape, block.dtype)
    out = lax.dynamic_update_index_in_dim(out, block, me, 0)
    if not paired:
        for shift in range(1, count):
            got = lax.ppermute(block, "seq", [(i, (i + shift) % count) for i in range(count)])
            out = lax.dynamic_update_index_in_dim(out, got, (me - shift) % count, 0)
        return out
    half = count // 2
    mine = jnp.zeros((half,) + block.shape, block.dtype)
    mine = lax.dynamic_update_index_in_dim(mine, block, me // 2, 0)
    for shift in range(1, half):
        got = lax.ppermute(
            block, "seq", [(i, (i + 2 * shift) % count) for i in range(count)]
        )
        src_dev = (me - 2 * shift) % count
        mine = lax.dynamic_update_index_in_dim(mine, got, src_dev // 2, 0)
        out = lax.dynamic_update_index_in_dim(out, got, src_dev, 0)
    other = lax.ppermute(mine, "seq", [(i, i ^ 1) for i in range(count)])
    partner = me ^ 1
    for k in range(half):
        out = lax.dynamic_update_index_in_dim(out, other[k], 2 * k + partner % 2, 0)
    return out


def cores_paired(mesh):
    count = mesh.shape["seq"]
    if count % 2:
        return False
    try:
        row = mesh.devices[0]
        return all(
            tuple(row[2 * k].coords) == tuple(row[2 * k + 1].coords) for k in range(count // 2)
        )
    except (AttributeError, TypeError, IndexError):
        return False


def seq_scatter_sum(full):
    count = lax.axis_size("seq")
    me = lax.axis_index("seq")
    rows = full.shape[0] // count
    total = lax.dynamic_slice_in_dim(full, me * rows, rows, axis=0).astype(jnp.float32)
    for shift in range(1, count):
        piece = lax.dynamic_slice_in_dim(full, ((me + shift) % count) * rows, rows, axis=0)
        got = lax.ppermute(piece, "seq", [(i, (i + shift) % count) for i in range(count)])
        total = total + got.astype(jnp.float32)
    return total


def dp_ring(mesh):
    count = mesh.shape["dp"]
    plain = list(range(count))
    try:
        coords = [tuple(int(c) for c in d.coords) for d in mesh.devices[:, 0]]
    except (AttributeError, TypeError, IndexError):
        return plain
    axes = [k for k in range(len(coords[0])) if len({c[k] for c in coords}) > 1]
    if len(axes) != 2:
        return plain
    low = [min(c[k] for c in coords) for k in axes]
    spots = {(c[axes[0]] - low[0], c[axes[1]] - low[1]): i for i, c in enumerate(coords)}
    sizes = [len({c[k] for c in coords}) for k in axes]
    if sizes[0] * sizes[1] != count or len(spots) != count:
        return plain
    if sizes[0] % 2 == 0:
        first, second, swap = sizes[0], sizes[1], False
    elif sizes[1] % 2 == 0:
        first, second, swap = sizes[1], sizes[0], True
    else:
        return plain
    path = [(0, 0)]
    for a in range(first):
        cols = range(1, second) if a % 2 == 0 else range(second - 1, 0, -1)
        path += [(a, b) for b in cols]
    path += [(a, 0) for a in range(first - 1, 0, -1)]
    if swap:
        path = [(b, a) for a, b in path]
    cycle = [spots.get(p) for p in path]
    if None in cycle or sorted(cycle) != plain:
        return plain
    return cycle


def ring_gather(block, ring):
    count = len(ring)
    me = lax.axis_index("dp")
    my_pos = jnp.asarray([ring.index(i) for i in range(count)], jnp.int32)[me]
    order = jnp.asarray(ring, jnp.int32)
    forward = [(ring[p], ring[(p + 1) % count]) for p in range(count)]
    backward = [(ring[p], ring[(p - 1) % count]) for p in range(count)]
    out = jnp.zeros((count,) + block.shape, block.dtype)
    out = lax.dynamic_update_index_in_dim(out, block, me, 0)
    ahead = behind = block
    for step in range(1, count // 2 + 1):
        ahead = lax.ppermute(ahead, "dp", forward)
        out = lax.dynamic_update_index_in_dim(out, ahead, order[(my_pos - step) % count], 0)
        if step <= count - 1 - count // 2:
            behind = lax.ppermute(behind, "dp", backward)
            out = lax.dynamic_update_index_in_dim(out, behind, order[(my_pos + step) % count], 0)
    return out


def after(token, value):
    return lax.optimization_barrier((token, value))[1]


def attend(projected, seg_all, head_size):
    group_rows = projected.shape[0]
    block_rows = 512
    heads_here = projected.shape[2] // head_size
    split = projected.reshape(group_rows, 3, heads_here, head_size)
    queries = split[:, 0]
    keys = split[:, 1]
    values = split[:, 2]
    blocks = group_rows // block_rows
    scale = 1.0 / head_size**0.5

    def one_block(block_data):
        query_block, seg_block = block_data
        scores = (
            jnp.einsum("qhe,khe->hqk", query_block, keys, preferred_element_type=jnp.float32)
            * scale
        )
        allowed = seg_block[:, None] == seg_all[None, :]
        scores = jnp.where(allowed[None], scores, -1e30)
        top_score = jnp.max(scores, axis=-1, keepdims=True)
        weights = jnp.exp(scores - top_score)
        probs = (weights / jnp.sum(weights, axis=-1, keepdims=True)).astype(jnp.bfloat16)
        mixed = jnp.einsum("hqk,khe->qhe", probs, values, preferred_element_type=jnp.float32)
        return mixed.astype(jnp.bfloat16).reshape(block_rows, heads_here * head_size)

    result = lax.map(
        one_block,
        (
            queries.reshape(blocks, block_rows, heads_here, head_size),
            seg_all.reshape(blocks, block_rows),
        ),
    )
    return result.reshape(group_rows, heads_here * head_size)


def depthwise(padded, kernel, seg_here, seg_near, count):
    total_acc = jnp.zeros((count, padded.shape[1]), jnp.float32)
    for tap_index in range(kernel.shape[0]):
        window = padded[tap_index : tap_index + count].astype(jnp.float32)
        same = (seg_near[tap_index : tap_index + count] == seg_here)[:, None]
        total_acc = total_acc + jnp.where(same, window * kernel[tap_index].astype(jnp.float32), 0.0)
    return jax.nn.silu(total_acc).astype(jnp.bfloat16)


def on_device(ring, paired, frames, lengths, ln1_gain, ln2_gain, w_qkv, w_out, w_glu, dw_kernel, w_proj):
    frame_rows = frames.shape[1]
    model_width = frames.shape[2]
    seq_count = lax.axis_size("seq")
    group_rows = frame_rows * seq_count
    group_width = model_width // seq_count
    kernel_reach = dw_kernel.shape[0] // 2
    qkv_parts = ring_gather(w_qkv.reshape(w_qkv.shape[0], 3 * group_width), ring)
    qkv_matrix = qkv_parts.reshape(model_width, 3 * group_width)
    out_parts = ring_gather(after(qkv_parts, w_out), ring)
    out_local = jnp.einsum("nrc->rnc", out_parts).reshape(w_out.shape[0], model_width)
    glu_rows = w_glu.shape[0]
    glu_local = w_glu.reshape(glu_rows, 2 * group_width)
    both_parts = ring_gather(
        after(out_parts, jnp.concatenate([glu_local, w_proj.reshape(-1, 2 * group_width)])), ring
    )
    glu_matrix = both_parts[:, :glu_rows].reshape(model_width, 2 * group_width)
    proj_parts = both_parts[:, glu_rows:].reshape(-1, *w_proj.shape)
    proj_local = jnp.einsum("nrc->rnc", proj_parts).reshape(w_proj.shape[0], model_width)
    inputs = frames[0].astype(jnp.float32)
    record_ends = jnp.cumsum(lengths[0])
    seg_all = segment_of(record_ends, jnp.arange(group_rows, dtype=jnp.int32))
    normed1 = layer_norm(inputs, ln1_gain)
    projected = (
        jnp.dot(seq_gather(normed1, paired).reshape(group_rows, model_width), qkv_matrix, preferred_element_type=jnp.float32)
        .astype(jnp.bfloat16)
        .reshape(group_rows, 3, group_width)
    )
    attended = attend(projected, seg_all, HD)
    attn_sum = seq_scatter_sum(
        jnp.dot(attended, out_local, preferred_element_type=jnp.float32).astype(jnp.bfloat16)
    )
    middle = (inputs + attn_sum).astype(jnp.bfloat16)
    normed2 = layer_norm(middle.astype(jnp.float32), ln2_gain)
    shard_piece = seq_gather(normed2, paired).reshape(group_rows, model_width)
    glu_pair = jnp.dot(shard_piece, glu_matrix, preferred_element_type=jnp.float32).reshape(
        shard_piece.shape[0], 2, group_width
    )
    gated = (glu_pair[:, 0] * jax.nn.sigmoid(glu_pair[:, 1])).astype(jnp.bfloat16)
    padded = jnp.pad(gated, ((kernel_reach, kernel_reach), (0, 0)))
    near_positions = jnp.arange(-kernel_reach, group_rows + kernel_reach, dtype=jnp.int32)
    activated = depthwise(
        padded, dw_kernel, seg_all, segment_of(record_ends, near_positions), group_rows
    )
    activated = lax.optimization_barrier(activated)
    conv_out = seq_scatter_sum(
        jnp.dot(activated, proj_local, preferred_element_type=jnp.float32).astype(jnp.bfloat16)
    )
    results = [(middle.astype(jnp.float32) + conv_out).astype(jnp.bfloat16)]
    return jnp.stack(results, axis=0)


def solution(mesh):
    in_specs = (
        P("dp", "seq", None),
        P("dp", None),
        P(),
        P(),
        P("dp", None, "seq"),
        P("seq", "dp"),
        P("dp", None, "seq"),
        P(None, "seq"),
        P("seq", "dp"),
    )
    out_specs = P("dp", "seq", None)
    return jax.shard_map(
        functools.partial(on_device, dp_ring(mesh), cores_paired(mesh)), mesh=mesh, in_specs=in_specs, out_specs=out_specs, check_vma=False
    )
```

```python
import functools

import jax
import jax.numpy as jnp
from jax import lax
from jax.sharding import PartitionSpec as P

HD = 96


def layer_norm(values, gain_vec):
    mean_value = jnp.mean(values, axis=-1, keepdims=True)
    centered = values - mean_value
    variance = jnp.mean(centered * centered, axis=-1, keepdims=True)
    return (centered * lax.rsqrt(variance + 1e-05) * gain_vec).astype(jnp.bfloat16)


def segment_of(record_ends, positions):
    return jnp.sum((positions[:, None] >= record_ends[None, :]).astype(jnp.int32), axis=1)


def seq_gather(block, paired):
    count = lax.axis_size("seq")
    me = lax.axis_index("seq")
    out = jnp.zeros((count,) + block.shape, block.dtype)
    out = lax.dynamic_update_index_in_dim(out, block, me, 0)
    if not paired:
        for shift in range(1, count):
            got = lax.ppermute(block, "seq", [(i, (i + shift) % count) for i in range(count)])
            out = lax.dynamic_update_index_in_dim(out, got, (me - shift) % count, 0)
        return out
    half = count // 2
    mine = jnp.zeros((half,) + block.shape, block.dtype)
    mine = lax.dynamic_update_index_in_dim(mine, block, me // 2, 0)
    for shift in range(1, half):
        got = lax.ppermute(
            block, "seq", [(i, (i + 2 * shift) % count) for i in range(count)]
        )
        src_dev = (me - 2 * shift) % count
        mine = lax.dynamic_update_index_in_dim(mine, got, src_dev // 2, 0)
        out = lax.dynamic_update_index_in_dim(out, got, src_dev, 0)
    other = lax.ppermute(mine, "seq", [(i, i ^ 1) for i in range(count)])
    partner = me ^ 1
    for k in range(half):
        out = lax.dynamic_update_index_in_dim(out, other[k], 2 * k + partner % 2, 0)
    return out


def cores_paired(mesh):
    count = mesh.shape["seq"]
    if count % 2:
        return False
    try:
        row = mesh.devices[0]
        return all(
            tuple(row[2 * k].coords) == tuple(row[2 * k + 1].coords) for k in range(count // 2)
        )
    except (AttributeError, TypeError, IndexError):
        return False


def seq_scatter_sum(full):
    count = lax.axis_size("seq")
    me = lax.axis_index("seq")
    rows = full.shape[0] // count
    total = lax.dynamic_slice_in_dim(full, me * rows, rows, axis=0).astype(jnp.float32)
    for shift in range(1, count):
        piece = lax.dynamic_slice_in_dim(full, ((me + shift) % count) * rows, rows, axis=0)
        got = lax.ppermute(piece, "seq", [(i, (i + shift) % count) for i in range(count)])
        total = total + got.astype(jnp.float32)
    return total


def dp_ring(mesh):
    count = mesh.shape["dp"]
    plain = list(range(count))
    try:
        coords = [tuple(int(c) for c in d.coords) for d in mesh.devices[:, 0]]
    except (AttributeError, TypeError, IndexError):
        return plain
    axes = [k for k in range(len(coords[0])) if len({c[k] for c in coords}) > 1]
    if len(axes) != 2:
        return plain
    low = [min(c[k] for c in coords) for k in axes]
    spots = {(c[axes[0]] - low[0], c[axes[1]] - low[1]): i for i, c in enumerate(coords)}
    sizes = [len({c[k] for c in coords}) for k in axes]
    if sizes[0] * sizes[1] != count or len(spots) != count:
        return plain
    if sizes[0] % 2 == 0:
        first, second, swap = sizes[0], sizes[1], False
    elif sizes[1] % 2 == 0:
        first, second, swap = sizes[1], sizes[0], True
    else:
        return plain
    path = [(0, 0)]
    for a in range(first):
        cols = range(1, second) if a % 2 == 0 else range(second - 1, 0, -1)
        path += [(a, b) for b in cols]
    path += [(a, 0) for a in range(first - 1, 0, -1)]
    if swap:
        path = [(b, a) for a, b in path]
    cycle = [spots.get(p) for p in path]
    if None in cycle or sorted(cycle) != plain:
        return plain
    return cycle


def ring_gather(block, ring):
    count = len(ring)
    me = lax.axis_index("dp")
    my_pos = jnp.asarray([ring.index(i) for i in range(count)], jnp.int32)[me]
    order = jnp.asarray(ring, jnp.int32)
    forward = [(ring[p], ring[(p + 1) % count]) for p in range(count)]
    backward = [(ring[p], ring[(p - 1) % count]) for p in range(count)]
    out = jnp.zeros((count,) + block.shape, block.dtype)
    out = lax.dynamic_update_index_in_dim(out, block, me, 0)
    ahead = behind = block
    for step in range(1, count // 2 + 1):
        ahead = lax.ppermute(ahead, "dp", forward)
        out = lax.dynamic_update_index_in_dim(out, ahead, order[(my_pos - step) % count], 0)
        if step <= count - 1 - count // 2:
            behind = lax.ppermute(behind, "dp", backward)
            out = lax.dynamic_update_index_in_dim(out, behind, order[(my_pos + step) % count], 0)
    return out


def after(token, value):
    return lax.optimization_barrier((token, value))[1]


def attend(projected, seg_all, head_size):
    group_rows = projected.shape[0]
    block_rows = 512
    heads_here = projected.shape[2] // head_size
    split = projected.reshape(group_rows, 3, heads_here, head_size)
    queries = split[:, 0]
    keys = split[:, 1]
    values = split[:, 2]
    blocks = group_rows // block_rows
    scale = 1.0 / head_size**0.5

    def one_block(block_data):
        query_block, seg_block = block_data
        scores = (
            jnp.einsum("qhe,khe->hqk", query_block, keys, preferred_element_type=jnp.float32)
            * scale
        )
        allowed = seg_block[:, None] == seg_all[None, :]
        scores = jnp.where(allowed[None], scores, -1e30)
        top_score = jnp.max(scores, axis=-1, keepdims=True)
        weights = jnp.exp(scores - top_score)
        probs = (weights / jnp.sum(weights, axis=-1, keepdims=True)).astype(jnp.bfloat16)
        mixed = jnp.einsum("hqk,khe->qhe", probs, values, preferred_element_type=jnp.float32)
        return mixed.astype(jnp.bfloat16).reshape(block_rows, heads_here * head_size)

    result = lax.map(
        one_block,
        (
            queries.reshape(blocks, block_rows, heads_here, head_size),
            seg_all.reshape(blocks, block_rows),
        ),
    )
    return result.reshape(group_rows, heads_here * head_size)


def depthwise(padded, kernel, seg_here, seg_near, count):
    total_acc = jnp.zeros((count, padded.shape[1]), jnp.float32)
    for tap_index in range(kernel.shape[0]):
        window = padded[tap_index : tap_index + count].astype(jnp.float32)
        same = (seg_near[tap_index : tap_index + count] == seg_here)[:, None]
        total_acc = total_acc + jnp.where(same, window * kernel[tap_index].astype(jnp.float32), 0.0)
    return jax.nn.silu(total_acc).astype(jnp.bfloat16)


def on_device(ring, paired, frames, lengths, ln1_gain, ln2_gain, w_qkv, w_out, w_glu, dw_kernel, w_proj):
    frame_rows = frames.shape[1]
    model_width = frames.shape[2]
    seq_count = lax.axis_size("seq")
    group_rows = frame_rows * seq_count
    group_width = model_width // seq_count
    kernel_reach = dw_kernel.shape[0] // 2
    qkv_parts = ring_gather(w_qkv.reshape(w_qkv.shape[0], 3 * group_width), ring)
    qkv_matrix = qkv_parts.reshape(model_width, 3 * group_width)
    kv_start = qkv_parts
    out_parts = ring_gather(after(qkv_parts, w_out), ring)
    out_local = jnp.einsum("nrc->rnc", out_parts).reshape(w_out.shape[0], model_width)
    glu_rows = w_glu.shape[0]
    glu_local = w_glu.reshape(glu_rows, 2 * group_width)
    both_parts = ring_gather(
        after(kv_start, jnp.concatenate([glu_local, w_proj.reshape(-1, 2 * group_width)])), ring
    )
    glu_matrix = both_parts[:, :glu_rows].reshape(model_width, 2 * group_width)
    proj_parts = both_parts[:, glu_rows:].reshape(-1, *w_proj.shape)
    proj_local = jnp.einsum("nrc->rnc", proj_parts).reshape(w_proj.shape[0], model_width)
    inputs = frames[0].astype(jnp.float32)
    record_ends = jnp.cumsum(lengths[0])
    seg_all = segment_of(record_ends, jnp.arange(group_rows, dtype=jnp.int32))
    normed1 = layer_norm(inputs, ln1_gain)
    projected = (
        jnp.dot(seq_gather(normed1, paired).reshape(group_rows, model_width), qkv_matrix, preferred_element_type=jnp.float32)
        .astype(jnp.bfloat16)
        .reshape(group_rows, 3, group_width)
    )
    attended = attend(projected, seg_all, HD)
    attn_sum = seq_scatter_sum(
        jnp.dot(attended, out_local, preferred_element_type=jnp.float32).astype(jnp.bfloat16)
    )
    middle = (inputs + attn_sum).astype(jnp.bfloat16)
    normed2 = layer_norm(middle.astype(jnp.float32), ln2_gain)
    shard_piece = seq_gather(normed2, paired).reshape(group_rows, model_width)
    glu_pair = jnp.dot(shard_piece, glu_matrix, preferred_element_type=jnp.float32).reshape(
        shard_piece.shape[0], 2, group_width
    )
    gated = (glu_pair[:, 0] * jax.nn.sigmoid(glu_pair[:, 1])).astype(jnp.bfloat16)
    padded = jnp.pad(gated, ((kernel_reach, kernel_reach), (0, 0)))
    near_positions = jnp.arange(-kernel_reach, group_rows + kernel_reach, dtype=jnp.int32)
    activated = depthwise(
        padded, dw_kernel, seg_all, segment_of(record_ends, near_positions), group_rows
    )
    activated = lax.optimization_barrier(activated)
    conv_out = seq_scatter_sum(
        jnp.dot(activated, proj_local, preferred_element_type=jnp.float32).astype(jnp.bfloat16)
    )
    results = [(middle.astype(jnp.float32) + conv_out).astype(jnp.bfloat16)]
    return jnp.stack(results, axis=0)


def solution(mesh):
    in_specs = (
        P("dp", "seq", None),
        P("dp", None),
        P(),
        P(),
        P("dp", None, "seq"),
        P("seq", "dp"),
        P("dp", None, "seq"),
        P(None, "seq"),
        P("seq", "dp"),
    )
    out_specs = P("dp", "seq", None)
    return jax.shard_map(
        functools.partial(on_device, dp_ring(mesh), cores_paired(mesh)), mesh=mesh, in_specs=in_specs, out_specs=out_specs, check_vma=False
    )
```

```python
import functools

import jax
import jax.numpy as jnp
from jax import lax
from jax.sharding import PartitionSpec as P

HD = 96


def layer_norm(values, gain_vec):
    mean_value = jnp.mean(values, axis=-1, keepdims=True)
    centered = values - mean_value
    variance = jnp.mean(centered * centered, axis=-1, keepdims=True)
    return (centered * lax.rsqrt(variance + 1e-05) * gain_vec).astype(jnp.bfloat16)


def segment_of(record_ends, positions):
    return jnp.sum((positions[:, None] >= record_ends[None, :]).astype(jnp.int32), axis=1)


def seq_gather(block, paired):
    count = lax.axis_size("seq")
    me = lax.axis_index("seq")
    out = jnp.zeros((count,) + block.shape, block.dtype)
    out = lax.dynamic_update_index_in_dim(out, block, me, 0)
    if not paired:
        for shift in range(1, count):
            got = lax.ppermute(block, "seq", [(i, (i + shift) % count) for i in range(count)])
            out = lax.dynamic_update_index_in_dim(out, got, (me - shift) % count, 0)
        return out
    half = count // 2
    mine = jnp.zeros((half,) + block.shape, block.dtype)
    mine = lax.dynamic_update_index_in_dim(mine, block, me // 2, 0)
    for shift in range(1, half):
        got = lax.ppermute(
            block, "seq", [(i, (i + 2 * shift) % count) for i in range(count)]
        )
        src_dev = (me - 2 * shift) % count
        mine = lax.dynamic_update_index_in_dim(mine, got, src_dev // 2, 0)
        out = lax.dynamic_update_index_in_dim(out, got, src_dev, 0)
    other = lax.ppermute(mine, "seq", [(i, i ^ 1) for i in range(count)])
    partner = me ^ 1
    for k in range(half):
        out = lax.dynamic_update_index_in_dim(out, other[k], 2 * k + partner % 2, 0)
    return out


def cores_paired(mesh):
    count = mesh.shape["seq"]
    if count % 2:
        return False
    try:
        row = mesh.devices[0]
        return all(
            tuple(row[2 * k].coords) == tuple(row[2 * k + 1].coords) for k in range(count // 2)
        )
    except (AttributeError, TypeError, IndexError):
        return False


def seq_scatter_sum(full):
    count = lax.axis_size("seq")
    me = lax.axis_index("seq")
    rows = full.shape[0] // count
    total = lax.dynamic_slice_in_dim(full, me * rows, rows, axis=0).astype(jnp.float32)
    for shift in range(1, count):
        piece = lax.dynamic_slice_in_dim(full, ((me + shift) % count) * rows, rows, axis=0)
        got = lax.ppermute(piece, "seq", [(i, (i + shift) % count) for i in range(count)])
        total = total + got.astype(jnp.float32)
    return total


def dp_ring(mesh):
    count = mesh.shape["dp"]
    plain = list(range(count))
    try:
        coords = [tuple(int(c) for c in d.coords) for d in mesh.devices[:, 0]]
    except (AttributeError, TypeError, IndexError):
        return plain
    axes = [k for k in range(len(coords[0])) if len({c[k] for c in coords}) > 1]
    if len(axes) != 2:
        return plain
    low = [min(c[k] for c in coords) for k in axes]
    spots = {(c[axes[0]] - low[0], c[axes[1]] - low[1]): i for i, c in enumerate(coords)}
    sizes = [len({c[k] for c in coords}) for k in axes]
    if sizes[0] * sizes[1] != count or len(spots) != count:
        return plain
    if sizes[0] % 2 == 0:
        first, second, swap = sizes[0], sizes[1], False
    elif sizes[1] % 2 == 0:
        first, second, swap = sizes[1], sizes[0], True
    else:
        return plain
    path = [(0, 0)]
    for a in range(first):
        cols = range(1, second) if a % 2 == 0 else range(second - 1, 0, -1)
        path += [(a, b) for b in cols]
    path += [(a, 0) for a in range(first - 1, 0, -1)]
    if swap:
        path = [(b, a) for a, b in path]
    cycle = [spots.get(p) for p in path]
    if None in cycle or sorted(cycle) != plain:
        return plain
    return cycle


def ring_gather(block, ring):
    count = len(ring)
    me = lax.axis_index("dp")
    my_pos = jnp.asarray([ring.index(i) for i in range(count)], jnp.int32)[me]
    order = jnp.asarray(ring, jnp.int32)
    forward = [(ring[p], ring[(p + 1) % count]) for p in range(count)]
    backward = [(ring[p], ring[(p - 1) % count]) for p in range(count)]
    out = jnp.zeros((count,) + block.shape, block.dtype)
    out = lax.dynamic_update_index_in_dim(out, block, me, 0)
    ahead = behind = block
    for step in range(1, count // 2 + 1):
        ahead = lax.ppermute(ahead, "dp", forward)
        out = lax.dynamic_update_index_in_dim(out, ahead, order[(my_pos - step) % count], 0)
        if step <= count - 1 - count // 2:
            behind = lax.ppermute(behind, "dp", backward)
            out = lax.dynamic_update_index_in_dim(out, behind, order[(my_pos + step) % count], 0)
    return out


def after(token, value):
    return lax.optimization_barrier((token, value))[1]


def attend(projected, seg_all, head_size):
    group_rows = projected.shape[0]
    block_rows = 512
    heads_here = projected.shape[2] // head_size
    split = projected.reshape(group_rows, 3, heads_here, head_size)
    queries = split[:, 0]
    keys = split[:, 1]
    values = split[:, 2]
    blocks = group_rows // block_rows
    scale = 1.0 / head_size**0.5

    def one_block(block_data):
        query_block, seg_block = block_data
        scores = (
            jnp.einsum("qhe,khe->hqk", query_block, keys, preferred_element_type=jnp.float32)
            * scale
        )
        allowed = seg_block[:, None] == seg_all[None, :]
        scores = jnp.where(allowed[None], scores, -1e30)
        top_score = jnp.max(scores, axis=-1, keepdims=True)
        weights = jnp.exp(scores - top_score)
        probs = (weights / jnp.sum(weights, axis=-1, keepdims=True)).astype(jnp.bfloat16)
        mixed = jnp.einsum("hqk,khe->qhe", probs, values, preferred_element_type=jnp.float32)
        return mixed.astype(jnp.bfloat16).reshape(block_rows, heads_here * head_size)

    result = lax.map(
        one_block,
        (
            queries.reshape(blocks, block_rows, heads_here, head_size),
            seg_all.reshape(blocks, block_rows),
        ),
    )
    return result.reshape(group_rows, heads_here * head_size)


def depthwise(padded, kernel, seg_here, seg_near, count):
    total_acc = jnp.zeros((count, padded.shape[1]), jnp.float32)
    for tap_index in range(kernel.shape[0]):
        window = padded[tap_index : tap_index + count].astype(jnp.float32)
        same = (seg_near[tap_index : tap_index + count] == seg_here)[:, None]
        total_acc = total_acc + jnp.where(same, window * kernel[tap_index].astype(jnp.float32), 0.0)
    return jax.nn.silu(total_acc).astype(jnp.bfloat16)


def on_device(ring, paired, frames, lengths, ln1_gain, ln2_gain, w_qkv, w_out, w_glu, dw_kernel, w_proj):
    frame_rows = frames.shape[1]
    model_width = frames.shape[2]
    seq_count = lax.axis_size("seq")
    group_rows = frame_rows * seq_count
    group_width = model_width // seq_count
    kernel_reach = dw_kernel.shape[0] // 2
    qkv_parts = ring_gather(w_qkv.reshape(w_qkv.shape[0], 3 * group_width), ring)
    qkv_matrix = qkv_parts.reshape(model_width, 3 * group_width)
    out_local = lax.all_gather(w_out, "dp", axis=1, tiled=True)
    glu_rows = w_glu.shape[0]
    glu_local = w_glu.reshape(glu_rows, 2 * group_width)
    both_parts = ring_gather(
        after(qkv_parts, jnp.concatenate([glu_local, w_proj.reshape(-1, 2 * group_width)])), ring
    )
    glu_matrix = both_parts[:, :glu_rows].reshape(model_width, 2 * group_width)
    proj_parts = both_parts[:, glu_rows:].reshape(-1, *w_proj.shape)
    proj_local = jnp.einsum("nrc->rnc", proj_parts).reshape(w_proj.shape[0], model_width)
    inputs = frames[0].astype(jnp.float32)
    record_ends = jnp.cumsum(lengths[0])
    seg_all = segment_of(record_ends, jnp.arange(group_rows, dtype=jnp.int32))
    normed1 = layer_norm(inputs, ln1_gain)
    projected = (
        jnp.dot(seq_gather(normed1, paired).reshape(group_rows, model_width), qkv_matrix, preferred_element_type=jnp.float32)
        .astype(jnp.bfloat16)
        .reshape(group_rows, 3, group_width)
    )
    attended = attend(projected, seg_all, HD)
    attn_sum = seq_scatter_sum(
        jnp.dot(attended, out_local, preferred_element_type=jnp.float32).astype(jnp.bfloat16)
    )
    middle = (inputs + attn_sum).astype(jnp.bfloat16)
    normed2 = layer_norm(middle.astype(jnp.float32), ln2_gain)
    shard_piece = seq_gather(normed2, paired).reshape(group_rows, model_width)
    glu_pair = jnp.dot(shard_piece, glu_matrix, preferred_element_type=jnp.float32).reshape(
        shard_piece.shape[0], 2, group_width
    )
    gated = (glu_pair[:, 0] * jax.nn.sigmoid(glu_pair[:, 1])).astype(jnp.bfloat16)
    padded = jnp.pad(gated, ((kernel_reach, kernel_reach), (0, 0)))
    near_positions = jnp.arange(-kernel_reach, group_rows + kernel_reach, dtype=jnp.int32)
    activated = depthwise(
        padded, dw_kernel, seg_all, segment_of(record_ends, near_positions), group_rows
    )
    activated = lax.optimization_barrier(activated)
    conv_out = seq_scatter_sum(
        jnp.dot(activated, proj_local, preferred_element_type=jnp.float32).astype(jnp.bfloat16)
    )
    results = [(middle.astype(jnp.float32) + conv_out).astype(jnp.bfloat16)]
    return jnp.stack(results, axis=0)


def solution(mesh):
    in_specs = (
        P("dp", "seq", None),
        P("dp", None),
        P(),
        P(),
        P("dp", None, "seq"),
        P("seq", "dp"),
        P("dp", None, "seq"),
        P(None, "seq"),
        P("seq", "dp"),
    )
    out_specs = P("dp", "seq", None)
    return jax.shard_map(
        functools.partial(on_device, dp_ring(mesh), cores_paired(mesh)), mesh=mesh, in_specs=in_specs, out_specs=out_specs, check_vma=False
    )
```

```python
import functools

import jax
import jax.numpy as jnp
from jax import lax
from jax.sharding import PartitionSpec as P

HD = 96


def layer_norm(values, gain_vec):
    mean_value = jnp.mean(values, axis=-1, keepdims=True)
    centered = values - mean_value
    variance = jnp.mean(centered * centered, axis=-1, keepdims=True)
    return (centered * lax.rsqrt(variance + 1e-05) * gain_vec).astype(jnp.bfloat16)


def segment_of(record_ends, positions):
    return jnp.sum((positions[:, None] >= record_ends[None, :]).astype(jnp.int32), axis=1)


def seq_gather(block, paired):
    count = lax.axis_size("seq")
    me = lax.axis_index("seq")
    out = jnp.zeros((count,) + block.shape, block.dtype)
    out = lax.dynamic_update_index_in_dim(out, block, me, 0)
    if not paired:
        for shift in range(1, count):
            got = lax.ppermute(block, "seq", [(i, (i + shift) % count) for i in range(count)])
            out = lax.dynamic_update_index_in_dim(out, got, (me - shift) % count, 0)
        return out
    half = count // 2
    mine = jnp.zeros((half,) + block.shape, block.dtype)
    mine = lax.dynamic_update_index_in_dim(mine, block, me // 2, 0)
    for shift in range(1, half):
        got = lax.ppermute(
            block, "seq", [(i, (i + 2 * shift) % count) for i in range(count)]
        )
        src_dev = (me - 2 * shift) % count
        mine = lax.dynamic_update_index_in_dim(mine, got, src_dev // 2, 0)
        out = lax.dynamic_update_index_in_dim(out, got, src_dev, 0)
    other = lax.ppermute(mine, "seq", [(i, i ^ 1) for i in range(count)])
    partner = me ^ 1
    for k in range(half):
        out = lax.dynamic_update_index_in_dim(out, other[k], 2 * k + partner % 2, 0)
    return out


def cores_paired(mesh):
    count = mesh.shape["seq"]
    if count % 2:
        return False
    try:
        row = mesh.devices[0]
        return all(
            tuple(row[2 * k].coords) == tuple(row[2 * k + 1].coords) for k in range(count // 2)
        )
    except (AttributeError, TypeError, IndexError):
        return False


def seq_scatter_sum(full, paired):
    count = lax.axis_size("seq")
    me = lax.axis_index("seq")
    rows = full.shape[0] // count
    if not paired:
        total = lax.dynamic_slice_in_dim(full, me * rows, rows, axis=0).astype(jnp.float32)
        for shift in range(1, count):
            piece = lax.dynamic_slice_in_dim(full, ((me + shift) % count) * rows, rows, axis=0)
            got = lax.ppermute(piece, "seq", [(i, (i + shift) % count) for i in range(count)])
            total = total + got.astype(jnp.float32)
        return total
    half = count // 2
    core = me % 2
    quads = full.reshape(half, 2, rows, full.shape[1])
    mine = lax.dynamic_index_in_dim(quads, core, axis=1, keepdims=False)
    theirs = lax.dynamic_index_in_dim(quads, 1 - core, axis=1, keepdims=False)
    got = lax.ppermute(theirs, "seq", [(i, i ^ 1) for i in range(count)])
    chip_sum = mine.astype(jnp.float32) + got.astype(jnp.float32)
    here = me // 2
    total = lax.dynamic_index_in_dim(chip_sum, here, axis=0, keepdims=False)
    for shift in range(1, half):
        piece = lax.dynamic_index_in_dim(chip_sum, (here + shift) % half, axis=0, keepdims=False)
        got = lax.ppermute(
            piece.astype(jnp.bfloat16),
            "seq",
            [(i, (i + 2 * shift) % count) for i in range(count)],
        )
        total = total + got.astype(jnp.float32)
    return total


def dp_ring(mesh):
    count = mesh.shape["dp"]
    plain = list(range(count))
    try:
        coords = [tuple(int(c) for c in d.coords) for d in mesh.devices[:, 0]]
    except (AttributeError, TypeError, IndexError):
        return plain
    axes = [k for k in range(len(coords[0])) if len({c[k] for c in coords}) > 1]
    if len(axes) != 2:
        return plain
    low = [min(c[k] for c in coords) for k in axes]
    spots = {(c[axes[0]] - low[0], c[axes[1]] - low[1]): i for i, c in enumerate(coords)}
    sizes = [len({c[k] for c in coords}) for k in axes]
    if sizes[0] * sizes[1] != count or len(spots) != count:
        return plain
    if sizes[0] % 2 == 0:
        first, second, swap = sizes[0], sizes[1], False
    elif sizes[1] % 2 == 0:
        first, second, swap = sizes[1], sizes[0], True
    else:
        return plain
    path = [(0, 0)]
    for a in range(first):
        cols = range(1, second) if a % 2 == 0 else range(second - 1, 0, -1)
        path += [(a, b) for b in cols]
    path += [(a, 0) for a in range(first - 1, 0, -1)]
    if swap:
        path = [(b, a) for a, b in path]
    cycle = [spots.get(p) for p in path]
    if None in cycle or sorted(cycle) != plain:
        return plain
    return cycle


def ring_gather(block, ring):
    count = len(ring)
    me = lax.axis_index("dp")
    my_pos = jnp.asarray([ring.index(i) for i in range(count)], jnp.int32)[me]
    order = jnp.asarray(ring, jnp.int32)
    forward = [(ring[p], ring[(p + 1) % count]) for p in range(count)]
    backward = [(ring[p], ring[(p - 1) % count]) for p in range(count)]
    out = jnp.zeros((count,) + block.shape, block.dtype)
    out = lax.dynamic_update_index_in_dim(out, block, me, 0)
    ahead = behind = block
    for step in range(1, count // 2 + 1):
        ahead = lax.ppermute(ahead, "dp", forward)
        out = lax.dynamic_update_index_in_dim(out, ahead, order[(my_pos - step) % count], 0)
        if step <= count - 1 - count // 2:
            behind = lax.ppermute(behind, "dp", backward)
            out = lax.dynamic_update_index_in_dim(out, behind, order[(my_pos + step) % count], 0)
    return out


def after(token, value):
    return lax.optimization_barrier((token, value))[1]


def attend(projected, seg_all, head_size):
    group_rows = projected.shape[0]
    block_rows = 512
    heads_here = projected.shape[2] // head_size
    split = projected.reshape(group_rows, 3, heads_here, head_size)
    queries = split[:, 0]
    keys = split[:, 1]
    values = split[:, 2]
    blocks = group_rows // block_rows
    scale = 1.0 / head_size**0.5

    def one_block(block_data):
        query_block, seg_block = block_data
        scores = (
            jnp.einsum("qhe,khe->hqk", query_block, keys, preferred_element_type=jnp.float32)
            * scale
        )
        allowed = seg_block[:, None] == seg_all[None, :]
        scores = jnp.where(allowed[None], scores, -1e30)
        top_score = jnp.max(scores, axis=-1, keepdims=True)
        weights = jnp.exp(scores - top_score)
        probs = (weights / jnp.sum(weights, axis=-1, keepdims=True)).astype(jnp.bfloat16)
        mixed = jnp.einsum("hqk,khe->qhe", probs, values, preferred_element_type=jnp.float32)
        return mixed.astype(jnp.bfloat16).reshape(block_rows, heads_here * head_size)

    result = lax.map(
        one_block,
        (
            queries.reshape(blocks, block_rows, heads_here, head_size),
            seg_all.reshape(blocks, block_rows),
        ),
    )
    return result.reshape(group_rows, heads_here * head_size)


def depthwise(padded, kernel, seg_here, seg_near, count):
    total_acc = jnp.zeros((count, padded.shape[1]), jnp.float32)
    for tap_index in range(kernel.shape[0]):
        window = padded[tap_index : tap_index + count].astype(jnp.float32)
        same = (seg_near[tap_index : tap_index + count] == seg_here)[:, None]
        total_acc = total_acc + jnp.where(same, window * kernel[tap_index].astype(jnp.float32), 0.0)
    return jax.nn.silu(total_acc).astype(jnp.bfloat16)


def on_device(ring, paired, frames, lengths, ln1_gain, ln2_gain, w_qkv, w_out, w_glu, dw_kernel, w_proj):
    frame_rows = frames.shape[1]
    model_width = frames.shape[2]
    seq_count = lax.axis_size("seq")
    group_rows = frame_rows * seq_count
    group_width = model_width // seq_count
    kernel_reach = dw_kernel.shape[0] // 2
    qkv_parts = ring_gather(w_qkv.reshape(w_qkv.shape[0], 3 * group_width), ring)
    qkv_matrix = qkv_parts.reshape(model_width, 3 * group_width)
    out_parts = ring_gather(after(qkv_parts, w_out), ring)
    out_local = jnp.einsum("nrc->rnc", out_parts).reshape(w_out.shape[0], model_width)
    glu_rows = w_glu.shape[0]
    glu_local = w_glu.reshape(glu_rows, 2 * group_width)
    both_parts = ring_gather(
        after(out_parts, jnp.concatenate([glu_local, w_proj.reshape(-1, 2 * group_width)])), ring
    )
    glu_matrix = both_parts[:, :glu_rows].reshape(model_width, 2 * group_width)
    proj_parts = both_parts[:, glu_rows:].reshape(-1, *w_proj.shape)
    proj_local = jnp.einsum("nrc->rnc", proj_parts).reshape(w_proj.shape[0], model_width)
    inputs = frames[0].astype(jnp.float32)
    record_ends = jnp.cumsum(lengths[0])
    seg_all = segment_of(record_ends, jnp.arange(group_rows, dtype=jnp.int32))
    normed1 = layer_norm(inputs, ln1_gain)
    projected = (
        jnp.dot(seq_gather(normed1, paired).reshape(group_rows, model_width), qkv_matrix, preferred_element_type=jnp.float32)
        .astype(jnp.bfloat16)
        .reshape(group_rows, 3, group_width)
    )
    attended = attend(projected, seg_all, HD)
    attn_sum = seq_scatter_sum(
        jnp.dot(attended, out_local, preferred_element_type=jnp.float32).astype(jnp.bfloat16),
        paired,
    )
    middle = (inputs + attn_sum).astype(jnp.bfloat16)
    normed2 = layer_norm(middle.astype(jnp.float32), ln2_gain)
    shard_piece = seq_gather(normed2, paired).reshape(group_rows, model_width)
    glu_pair = jnp.dot(shard_piece, glu_matrix, preferred_element_type=jnp.float32).reshape(
        shard_piece.shape[0], 2, group_width
    )
    gated = (glu_pair[:, 0] * jax.nn.sigmoid(glu_pair[:, 1])).astype(jnp.bfloat16)
    padded = jnp.pad(gated, ((kernel_reach, kernel_reach), (0, 0)))
    near_positions = jnp.arange(-kernel_reach, group_rows + kernel_reach, dtype=jnp.int32)
    activated = depthwise(
        padded, dw_kernel, seg_all, segment_of(record_ends, near_positions), group_rows
    )
    activated = lax.optimization_barrier(activated)
    conv_out = seq_scatter_sum(
        jnp.dot(activated, proj_local, preferred_element_type=jnp.float32).astype(jnp.bfloat16),
        paired,
    )
    results = [(middle.astype(jnp.float32) + conv_out).astype(jnp.bfloat16)]
    return jnp.stack(results, axis=0)


def solution(mesh):
    in_specs = (
        P("dp", "seq", None),
        P("dp", None),
        P(),
        P(),
        P("dp", None, "seq"),
        P("seq", "dp"),
        P("dp", None, "seq"),
        P(None, "seq"),
        P("seq", "dp"),
    )
    out_specs = P("dp", "seq", None)
    return jax.shard_map(
        functools.partial(on_device, dp_ring(mesh), cores_paired(mesh)), mesh=mesh, in_specs=in_specs, out_specs=out_specs, check_vma=False
    )
```

```python
import functools

import jax
import jax.numpy as jnp
from jax import lax
from jax.sharding import PartitionSpec as P

HD = 96


def layer_norm(values, gain_vec):
    mean_value = jnp.mean(values, axis=-1, keepdims=True)
    centered = values - mean_value
    variance = jnp.mean(centered * centered, axis=-1, keepdims=True)
    return (centered * lax.rsqrt(variance + 1e-05) * gain_vec).astype(jnp.bfloat16)


def segment_of(record_ends, positions):
    return jnp.sum((positions[:, None] >= record_ends[None, :]).astype(jnp.int32), axis=1)


def seq_gather(block, paired):
    count = lax.axis_size("seq")
    me = lax.axis_index("seq")
    out = jnp.zeros((count,) + block.shape, block.dtype)
    out = lax.dynamic_update_index_in_dim(out, block, me, 0)
    if not paired:
        for shift in range(1, count):
            got = lax.ppermute(block, "seq", [(i, (i + shift) % count) for i in range(count)])
            out = lax.dynamic_update_index_in_dim(out, got, (me - shift) % count, 0)
        return out
    half = count // 2
    mine = jnp.zeros((half,) + block.shape, block.dtype)
    mine = lax.dynamic_update_index_in_dim(mine, block, me // 2, 0)
    for shift in range(1, half):
        got = lax.ppermute(
            block, "seq", [(i, (i + 2 * shift) % count) for i in range(count)]
        )
        src_dev = (me - 2 * shift) % count
        mine = lax.dynamic_update_index_in_dim(mine, got, src_dev // 2, 0)
        out = lax.dynamic_update_index_in_dim(out, got, src_dev, 0)
    other = lax.ppermute(mine, "seq", [(i, i ^ 1) for i in range(count)])
    partner = me ^ 1
    for k in range(half):
        out = lax.dynamic_update_index_in_dim(out, other[k], 2 * k + partner % 2, 0)
    return out


def cores_paired(mesh):
    count = mesh.shape["seq"]
    if count % 2:
        return False
    try:
        row = mesh.devices[0]
        return all(
            tuple(row[2 * k].coords) == tuple(row[2 * k + 1].coords) for k in range(count // 2)
        )
    except (AttributeError, TypeError, IndexError):
        return False


def seq_scatter_sum(full, paired):
    count = lax.axis_size("seq")
    me = lax.axis_index("seq")
    rows = full.shape[0] // count
    if not paired:
        total = lax.dynamic_slice_in_dim(full, me * rows, rows, axis=0).astype(jnp.float32)
        for shift in range(1, count):
            piece = lax.dynamic_slice_in_dim(full, ((me + shift) % count) * rows, rows, axis=0)
            got = lax.ppermute(piece, "seq", [(i, (i + shift) % count) for i in range(count)])
            total = total + got.astype(jnp.float32)
        return total
    half = count // 2
    core = me % 2
    quads = full.reshape(half, 2, rows, full.shape[1])
    mine = lax.dynamic_index_in_dim(quads, core, axis=1, keepdims=False)
    theirs = lax.dynamic_index_in_dim(quads, 1 - core, axis=1, keepdims=False)
    got = lax.ppermute(theirs, "seq", [(i, i ^ 1) for i in range(count)])
    chip_sum = mine.astype(jnp.float32) + got.astype(jnp.float32)
    here = me // 2
    total = lax.dynamic_index_in_dim(chip_sum, here, axis=0, keepdims=False)
    for shift in range(1, half):
        piece = lax.dynamic_index_in_dim(chip_sum, (here + shift) % half, axis=0, keepdims=False)
        got = lax.ppermute(
            piece.astype(jnp.bfloat16),
            "seq",
            [(i, (i + 2 * shift) % count) for i in range(count)],
        )
        total = total + got.astype(jnp.float32)
    return total


def dp_ring(mesh):
    count = mesh.shape["dp"]
    plain = list(range(count))
    try:
        coords = [tuple(int(c) for c in d.coords) for d in mesh.devices[:, 0]]
    except (AttributeError, TypeError, IndexError):
        return plain
    axes = [k for k in range(len(coords[0])) if len({c[k] for c in coords}) > 1]
    if len(axes) != 2:
        return plain
    low = [min(c[k] for c in coords) for k in axes]
    spots = {(c[axes[0]] - low[0], c[axes[1]] - low[1]): i for i, c in enumerate(coords)}
    sizes = [len({c[k] for c in coords}) for k in axes]
    if sizes[0] * sizes[1] != count or len(spots) != count:
        return plain
    if sizes[0] % 2 == 0:
        first, second, swap = sizes[0], sizes[1], False
    elif sizes[1] % 2 == 0:
        first, second, swap = sizes[1], sizes[0], True
    else:
        return plain
    path = [(0, 0)]
    for a in range(first):
        cols = range(1, second) if a % 2 == 0 else range(second - 1, 0, -1)
        path += [(a, b) for b in cols]
    path += [(a, 0) for a in range(first - 1, 0, -1)]
    if swap:
        path = [(b, a) for a, b in path]
    cycle = [spots.get(p) for p in path]
    if None in cycle or sorted(cycle) != plain:
        return plain
    return cycle


def ring_gather(block, ring):
    count = len(ring)
    me = lax.axis_index("dp")
    my_pos = jnp.asarray([ring.index(i) for i in range(count)], jnp.int32)[me]
    order = jnp.asarray(ring, jnp.int32)
    forward = [(ring[p], ring[(p + 1) % count]) for p in range(count)]
    backward = [(ring[p], ring[(p - 1) % count]) for p in range(count)]
    out = jnp.zeros((count,) + block.shape, block.dtype)
    out = lax.dynamic_update_index_in_dim(out, block, me, 0)
    ahead = behind = block
    for step in range(1, count // 2 + 1):
        ahead = lax.ppermute(ahead, "dp", forward)
        out = lax.dynamic_update_index_in_dim(out, ahead, order[(my_pos - step) % count], 0)
        if step <= count - 1 - count // 2:
            behind = lax.ppermute(behind, "dp", backward)
            out = lax.dynamic_update_index_in_dim(out, behind, order[(my_pos + step) % count], 0)
    return out


def after(token, value):
    return lax.optimization_barrier((token, value))[1]


def attend(projected, seg_all, head_size):
    group_rows = projected.shape[0]
    block_rows = 512
    heads_here = projected.shape[2] // head_size
    split = projected.reshape(group_rows, 3, heads_here, head_size)
    queries = split[:, 0]
    keys = split[:, 1]
    values = split[:, 2]
    blocks = group_rows // block_rows
    scale = 1.0 / head_size**0.5

    def one_block(block_data):
        query_block, seg_block = block_data
        scores = (
            jnp.einsum("qhe,khe->hqk", query_block, keys, preferred_element_type=jnp.float32)
            * scale
        )
        allowed = seg_block[:, None] == seg_all[None, :]
        scores = jnp.where(allowed[None], scores, -1e30)
        top_score = jnp.max(scores, axis=-1, keepdims=True)
        weights = jnp.exp(scores - top_score)
        probs = (weights / jnp.sum(weights, axis=-1, keepdims=True)).astype(jnp.bfloat16)
        mixed = jnp.einsum("hqk,khe->qhe", probs, values, preferred_element_type=jnp.float32)
        return mixed.astype(jnp.bfloat16).reshape(block_rows, heads_here * head_size)

    result = lax.map(
        one_block,
        (
            queries.reshape(blocks, block_rows, heads_here, head_size),
            seg_all.reshape(blocks, block_rows),
        ),
    )
    return result.reshape(group_rows, heads_here * head_size)


def depthwise(padded, kernel, seg_here, seg_near, count):
    total_acc = jnp.zeros((count, padded.shape[1]), jnp.float32)
    for tap_index in range(kernel.shape[0]):
        window = padded[tap_index : tap_index + count].astype(jnp.float32)
        same = (seg_near[tap_index : tap_index + count] == seg_here)[:, None]
        total_acc = total_acc + jnp.where(same, window * kernel[tap_index].astype(jnp.float32), 0.0)
    return jax.nn.silu(total_acc).astype(jnp.bfloat16)


def on_device(ring, paired, frames, lengths, ln1_gain, ln2_gain, w_qkv, w_out, w_glu, dw_kernel, w_proj):
    frame_rows = frames.shape[1]
    model_width = frames.shape[2]
    seq_count = lax.axis_size("seq")
    group_rows = frame_rows * seq_count
    group_width = model_width // seq_count
    kernel_reach = dw_kernel.shape[0] // 2
    qkv_parts = ring_gather(w_qkv.reshape(w_qkv.shape[0], 3 * group_width), ring)
    qkv_matrix = qkv_parts.reshape(model_width, 3 * group_width)
    out_parts = ring_gather(after(qkv_parts, w_out.T), ring)
    out_cols = out_parts.reshape(model_width, w_out.shape[0])
    glu_rows = w_glu.shape[0]
    glu_local = w_glu.reshape(glu_rows, 2 * group_width)
    both_parts = ring_gather(after(out_parts, jnp.concatenate([glu_local, w_proj.T], axis=1)), ring)
    glu_matrix = both_parts[:, :, : 2 * group_width].reshape(model_width, 2 * group_width)
    proj_cols = both_parts[:, :, 2 * group_width :].reshape(model_width, w_proj.shape[0])
    inputs = frames[0].astype(jnp.float32)
    record_ends = jnp.cumsum(lengths[0])
    seg_all = segment_of(record_ends, jnp.arange(group_rows, dtype=jnp.int32))
    normed1 = layer_norm(inputs, ln1_gain)
    projected = (
        jnp.dot(seq_gather(normed1, paired).reshape(group_rows, model_width), qkv_matrix, preferred_element_type=jnp.float32)
        .astype(jnp.bfloat16)
        .reshape(group_rows, 3, group_width)
    )
    attended = attend(projected, seg_all, HD)
    attn_sum = seq_scatter_sum(
        jnp.dot(attended, out_cols.T, preferred_element_type=jnp.float32).astype(jnp.bfloat16),
        paired,
    )
    middle = (inputs + attn_sum).astype(jnp.bfloat16)
    normed2 = layer_norm(middle.astype(jnp.float32), ln2_gain)
    shard_piece = seq_gather(normed2, paired).reshape(group_rows, model_width)
    glu_pair = jnp.dot(shard_piece, glu_matrix, preferred_element_type=jnp.float32).reshape(
        shard_piece.shape[0], 2, group_width
    )
    gated = (glu_pair[:, 0] * jax.nn.sigmoid(glu_pair[:, 1])).astype(jnp.bfloat16)
    padded = jnp.pad(gated, ((kernel_reach, kernel_reach), (0, 0)))
    near_positions = jnp.arange(-kernel_reach, group_rows + kernel_reach, dtype=jnp.int32)
    activated = depthwise(
        padded, dw_kernel, seg_all, segment_of(record_ends, near_positions), group_rows
    )
    activated = lax.optimization_barrier(activated)
    conv_out = seq_scatter_sum(
        jnp.dot(activated, proj_cols.T, preferred_element_type=jnp.float32).astype(jnp.bfloat16),
        paired,
    )
    results = [(middle.astype(jnp.float32) + conv_out).astype(jnp.bfloat16)]
    return jnp.stack(results, axis=0)


def solution(mesh):
    in_specs = (
        P("dp", "seq", None),
        P("dp", None),
        P(),
        P(),
        P("dp", None, "seq"),
        P("seq", "dp"),
        P("dp", None, "seq"),
        P(None, "seq"),
        P("seq", "dp"),
    )
    out_specs = P("dp", "seq", None)
    return jax.shard_map(
        functools.partial(on_device, dp_ring(mesh), cores_paired(mesh)), mesh=mesh, in_specs=in_specs, out_specs=out_specs, check_vma=False
    )
```

```python
import functools

import jax
import jax.numpy as jnp
from jax import lax
from jax.sharding import PartitionSpec as P

HD = 96


def layer_norm(values, gain_vec):
    mean_value = jnp.mean(values, axis=-1, keepdims=True)
    centered = values - mean_value
    variance = jnp.mean(centered * centered, axis=-1, keepdims=True)
    return (centered * lax.rsqrt(variance + 1e-05) * gain_vec).astype(jnp.bfloat16)


def segment_of(record_ends, positions):
    return jnp.sum((positions[:, None] >= record_ends[None, :]).astype(jnp.int32), axis=1)


def seq_gather(block, paired):
    count = lax.axis_size("seq")
    me = lax.axis_index("seq")
    out = jnp.zeros((count,) + block.shape, block.dtype)
    out = lax.dynamic_update_index_in_dim(out, block, me, 0)
    if not paired:
        for shift in range(1, count):
            got = lax.ppermute(block, "seq", [(i, (i + shift) % count) for i in range(count)])
            out = lax.dynamic_update_index_in_dim(out, got, (me - shift) % count, 0)
        return out
    half = count // 2
    mine = jnp.zeros((half,) + block.shape, block.dtype)
    mine = lax.dynamic_update_index_in_dim(mine, block, me // 2, 0)
    for shift in range(1, half):
        got = lax.ppermute(
            block, "seq", [(i, (i + 2 * shift) % count) for i in range(count)]
        )
        src_dev = (me - 2 * shift) % count
        mine = lax.dynamic_update_index_in_dim(mine, got, src_dev // 2, 0)
        out = lax.dynamic_update_index_in_dim(out, got, src_dev, 0)
    other = lax.ppermute(mine, "seq", [(i, i ^ 1) for i in range(count)])
    partner = me ^ 1
    for k in range(half):
        out = lax.dynamic_update_index_in_dim(out, other[k], 2 * k + partner % 2, 0)
    return out


def cores_paired(mesh):
    count = mesh.shape["seq"]
    if count % 2:
        return False
    try:
        row = mesh.devices[0]
        return all(
            tuple(row[2 * k].coords) == tuple(row[2 * k + 1].coords) for k in range(count // 2)
        )
    except (AttributeError, TypeError, IndexError):
        return False


def seq_scatter_sum(full, paired):
    count = lax.axis_size("seq")
    me = lax.axis_index("seq")
    rows = full.shape[0] // count
    if not paired:
        total = lax.dynamic_slice_in_dim(full, me * rows, rows, axis=0).astype(jnp.float32)
        for shift in range(1, count):
            piece = lax.dynamic_slice_in_dim(full, ((me + shift) % count) * rows, rows, axis=0)
            got = lax.ppermute(piece, "seq", [(i, (i + shift) % count) for i in range(count)])
            total = total + got.astype(jnp.float32)
        return total
    half = count // 2
    core = me % 2
    quads = full.reshape(half, 2, rows, full.shape[1])
    mine = lax.dynamic_index_in_dim(quads, core, axis=1, keepdims=False)
    theirs = lax.dynamic_index_in_dim(quads, 1 - core, axis=1, keepdims=False)
    got = lax.ppermute(theirs, "seq", [(i, i ^ 1) for i in range(count)])
    chip_sum = mine.astype(jnp.float32) + got.astype(jnp.float32)
    here = me // 2
    total = lax.dynamic_index_in_dim(chip_sum, here, axis=0, keepdims=False)
    for shift in range(1, half):
        piece = lax.dynamic_index_in_dim(chip_sum, (here + shift) % half, axis=0, keepdims=False)
        got = lax.ppermute(
            piece.astype(jnp.bfloat16),
            "seq",
            [(i, (i + 2 * shift) % count) for i in range(count)],
        )
        total = total + got.astype(jnp.float32)
    return total


def dp_ring(mesh):
    count = mesh.shape["dp"]
    plain = list(range(count))
    try:
        coords = [tuple(int(c) for c in d.coords) for d in mesh.devices[:, 0]]
    except (AttributeError, TypeError, IndexError):
        return plain
    axes = [k for k in range(len(coords[0])) if len({c[k] for c in coords}) > 1]
    if len(axes) != 2:
        return plain
    low = [min(c[k] for c in coords) for k in axes]
    spots = {(c[axes[0]] - low[0], c[axes[1]] - low[1]): i for i, c in enumerate(coords)}
    sizes = [len({c[k] for c in coords}) for k in axes]
    if sizes[0] * sizes[1] != count or len(spots) != count:
        return plain
    if sizes[0] % 2 == 0:
        first, second, swap = sizes[0], sizes[1], False
    elif sizes[1] % 2 == 0:
        first, second, swap = sizes[1], sizes[0], True
    else:
        return plain
    path = [(0, 0)]
    for a in range(first):
        cols = range(1, second) if a % 2 == 0 else range(second - 1, 0, -1)
        path += [(a, b) for b in cols]
    path += [(a, 0) for a in range(first - 1, 0, -1)]
    if swap:
        path = [(b, a) for a, b in path]
    cycle = [spots.get(p) for p in path]
    if None in cycle or sorted(cycle) != plain:
        return plain
    return cycle


def ring_gather(block, ring):
    count = len(ring)
    me = lax.axis_index("dp")
    my_pos = jnp.asarray([ring.index(i) for i in range(count)], jnp.int32)[me]
    order = jnp.asarray(ring, jnp.int32)
    forward = [(ring[p], ring[(p + 1) % count]) for p in range(count)]
    backward = [(ring[p], ring[(p - 1) % count]) for p in range(count)]
    out = jnp.zeros((count,) + block.shape, block.dtype)
    out = lax.dynamic_update_index_in_dim(out, block, me, 0)
    ahead = behind = block
    for step in range(1, count // 2 + 1):
        ahead = lax.ppermute(ahead, "dp", forward)
        out = lax.dynamic_update_index_in_dim(out, ahead, order[(my_pos - step) % count], 0)
        if step <= count - 1 - count // 2:
            behind = lax.ppermute(behind, "dp", backward)
            out = lax.dynamic_update_index_in_dim(out, behind, order[(my_pos + step) % count], 0)
    return out


def after(token, value):
    return lax.optimization_barrier((token, value))[1]


def attend(projected, seg_all, head_size):
    group_rows = projected.shape[0]
    block_rows = 512
    heads_here = projected.shape[2] // head_size
    split = projected.reshape(group_rows, 3, heads_here, head_size)
    queries = split[:, 0]
    keys = split[:, 1]
    values = split[:, 2]
    blocks = group_rows // block_rows
    scale = 1.0 / head_size**0.5

    def one_block(block_data):
        query_block, seg_block = block_data
        scores = (
            jnp.einsum("qhe,khe->hqk", query_block, keys, preferred_element_type=jnp.float32)
            * scale
        )
        allowed = seg_block[:, None] == seg_all[None, :]
        scores = jnp.where(allowed[None], scores, -1e30)
        top_score = jnp.max(scores, axis=-1, keepdims=True)
        weights = jnp.exp(scores - top_score)
        probs = (weights / jnp.sum(weights, axis=-1, keepdims=True)).astype(jnp.bfloat16)
        mixed = jnp.einsum("hqk,khe->qhe", probs, values, preferred_element_type=jnp.float32)
        return mixed.astype(jnp.bfloat16).reshape(block_rows, heads_here * head_size)

    result = lax.map(
        one_block,
        (
            queries.reshape(blocks, block_rows, heads_here, head_size),
            seg_all.reshape(blocks, block_rows),
        ),
    )
    return result.reshape(group_rows, heads_here * head_size)


def depthwise(padded, kernel, seg_here, seg_near, count):
    total_acc = jnp.zeros((count, padded.shape[1]), jnp.float32)
    for tap_index in range(kernel.shape[0]):
        window = padded[tap_index : tap_index + count].astype(jnp.float32)
        same = (seg_near[tap_index : tap_index + count] == seg_here)[:, None]
        total_acc = total_acc + jnp.where(same, window * kernel[tap_index].astype(jnp.float32), 0.0)
    return jax.nn.silu(total_acc).astype(jnp.bfloat16)


def on_device(ring, paired, frames, lengths, ln1_gain, ln2_gain, w_qkv, w_out, w_glu, dw_kernel, w_proj):
    frame_rows = frames.shape[1]
    model_width = frames.shape[2]
    seq_count = lax.axis_size("seq")
    group_rows = frame_rows * seq_count
    group_width = model_width // seq_count
    kernel_reach = dw_kernel.shape[0] // 2
    qkv_local = w_qkv.reshape(w_qkv.shape[0], 3 * group_width)
    out_parts = ring_gather(jnp.concatenate([qkv_local, w_out.T], axis=1), ring)
    qkv_matrix = out_parts[:, :, : 3 * group_width].reshape(model_width, 3 * group_width)
    out_cols = out_parts[:, :, 3 * group_width :].reshape(model_width, w_out.shape[0])
    glu_rows = w_glu.shape[0]
    glu_local = w_glu.reshape(glu_rows, 2 * group_width)
    both_parts = ring_gather(after(out_parts, jnp.concatenate([glu_local, w_proj.T], axis=1)), ring)
    glu_matrix = both_parts[:, :, : 2 * group_width].reshape(model_width, 2 * group_width)
    proj_cols = both_parts[:, :, 2 * group_width :].reshape(model_width, w_proj.shape[0])
    inputs = frames[0].astype(jnp.float32)
    record_ends = jnp.cumsum(lengths[0])
    seg_all = segment_of(record_ends, jnp.arange(group_rows, dtype=jnp.int32))
    normed1 = layer_norm(inputs, ln1_gain)
    projected = (
        jnp.dot(seq_gather(normed1, paired).reshape(group_rows, model_width), qkv_matrix, preferred_element_type=jnp.float32)
        .astype(jnp.bfloat16)
        .reshape(group_rows, 3, group_width)
    )
    attended = attend(projected, seg_all, HD)
    attn_sum = seq_scatter_sum(
        jnp.dot(attended, out_cols.T, preferred_element_type=jnp.float32).astype(jnp.bfloat16),
        paired,
    )
    middle = (inputs + attn_sum).astype(jnp.bfloat16)
    normed2 = layer_norm(middle.astype(jnp.float32), ln2_gain)
    shard_piece = seq_gather(normed2, paired).reshape(group_rows, model_width)
    glu_pair = jnp.dot(shard_piece, glu_matrix, preferred_element_type=jnp.float32).reshape(
        shard_piece.shape[0], 2, group_width
    )
    gated = (glu_pair[:, 0] * jax.nn.sigmoid(glu_pair[:, 1])).astype(jnp.bfloat16)
    padded = jnp.pad(gated, ((kernel_reach, kernel_reach), (0, 0)))
    near_positions = jnp.arange(-kernel_reach, group_rows + kernel_reach, dtype=jnp.int32)
    activated = depthwise(
        padded, dw_kernel, seg_all, segment_of(record_ends, near_positions), group_rows
    )
    activated = lax.optimization_barrier(activated)
    conv_out = seq_scatter_sum(
        jnp.dot(activated, proj_cols.T, preferred_element_type=jnp.float32).astype(jnp.bfloat16),
        paired,
    )
    results = [(middle.astype(jnp.float32) + conv_out).astype(jnp.bfloat16)]
    return jnp.stack(results, axis=0)


def solution(mesh):
    in_specs = (
        P("dp", "seq", None),
        P("dp", None),
        P(),
        P(),
        P("dp", None, "seq"),
        P("seq", "dp"),
        P("dp", None, "seq"),
        P(None, "seq"),
        P("seq", "dp"),
    )
    out_specs = P("dp", "seq", None)
    return jax.shard_map(
        functools.partial(on_device, dp_ring(mesh), cores_paired(mesh)), mesh=mesh, in_specs=in_specs, out_specs=out_specs, check_vma=False
    )
```

```python
import functools

import jax
import jax.numpy as jnp
from jax import lax
from jax.sharding import PartitionSpec as P

HD = 96


def layer_norm(values, gain_vec):
    mean_value = jnp.mean(values, axis=-1, keepdims=True)
    centered = values - mean_value
    variance = jnp.mean(centered * centered, axis=-1, keepdims=True)
    return (centered * lax.rsqrt(variance + 1e-05) * gain_vec).astype(jnp.bfloat16)


def segment_of(record_ends, positions):
    return jnp.sum((positions[:, None] >= record_ends[None, :]).astype(jnp.int32), axis=1)


def seq_gather(block, paired):
    count = lax.axis_size("seq")
    me = lax.axis_index("seq")
    out = jnp.zeros((count,) + block.shape, block.dtype)
    out = lax.dynamic_update_index_in_dim(out, block, me, 0)
    if not paired:
        for shift in range(1, count):
            got = lax.ppermute(block, "seq", [(i, (i + shift) % count) for i in range(count)])
            out = lax.dynamic_update_index_in_dim(out, got, (me - shift) % count, 0)
        return out
    half = count // 2
    mine = jnp.zeros((half,) + block.shape, block.dtype)
    mine = lax.dynamic_update_index_in_dim(mine, block, me // 2, 0)
    for shift in range(1, half):
        got = lax.ppermute(
            block, "seq", [(i, (i + 2 * shift) % count) for i in range(count)]
        )
        src_dev = (me - 2 * shift) % count
        mine = lax.dynamic_update_index_in_dim(mine, got, src_dev // 2, 0)
        out = lax.dynamic_update_index_in_dim(out, got, src_dev, 0)
    other = lax.ppermute(mine, "seq", [(i, i ^ 1) for i in range(count)])
    partner = me ^ 1
    for k in range(half):
        out = lax.dynamic_update_index_in_dim(out, other[k], 2 * k + partner % 2, 0)
    return out


def cores_paired(mesh):
    count = mesh.shape["seq"]
    if count % 2:
        return False
    try:
        row = mesh.devices[0]
        return all(
            tuple(row[2 * k].coords) == tuple(row[2 * k + 1].coords) for k in range(count // 2)
        )
    except (AttributeError, TypeError, IndexError):
        return False


def seq_scatter_sum(full, paired):
    count = lax.axis_size("seq")
    me = lax.axis_index("seq")
    rows = full.shape[0] // count
    if not paired:
        total = lax.dynamic_slice_in_dim(full, me * rows, rows, axis=0).astype(jnp.float32)
        for shift in range(1, count):
            piece = lax.dynamic_slice_in_dim(full, ((me + shift) % count) * rows, rows, axis=0)
            got = lax.ppermute(piece, "seq", [(i, (i + shift) % count) for i in range(count)])
            total = total + got.astype(jnp.float32)
        return total
    half = count // 2
    core = me % 2
    quads = full.reshape(half, 2, rows, full.shape[1])
    mine = lax.dynamic_index_in_dim(quads, core, axis=1, keepdims=False)
    theirs = lax.dynamic_index_in_dim(quads, 1 - core, axis=1, keepdims=False)
    got = lax.ppermute(theirs, "seq", [(i, i ^ 1) for i in range(count)])
    chip_sum = mine.astype(jnp.float32) + got.astype(jnp.float32)
    here = me // 2
    total = lax.dynamic_index_in_dim(chip_sum, here, axis=0, keepdims=False)
    for shift in range(1, half):
        piece = lax.dynamic_index_in_dim(chip_sum, (here + shift) % half, axis=0, keepdims=False)
        got = lax.ppermute(
            piece.astype(jnp.bfloat16),
            "seq",
            [(i, (i + 2 * shift) % count) for i in range(count)],
        )
        total = total + got.astype(jnp.float32)
    return total


def dp_ring(mesh):
    count = mesh.shape["dp"]
    plain = list(range(count))
    try:
        coords = [tuple(int(c) for c in d.coords) for d in mesh.devices[:, 0]]
    except (AttributeError, TypeError, IndexError):
        return plain
    axes = [k for k in range(len(coords[0])) if len({c[k] for c in coords}) > 1]
    if len(axes) != 2:
        return plain
    low = [min(c[k] for c in coords) for k in axes]
    spots = {(c[axes[0]] - low[0], c[axes[1]] - low[1]): i for i, c in enumerate(coords)}
    sizes = [len({c[k] for c in coords}) for k in axes]
    if sizes[0] * sizes[1] != count or len(spots) != count:
        return plain
    if sizes[0] % 2 == 0:
        first, second, swap = sizes[0], sizes[1], False
    elif sizes[1] % 2 == 0:
        first, second, swap = sizes[1], sizes[0], True
    else:
        return plain
    path = [(0, 0)]
    for a in range(first):
        cols = range(1, second) if a % 2 == 0 else range(second - 1, 0, -1)
        path += [(a, b) for b in cols]
    path += [(a, 0) for a in range(first - 1, 0, -1)]
    if swap:
        path = [(b, a) for a, b in path]
    cycle = [spots.get(p) for p in path]
    if None in cycle or sorted(cycle) != plain:
        return plain
    return cycle


def ring_gather(block, ring, cuts):
    count = len(ring)
    me = lax.axis_index("dp")
    my_pos = jnp.asarray([ring.index(i) for i in range(count)], jnp.int32)[me]
    order = jnp.asarray(ring, jnp.int32)
    forward = [(ring[p], ring[(p + 1) % count]) for p in range(count)]
    backward = [(ring[p], ring[(p - 1) % count]) for p in range(count)]
    edges = [0] + list(cuts) + [block.shape[-1]]
    spans = list(zip(edges[:-1], edges[1:]))
    outs = [jnp.zeros((count,) + block.shape[:-1] + (hi - lo,), block.dtype) for lo, hi in spans]

    def place(outs, piece, where):
        return [
            lax.dynamic_update_index_in_dim(out, piece[..., lo:hi], where, 0)
            for out, (lo, hi) in zip(outs, spans)
        ]

    outs = place(outs, block, me)
    ahead = behind = block
    for step in range(1, count // 2 + 1):
        ahead = lax.ppermute(ahead, "dp", forward)
        outs = place(outs, ahead, order[(my_pos - step) % count])
        if step <= count - 1 - count // 2:
            behind = lax.ppermute(behind, "dp", backward)
            outs = place(outs, behind, order[(my_pos + step) % count])
    return outs


def after(token, value):
    return lax.optimization_barrier((token, value))[1]


def attend(projected, seg_all, head_size):
    group_rows = projected.shape[0]
    block_rows = 512
    heads_here = projected.shape[2] // head_size
    split = projected.reshape(group_rows, 3, heads_here, head_size)
    queries = split[:, 0]
    keys = split[:, 1]
    values = split[:, 2]
    blocks = group_rows // block_rows
    scale = 1.0 / head_size**0.5

    def one_block(block_data):
        query_block, seg_block = block_data
        scores = (
            jnp.einsum("qhe,khe->hqk", query_block, keys, preferred_element_type=jnp.float32)
            * scale
        )
        allowed = seg_block[:, None] == seg_all[None, :]
        scores = jnp.where(allowed[None], scores, -1e30)
        top_score = jnp.max(scores, axis=-1, keepdims=True)
        weights = jnp.exp(scores - top_score)
        probs = (weights / jnp.sum(weights, axis=-1, keepdims=True)).astype(jnp.bfloat16)
        mixed = jnp.einsum("hqk,khe->qhe", probs, values, preferred_element_type=jnp.float32)
        return mixed.astype(jnp.bfloat16).reshape(block_rows, heads_here * head_size)

    result = lax.map(
        one_block,
        (
            queries.reshape(blocks, block_rows, heads_here, head_size),
            seg_all.reshape(blocks, block_rows),
        ),
    )
    return result.reshape(group_rows, heads_here * head_size)


def depthwise(padded, kernel, seg_here, seg_near, count):
    total_acc = jnp.zeros((count, padded.shape[1]), jnp.float32)
    for tap_index in range(kernel.shape[0]):
        window = padded[tap_index : tap_index + count].astype(jnp.float32)
        same = (seg_near[tap_index : tap_index + count] == seg_here)[:, None]
        total_acc = total_acc + jnp.where(same, window * kernel[tap_index].astype(jnp.float32), 0.0)
    return jax.nn.silu(total_acc).astype(jnp.bfloat16)


def on_device(ring, paired, frames, lengths, ln1_gain, ln2_gain, w_qkv, w_out, w_glu, dw_kernel, w_proj):
    frame_rows = frames.shape[1]
    model_width = frames.shape[2]
    seq_count = lax.axis_size("seq")
    group_rows = frame_rows * seq_count
    group_width = model_width // seq_count
    kernel_reach = dw_kernel.shape[0] // 2
    qkv_local = w_qkv.reshape(w_qkv.shape[0], 3 * group_width)
    qkv_parts, out_parts = ring_gather(
        jnp.concatenate([qkv_local, w_out.T], axis=1), ring, [3 * group_width]
    )
    qkv_matrix = qkv_parts.reshape(model_width, 3 * group_width)
    out_cols = out_parts.reshape(model_width, w_out.shape[0])
    glu_rows = w_glu.shape[0]
    glu_local = w_glu.reshape(glu_rows, 2 * group_width)
    glu_parts, proj_parts = ring_gather(
        after(out_parts, jnp.concatenate([glu_local, w_proj.T], axis=1)), ring, [2 * group_width]
    )
    glu_matrix = glu_parts.reshape(model_width, 2 * group_width)
    proj_cols = proj_parts.reshape(model_width, w_proj.shape[0])
    inputs = frames[0].astype(jnp.float32)
    record_ends = jnp.cumsum(lengths[0])
    seg_all = segment_of(record_ends, jnp.arange(group_rows, dtype=jnp.int32))
    normed1 = layer_norm(inputs, ln1_gain)
    projected = (
        jnp.dot(seq_gather(normed1, paired).reshape(group_rows, model_width), qkv_matrix, preferred_element_type=jnp.float32)
        .astype(jnp.bfloat16)
        .reshape(group_rows, 3, group_width)
    )
    attended = attend(projected, seg_all, HD)
    attn_sum = seq_scatter_sum(
        jnp.dot(attended, out_cols.T, preferred_element_type=jnp.float32).astype(jnp.bfloat16),
        paired,
    )
    middle = (inputs + attn_sum).astype(jnp.bfloat16)
    normed2 = layer_norm(middle.astype(jnp.float32), ln2_gain)
    shard_piece = seq_gather(normed2, paired).reshape(group_rows, model_width)
    glu_pair = jnp.dot(shard_piece, glu_matrix, preferred_element_type=jnp.float32).reshape(
        shard_piece.shape[0], 2, group_width
    )
    gated = (glu_pair[:, 0] * jax.nn.sigmoid(glu_pair[:, 1])).astype(jnp.bfloat16)
    padded = jnp.pad(gated, ((kernel_reach, kernel_reach), (0, 0)))
    near_positions = jnp.arange(-kernel_reach, group_rows + kernel_reach, dtype=jnp.int32)
    activated = depthwise(
        padded, dw_kernel, seg_all, segment_of(record_ends, near_positions), group_rows
    )
    activated = lax.optimization_barrier(activated)
    conv_out = seq_scatter_sum(
        jnp.dot(activated, proj_cols.T, preferred_element_type=jnp.float32).astype(jnp.bfloat16),
        paired,
    )
    results = [(middle.astype(jnp.float32) + conv_out).astype(jnp.bfloat16)]
    return jnp.stack(results, axis=0)


def solution(mesh):
    in_specs = (
        P("dp", "seq", None),
        P("dp", None),
        P(),
        P(),
        P("dp", None, "seq"),
        P("seq", "dp"),
        P("dp", None, "seq"),
        P(None, "seq"),
        P("seq", "dp"),
    )
    out_specs = P("dp", "seq", None)
    return jax.shard_map(
        functools.partial(on_device, dp_ring(mesh), cores_paired(mesh)), mesh=mesh, in_specs=in_specs, out_specs=out_specs, check_vma=False
    )
```

```python
import functools

import jax
import jax.numpy as jnp
from jax import lax
from jax.sharding import PartitionSpec as P

HD = 96


def layer_norm(values, gain_vec):
    mean_value = jnp.mean(values, axis=-1, keepdims=True)
    centered = values - mean_value
    variance = jnp.mean(centered * centered, axis=-1, keepdims=True)
    return (centered * lax.rsqrt(variance + 1e-05) * gain_vec).astype(jnp.bfloat16)


def segment_of(record_ends, positions):
    return jnp.sum((positions[:, None] >= record_ends[None, :]).astype(jnp.int32), axis=1)


def seq_gather(block, paired):
    count = lax.axis_size("seq")
    me = lax.axis_index("seq")
    out = jnp.zeros((count,) + block.shape, block.dtype)
    out = lax.dynamic_update_index_in_dim(out, block, me, 0)
    if not paired:
        for shift in range(1, count):
            got = lax.ppermute(block, "seq", [(i, (i + shift) % count) for i in range(count)])
            out = lax.dynamic_update_index_in_dim(out, got, (me - shift) % count, 0)
        return out
    half = count // 2
    mine = jnp.zeros((half,) + block.shape, block.dtype)
    mine = lax.dynamic_update_index_in_dim(mine, block, me // 2, 0)
    for shift in range(1, half):
        got = lax.ppermute(
            block, "seq", [(i, (i + 2 * shift) % count) for i in range(count)]
        )
        src_dev = (me - 2 * shift) % count
        mine = lax.dynamic_update_index_in_dim(mine, got, src_dev // 2, 0)
        out = lax.dynamic_update_index_in_dim(out, got, src_dev, 0)
    other = lax.ppermute(mine, "seq", [(i, i ^ 1) for i in range(count)])
    partner = me ^ 1
    for k in range(half):
        out = lax.dynamic_update_index_in_dim(out, other[k], 2 * k + partner % 2, 0)
    return out


def cores_paired(mesh):
    count = mesh.shape["seq"]
    if count % 2:
        return False
    try:
        row = mesh.devices[0]
        return all(
            tuple(row[2 * k].coords) == tuple(row[2 * k + 1].coords) for k in range(count // 2)
        )
    except (AttributeError, TypeError, IndexError):
        return False


def seq_scatter_sum(full, paired):
    count = lax.axis_size("seq")
    me = lax.axis_index("seq")
    rows = full.shape[0] // count
    if not paired:
        total = lax.dynamic_slice_in_dim(full, me * rows, rows, axis=0).astype(jnp.float32)
        for shift in range(1, count):
            piece = lax.dynamic_slice_in_dim(full, ((me + shift) % count) * rows, rows, axis=0)
            got = lax.ppermute(piece, "seq", [(i, (i + shift) % count) for i in range(count)])
            total = total + got.astype(jnp.float32)
        return total
    half = count // 2
    core = me % 2
    quads = full.reshape(half, 2, rows, full.shape[1])
    mine = lax.dynamic_index_in_dim(quads, core, axis=1, keepdims=False)
    theirs = lax.dynamic_index_in_dim(quads, 1 - core, axis=1, keepdims=False)
    got = lax.ppermute(theirs, "seq", [(i, i ^ 1) for i in range(count)])
    chip_sum = mine.astype(jnp.float32) + got.astype(jnp.float32)
    here = me // 2
    total = lax.dynamic_index_in_dim(chip_sum, here, axis=0, keepdims=False)
    for shift in range(1, half):
        piece = lax.dynamic_index_in_dim(chip_sum, (here + shift) % half, axis=0, keepdims=False)
        got = lax.ppermute(
            piece.astype(jnp.bfloat16),
            "seq",
            [(i, (i + 2 * shift) % count) for i in range(count)],
        )
        total = total + got.astype(jnp.float32)
    return total


def dp_ring(mesh):
    count = mesh.shape["dp"]
    plain = list(range(count))
    try:
        coords = [tuple(int(c) for c in d.coords) for d in mesh.devices[:, 0]]
    except (AttributeError, TypeError, IndexError):
        return plain
    axes = [k for k in range(len(coords[0])) if len({c[k] for c in coords}) > 1]
    if len(axes) != 2:
        return plain
    low = [min(c[k] for c in coords) for k in axes]
    spots = {(c[axes[0]] - low[0], c[axes[1]] - low[1]): i for i, c in enumerate(coords)}
    sizes = [len({c[k] for c in coords}) for k in axes]
    if sizes[0] * sizes[1] != count or len(spots) != count:
        return plain
    if sizes[0] % 2 == 0:
        first, second, swap = sizes[0], sizes[1], False
    elif sizes[1] % 2 == 0:
        first, second, swap = sizes[1], sizes[0], True
    else:
        return plain
    path = [(0, 0)]
    for a in range(first):
        cols = range(1, second) if a % 2 == 0 else range(second - 1, 0, -1)
        path += [(a, b) for b in cols]
    path += [(a, 0) for a in range(first - 1, 0, -1)]
    if swap:
        path = [(b, a) for a, b in path]
    cycle = [spots.get(p) for p in path]
    if None in cycle or sorted(cycle) != plain:
        return plain
    return cycle


def ring_gather(block, ring, cuts):
    count = len(ring)
    me = lax.axis_index("dp")
    my_pos = jnp.asarray([ring.index(i) for i in range(count)], jnp.int32)[me]
    order = jnp.asarray(ring, jnp.int32)
    forward = [(ring[p], ring[(p + 1) % count]) for p in range(count)]
    backward = [(ring[p], ring[(p - 1) % count]) for p in range(count)]
    edges = [0] + list(cuts) + [block.shape[-1]]
    spans = list(zip(edges[:-1], edges[1:]))
    outs = [jnp.zeros((count,) + block.shape[:-1] + (hi - lo,), block.dtype) for lo, hi in spans]

    def place(outs, piece, where):
        return [
            lax.dynamic_update_index_in_dim(out, piece[..., lo:hi], where, 0)
            for out, (lo, hi) in zip(outs, spans)
        ]

    outs = place(outs, block, me)
    ahead = behind = block
    far = count // 2
    for step in range(1, far + 1):
        if step == far and count % 2 == 0:
            rows = block.shape[0] // 2
            where = order[(my_pos - step) % count]
            front = lax.ppermute(ahead[:rows], "dp", forward)
            back = lax.ppermute(behind[rows:], "dp", backward)
            outs = [
                lax.dynamic_update_slice(
                    lax.dynamic_update_slice(out, front[None, :, lo:hi], (where, 0, 0)),
                    back[None, :, lo:hi],
                    (where, rows, 0),
                )
                for out, (lo, hi) in zip(outs, spans)
            ]
            break
        ahead = lax.ppermute(ahead, "dp", forward)
        outs = place(outs, ahead, order[(my_pos - step) % count])
        if step < far or count % 2 == 1:
            behind = lax.ppermute(behind, "dp", backward)
            outs = place(outs, behind, order[(my_pos + step) % count])
    return outs


def after(token, value):
    return lax.optimization_barrier((token, value))[1]


def attend(projected, seg_all, head_size):
    group_rows = projected.shape[0]
    block_rows = 512
    heads_here = projected.shape[2] // head_size
    split = projected.reshape(group_rows, 3, heads_here, head_size)
    queries = split[:, 0]
    keys = split[:, 1]
    values = split[:, 2]
    blocks = group_rows // block_rows
    scale = 1.0 / head_size**0.5

    def one_block(block_data):
        query_block, seg_block = block_data
        scores = (
            jnp.einsum("qhe,khe->hqk", query_block, keys, preferred_element_type=jnp.float32)
            * scale
        )
        allowed = seg_block[:, None] == seg_all[None, :]
        scores = jnp.where(allowed[None], scores, -1e30)
        top_score = jnp.max(scores, axis=-1, keepdims=True)
        weights = jnp.exp(scores - top_score)
        probs = (weights / jnp.sum(weights, axis=-1, keepdims=True)).astype(jnp.bfloat16)
        mixed = jnp.einsum("hqk,khe->qhe", probs, values, preferred_element_type=jnp.float32)
        return mixed.astype(jnp.bfloat16).reshape(block_rows, heads_here * head_size)

    result = lax.map(
        one_block,
        (
            queries.reshape(blocks, block_rows, heads_here, head_size),
            seg_all.reshape(blocks, block_rows),
        ),
    )
    return result.reshape(group_rows, heads_here * head_size)


def depthwise(padded, kernel, seg_here, seg_near, count):
    total_acc = jnp.zeros((count, padded.shape[1]), jnp.float32)
    for tap_index in range(kernel.shape[0]):
        window = padded[tap_index : tap_index + count].astype(jnp.float32)
        same = (seg_near[tap_index : tap_index + count] == seg_here)[:, None]
        total_acc = total_acc + jnp.where(same, window * kernel[tap_index].astype(jnp.float32), 0.0)
    return jax.nn.silu(total_acc).astype(jnp.bfloat16)


def on_device(ring, paired, frames, lengths, ln1_gain, ln2_gain, w_qkv, w_out, w_glu, dw_kernel, w_proj):
    frame_rows = frames.shape[1]
    model_width = frames.shape[2]
    seq_count = lax.axis_size("seq")
    group_rows = frame_rows * seq_count
    group_width = model_width // seq_count
    kernel_reach = dw_kernel.shape[0] // 2
    qkv_local = w_qkv.reshape(w_qkv.shape[0], 3 * group_width)
    qkv_parts, out_parts = ring_gather(
        jnp.concatenate([qkv_local, w_out.T], axis=1), ring, [3 * group_width]
    )
    qkv_matrix = qkv_parts.reshape(model_width, 3 * group_width)
    out_cols = out_parts.reshape(model_width, w_out.shape[0])
    glu_rows = w_glu.shape[0]
    glu_local = w_glu.reshape(glu_rows, 2 * group_width)
    glu_parts, proj_parts = ring_gather(
        after(out_parts, jnp.concatenate([glu_local, w_proj.T], axis=1)), ring, [2 * group_width]
    )
    glu_matrix = glu_parts.reshape(model_width, 2 * group_width)
    proj_cols = proj_parts.reshape(model_width, w_proj.shape[0])
    inputs = frames[0].astype(jnp.float32)
    record_ends = jnp.cumsum(lengths[0])
    seg_all = segment_of(record_ends, jnp.arange(group_rows, dtype=jnp.int32))
    normed1 = layer_norm(inputs, ln1_gain)
    projected = (
        jnp.dot(seq_gather(normed1, paired).reshape(group_rows, model_width), qkv_matrix, preferred_element_type=jnp.float32)
        .astype(jnp.bfloat16)
        .reshape(group_rows, 3, group_width)
    )
    attended = attend(projected, seg_all, HD)
    attn_sum = seq_scatter_sum(
        jnp.dot(attended, out_cols.T, preferred_element_type=jnp.float32).astype(jnp.bfloat16),
        paired,
    )
    middle = (inputs + attn_sum).astype(jnp.bfloat16)
    normed2 = layer_norm(middle.astype(jnp.float32), ln2_gain)
    shard_piece = seq_gather(normed2, paired).reshape(group_rows, model_width)
    glu_pair = jnp.dot(shard_piece, glu_matrix, preferred_element_type=jnp.float32).reshape(
        shard_piece.shape[0], 2, group_width
    )
    gated = (glu_pair[:, 0] * jax.nn.sigmoid(glu_pair[:, 1])).astype(jnp.bfloat16)
    padded = jnp.pad(gated, ((kernel_reach, kernel_reach), (0, 0)))
    near_positions = jnp.arange(-kernel_reach, group_rows + kernel_reach, dtype=jnp.int32)
    activated = depthwise(
        padded, dw_kernel, seg_all, segment_of(record_ends, near_positions), group_rows
    )
    activated = lax.optimization_barrier(activated)
    conv_out = seq_scatter_sum(
        jnp.dot(activated, proj_cols.T, preferred_element_type=jnp.float32).astype(jnp.bfloat16),
        paired,
    )
    results = [(middle.astype(jnp.float32) + conv_out).astype(jnp.bfloat16)]
    return jnp.stack(results, axis=0)


def solution(mesh):
    in_specs = (
        P("dp", "seq", None),
        P("dp", None),
        P(),
        P(),
        P("dp", None, "seq"),
        P("seq", "dp"),
        P("dp", None, "seq"),
        P(None, "seq"),
        P("seq", "dp"),
    )
    out_specs = P("dp", "seq", None)
    return jax.shard_map(
        functools.partial(on_device, dp_ring(mesh), cores_paired(mesh)), mesh=mesh, in_specs=in_specs, out_specs=out_specs, check_vma=False
    )
```

```python
import functools

import jax
import jax.numpy as jnp
from jax import lax
from jax.sharding import PartitionSpec as P

HD = 96


def layer_norm(values, gain_vec):
    mean_value = jnp.mean(values, axis=-1, keepdims=True)
    centered = values - mean_value
    variance = jnp.mean(centered * centered, axis=-1, keepdims=True)
    return (centered * lax.rsqrt(variance + 1e-05) * gain_vec).astype(jnp.bfloat16)


def segment_of(record_ends, positions):
    return jnp.sum((positions[:, None] >= record_ends[None, :]).astype(jnp.int32), axis=1)


def seq_gather(block, paired):
    count = lax.axis_size("seq")
    me = lax.axis_index("seq")
    out = jnp.zeros((count,) + block.shape, block.dtype)
    out = lax.dynamic_update_index_in_dim(out, block, me, 0)
    if not paired:
        for shift in range(1, count):
            got = lax.ppermute(block, "seq", [(i, (i + shift) % count) for i in range(count)])
            out = lax.dynamic_update_index_in_dim(out, got, (me - shift) % count, 0)
        return out
    half = count // 2
    mine = jnp.zeros((half,) + block.shape, block.dtype)
    mine = lax.dynamic_update_index_in_dim(mine, block, me // 2, 0)
    for shift in range(1, half):
        got = lax.ppermute(
            block, "seq", [(i, (i + 2 * shift) % count) for i in range(count)]
        )
        src_dev = (me - 2 * shift) % count
        mine = lax.dynamic_update_index_in_dim(mine, got, src_dev // 2, 0)
        out = lax.dynamic_update_index_in_dim(out, got, src_dev, 0)
    other = lax.ppermute(mine, "seq", [(i, i ^ 1) for i in range(count)])
    partner = me ^ 1
    for k in range(half):
        out = lax.dynamic_update_index_in_dim(out, other[k], 2 * k + partner % 2, 0)
    return out


def cores_paired(mesh):
    count = mesh.shape["seq"]
    if count % 2:
        return False
    try:
        row = mesh.devices[0]
        return all(
            tuple(row[2 * k].coords) == tuple(row[2 * k + 1].coords) for k in range(count // 2)
        )
    except (AttributeError, TypeError, IndexError):
        return False


def seq_scatter_sum(full, paired):
    count = lax.axis_size("seq")
    me = lax.axis_index("seq")
    rows = full.shape[0] // count
    if not paired:
        total = lax.dynamic_slice_in_dim(full, me * rows, rows, axis=0).astype(jnp.float32)
        for shift in range(1, count):
            piece = lax.dynamic_slice_in_dim(full, ((me + shift) % count) * rows, rows, axis=0)
            got = lax.ppermute(piece, "seq", [(i, (i + shift) % count) for i in range(count)])
            total = total + got.astype(jnp.float32)
        return total
    half = count // 2
    core = me % 2
    quads = full.reshape(half, 2, rows, full.shape[1])
    mine = lax.dynamic_index_in_dim(quads, core, axis=1, keepdims=False)
    theirs = lax.dynamic_index_in_dim(quads, 1 - core, axis=1, keepdims=False)
    got = lax.ppermute(theirs, "seq", [(i, i ^ 1) for i in range(count)])
    chip_sum = mine.astype(jnp.float32) + got.astype(jnp.float32)
    here = me // 2
    total = lax.dynamic_index_in_dim(chip_sum, here, axis=0, keepdims=False)
    for shift in range(1, half):
        piece = lax.dynamic_index_in_dim(chip_sum, (here + shift) % half, axis=0, keepdims=False)
        got = lax.ppermute(
            piece.astype(jnp.bfloat16),
            "seq",
            [(i, (i + 2 * shift) % count) for i in range(count)],
        )
        total = total + got.astype(jnp.float32)
    return total


def dp_ring(mesh):
    count = mesh.shape["dp"]
    plain = list(range(count))
    try:
        coords = [tuple(int(c) for c in d.coords) for d in mesh.devices[:, 0]]
    except (AttributeError, TypeError, IndexError):
        return plain
    axes = [k for k in range(len(coords[0])) if len({c[k] for c in coords}) > 1]
    if len(axes) != 2:
        return plain
    low = [min(c[k] for c in coords) for k in axes]
    spots = {(c[axes[0]] - low[0], c[axes[1]] - low[1]): i for i, c in enumerate(coords)}
    sizes = [len({c[k] for c in coords}) for k in axes]
    if sizes[0] * sizes[1] != count or len(spots) != count:
        return plain
    if sizes[0] % 2 == 0:
        first, second, swap = sizes[0], sizes[1], False
    elif sizes[1] % 2 == 0:
        first, second, swap = sizes[1], sizes[0], True
    else:
        return plain
    path = [(0, 0)]
    for a in range(first):
        cols = range(1, second) if a % 2 == 0 else range(second - 1, 0, -1)
        path += [(a, b) for b in cols]
    path += [(a, 0) for a in range(first - 1, 0, -1)]
    if swap:
        path = [(b, a) for a, b in path]
    cycle = [spots.get(p) for p in path]
    if None in cycle or sorted(cycle) != plain:
        return plain
    return cycle


def ring_gather(block, ring, cuts):
    count = len(ring)
    me = lax.axis_index("dp")
    my_pos = jnp.asarray([ring.index(i) for i in range(count)], jnp.int32)[me]
    order = jnp.asarray(ring, jnp.int32)
    forward = [(ring[p], ring[(p + 1) % count]) for p in range(count)]
    backward = [(ring[p], ring[(p - 1) % count]) for p in range(count)]
    edges = [0] + list(cuts) + [block.shape[-1]]
    spans = list(zip(edges[:-1], edges[1:]))
    outs = [jnp.zeros((count,) + block.shape[:-1] + (hi - lo,), block.dtype) for lo, hi in spans]

    def place(outs, piece, where):
        return [
            lax.dynamic_update_index_in_dim(out, piece[..., lo:hi], where, 0)
            for out, (lo, hi) in zip(outs, spans)
        ]

    outs = place(outs, block, me)
    ahead = behind = block
    far = count // 2
    for step in range(1, far + 1):
        if step == far and count % 2 == 0:
            rows = block.shape[0] // 2
            where = order[(my_pos - step) % count]
            front = lax.ppermute(ahead[:rows], "dp", forward)
            back = lax.ppermute(behind[rows:], "dp", backward)
            outs = [
                lax.dynamic_update_slice(
                    lax.dynamic_update_slice(out, front[None, :, lo:hi], (where, 0, 0)),
                    back[None, :, lo:hi],
                    (where, rows, 0),
                )
                for out, (lo, hi) in zip(outs, spans)
            ]
            break
        ahead = lax.ppermute(ahead, "dp", forward)
        outs = place(outs, ahead, order[(my_pos - step) % count])
        if step < far or count % 2 == 1:
            behind = lax.ppermute(behind, "dp", backward)
            outs = place(outs, behind, order[(my_pos + step) % count])
    return outs


def after(token, value):
    return lax.optimization_barrier((token, value))[1]


def attend(projected, seg_all, head_size):
    group_rows = projected.shape[0]
    block_rows = 512
    heads_here = projected.shape[2] // head_size
    split = projected.reshape(group_rows, 3, heads_here, head_size)
    queries = split[:, 0]
    keys = split[:, 1]
    values = split[:, 2]
    blocks = group_rows // block_rows
    scale = 1.0 / head_size**0.5

    def one_block(block_data):
        query_block, seg_block = block_data
        scores = (
            jnp.einsum("qhe,khe->hqk", query_block, keys, preferred_element_type=jnp.float32)
            * scale
        )
        allowed = seg_block[:, None] == seg_all[None, :]
        scores = jnp.where(allowed[None], scores, -1e30)
        top_score = jnp.max(scores, axis=-1, keepdims=True)
        weights = jnp.exp(scores - top_score)
        probs = (weights / jnp.sum(weights, axis=-1, keepdims=True)).astype(jnp.bfloat16)
        mixed = jnp.einsum("hqk,khe->qhe", probs, values, preferred_element_type=jnp.float32)
        return mixed.astype(jnp.bfloat16).reshape(block_rows, heads_here * head_size)

    result = lax.map(
        one_block,
        (
            queries.reshape(blocks, block_rows, heads_here, head_size),
            seg_all.reshape(blocks, block_rows),
        ),
    )
    return result.reshape(group_rows, heads_here * head_size)


def depthwise(padded, kernel, seg_here, seg_near, count):
    total_acc = jnp.zeros((count, padded.shape[1]), jnp.float32)
    for tap_index in range(kernel.shape[0]):
        window = padded[tap_index : tap_index + count].astype(jnp.float32)
        same = (seg_near[tap_index : tap_index + count] == seg_here)[:, None]
        total_acc = total_acc + jnp.where(same, window * kernel[tap_index].astype(jnp.float32), 0.0)
    return jax.nn.silu(total_acc).astype(jnp.bfloat16)


def on_device(ring, paired, frames, lengths, ln1_gain, ln2_gain, w_qkv, w_out, w_glu, dw_kernel, w_proj):
    frame_rows = frames.shape[1]
    model_width = frames.shape[2]
    seq_count = lax.axis_size("seq")
    group_rows = frame_rows * seq_count
    group_width = model_width // seq_count
    kernel_reach = dw_kernel.shape[0] // 2
    qkv_local = w_qkv.reshape(w_qkv.shape[0], 3 * group_width)
    qkv_parts, out_parts = ring_gather(
        jnp.concatenate([qkv_local, w_out.T], axis=1), ring, [3 * group_width]
    )
    qkv_matrix = qkv_parts.reshape(model_width, 3 * group_width)
    out_cols = out_parts.reshape(model_width, w_out.shape[0])
    glu_rows = w_glu.shape[0]
    glu_local = w_glu.reshape(glu_rows, 2 * group_width)
    glu_parts, proj_parts = ring_gather(
        after(out_parts, jnp.concatenate([glu_local, w_proj.T], axis=1)), ring, [2 * group_width]
    )
    glu_matrix = glu_parts.reshape(model_width, 2 * group_width)
    proj_cols = proj_parts.reshape(model_width, w_proj.shape[0])
    inputs = frames[0].astype(jnp.float32)
    record_ends = jnp.cumsum(lengths[0])
    seg_all = segment_of(record_ends, jnp.arange(group_rows, dtype=jnp.int32))
    normed1 = layer_norm(inputs, ln1_gain)
    projected = (
        jnp.dot(seq_gather(normed1, paired).reshape(group_rows, model_width), qkv_matrix, preferred_element_type=jnp.float32)
        .astype(jnp.bfloat16)
        .reshape(group_rows, 3, group_width)
    )
    attended = attend(projected, seg_all, HD)
    attn_sum = seq_scatter_sum(
        jnp.dot(attended, out_cols.T, preferred_element_type=jnp.float32).astype(jnp.bfloat16),
        paired,
    )
    middle = (inputs + attn_sum).astype(jnp.bfloat16)
    normed2 = layer_norm(middle.astype(jnp.float32), ln2_gain)
    shard_piece = seq_gather(normed2, paired).reshape(group_rows, model_width)
    glu_pair = jnp.dot(shard_piece, glu_matrix, preferred_element_type=jnp.float32).reshape(
        shard_piece.shape[0], 2, group_width
    )
    gated = (glu_pair[:, 0] * jax.nn.sigmoid(glu_pair[:, 1])).astype(jnp.bfloat16)
    padded = jnp.pad(gated, ((kernel_reach, kernel_reach), (0, 0)))
    near_positions = jnp.arange(-kernel_reach, group_rows + kernel_reach, dtype=jnp.int32)
    near_segments = segment_of(record_ends, near_positions)
    if paired and seq_count == 4:
        chip_rows = group_rows // 2
        here = lax.axis_index("seq") // 2
        core = lax.axis_index("seq") % 2

        def conv_rows(first, source):
            window = lax.dynamic_slice_in_dim(source, first, chip_rows + 2 * kernel_reach, 0)
            near = lax.dynamic_slice_in_dim(near_segments, first, chip_rows + 2 * kernel_reach, 0)
            own = lax.dynamic_slice_in_dim(seg_all, first, chip_rows, 0)
            rows_out = depthwise(window, dw_kernel, own, near, chip_rows)
            rows_out = lax.optimization_barrier(rows_out)
            part = jnp.dot(rows_out, proj_cols.T, preferred_element_type=jnp.float32)
            part = part.astype(jnp.bfloat16).reshape(2, frame_rows, model_width)
            mine = lax.dynamic_index_in_dim(part, core, axis=0, keepdims=False)
            theirs = lax.dynamic_index_in_dim(part, 1 - core, axis=0, keepdims=False)
            got = lax.ppermute(theirs, "seq", [(i, i ^ 1) for i in range(seq_count)])
            return mine.astype(jnp.float32) + got.astype(jnp.float32)

        far_sum = conv_rows((1 - here) * chip_rows, padded)
        crossed = lax.ppermute(
            far_sum.astype(jnp.bfloat16), "seq", [(i, (i + 2) % seq_count) for i in range(seq_count)]
        )
        conv_out = conv_rows(here * chip_rows, after(far_sum, padded)) + crossed.astype(
            jnp.float32
        )
    else:
        activated = depthwise(padded, dw_kernel, seg_all, near_segments, group_rows)
        activated = lax.optimization_barrier(activated)
        conv_out = seq_scatter_sum(
            jnp.dot(activated, proj_cols.T, preferred_element_type=jnp.float32).astype(
                jnp.bfloat16
            ),
            paired,
        )
    results = [(middle.astype(jnp.float32) + conv_out).astype(jnp.bfloat16)]
    return jnp.stack(results, axis=0)


def solution(mesh):
    in_specs = (
        P("dp", "seq", None),
        P("dp", None),
        P(),
        P(),
        P("dp", None, "seq"),
        P("seq", "dp"),
        P("dp", None, "seq"),
        P(None, "seq"),
        P("seq", "dp"),
    )
    out_specs = P("dp", "seq", None)
    return jax.shard_map(
        functools.partial(on_device, dp_ring(mesh), cores_paired(mesh)), mesh=mesh, in_specs=in_specs, out_specs=out_specs, check_vma=False
    )
```

```python
import functools

import jax
import jax.numpy as jnp
from jax import lax
from jax.sharding import PartitionSpec as P

HD = 96


def layer_norm(values, gain_vec):
    mean_value = jnp.mean(values, axis=-1, keepdims=True)
    centered = values - mean_value
    variance = jnp.mean(centered * centered, axis=-1, keepdims=True)
    return (centered * lax.rsqrt(variance + 1e-05) * gain_vec).astype(jnp.bfloat16)


def segment_of(record_ends, positions):
    return jnp.sum((positions[:, None] >= record_ends[None, :]).astype(jnp.int32), axis=1)


def seq_gather(block, paired):
    count = lax.axis_size("seq")
    me = lax.axis_index("seq")
    out = jnp.zeros((count,) + block.shape, block.dtype)
    out = lax.dynamic_update_index_in_dim(out, block, me, 0)
    if not paired:
        for shift in range(1, count):
            got = lax.ppermute(block, "seq", [(i, (i + shift) % count) for i in range(count)])
            out = lax.dynamic_update_index_in_dim(out, got, (me - shift) % count, 0)
        return out
    half = count // 2
    mine = jnp.zeros((half,) + block.shape, block.dtype)
    mine = lax.dynamic_update_index_in_dim(mine, block, me // 2, 0)
    for shift in range(1, half):
        got = lax.ppermute(
            block, "seq", [(i, (i + 2 * shift) % count) for i in range(count)]
        )
        src_dev = (me - 2 * shift) % count
        mine = lax.dynamic_update_index_in_dim(mine, got, src_dev // 2, 0)
        out = lax.dynamic_update_index_in_dim(out, got, src_dev, 0)
    other = lax.ppermute(mine, "seq", [(i, i ^ 1) for i in range(count)])
    partner = me ^ 1
    for k in range(half):
        out = lax.dynamic_update_index_in_dim(out, other[k], 2 * k + partner % 2, 0)
    return out


def cores_paired(mesh):
    count = mesh.shape["seq"]
    if count % 2:
        return False
    try:
        row = mesh.devices[0]
        return all(
            tuple(row[2 * k].coords) == tuple(row[2 * k + 1].coords) for k in range(count // 2)
        )
    except (AttributeError, TypeError, IndexError):
        return False


def seq_scatter_sum(full, paired):
    count = lax.axis_size("seq")
    me = lax.axis_index("seq")
    rows = full.shape[0] // count
    if not paired:
        total = lax.dynamic_slice_in_dim(full, me * rows, rows, axis=0).astype(jnp.float32)
        for shift in range(1, count):
            piece = lax.dynamic_slice_in_dim(full, ((me + shift) % count) * rows, rows, axis=0)
            got = lax.ppermute(piece, "seq", [(i, (i + shift) % count) for i in range(count)])
            total = total + got.astype(jnp.float32)
        return total
    half = count // 2
    core = me % 2
    quads = full.reshape(half, 2, rows, full.shape[1])
    mine = lax.dynamic_index_in_dim(quads, core, axis=1, keepdims=False)
    theirs = lax.dynamic_index_in_dim(quads, 1 - core, axis=1, keepdims=False)
    got = lax.ppermute(theirs, "seq", [(i, i ^ 1) for i in range(count)])
    chip_sum = mine.astype(jnp.float32) + got.astype(jnp.float32)
    here = me // 2
    total = lax.dynamic_index_in_dim(chip_sum, here, axis=0, keepdims=False)
    for shift in range(1, half):
        piece = lax.dynamic_index_in_dim(chip_sum, (here + shift) % half, axis=0, keepdims=False)
        got = lax.ppermute(
            piece.astype(jnp.bfloat16),
            "seq",
            [(i, (i + 2 * shift) % count) for i in range(count)],
        )
        total = total + got.astype(jnp.float32)
    return total


def dp_ring(mesh):
    count = mesh.shape["dp"]
    plain = list(range(count))
    try:
        coords = [tuple(int(c) for c in d.coords) for d in mesh.devices[:, 0]]
    except (AttributeError, TypeError, IndexError):
        return plain
    axes = [k for k in range(len(coords[0])) if len({c[k] for c in coords}) > 1]
    if len(axes) != 2:
        return plain
    low = [min(c[k] for c in coords) for k in axes]
    spots = {(c[axes[0]] - low[0], c[axes[1]] - low[1]): i for i, c in enumerate(coords)}
    sizes = [len({c[k] for c in coords}) for k in axes]
    if sizes[0] * sizes[1] != count or len(spots) != count:
        return plain
    if sizes[0] % 2 == 0:
        first, second, swap = sizes[0], sizes[1], False
    elif sizes[1] % 2 == 0:
        first, second, swap = sizes[1], sizes[0], True
    else:
        return plain
    path = [(0, 0)]
    for a in range(first):
        cols = range(1, second) if a % 2 == 0 else range(second - 1, 0, -1)
        path += [(a, b) for b in cols]
    path += [(a, 0) for a in range(first - 1, 0, -1)]
    if swap:
        path = [(b, a) for a, b in path]
    cycle = [spots.get(p) for p in path]
    if None in cycle or sorted(cycle) != plain:
        return plain
    return cycle


def ring_gather(block, ring, cuts):
    count = len(ring)
    me = lax.axis_index("dp")
    my_pos = jnp.asarray([ring.index(i) for i in range(count)], jnp.int32)[me]
    order = jnp.asarray(ring, jnp.int32)
    forward = [(ring[p], ring[(p + 1) % count]) for p in range(count)]
    backward = [(ring[p], ring[(p - 1) % count]) for p in range(count)]
    edges = [0] + list(cuts) + [block.shape[-1]]
    spans = list(zip(edges[:-1], edges[1:]))
    outs = [jnp.zeros((count,) + block.shape[:-1] + (hi - lo,), block.dtype) for lo, hi in spans]

    def place(outs, piece, where):
        return [
            lax.dynamic_update_index_in_dim(out, piece[..., lo:hi], where, 0)
            for out, (lo, hi) in zip(outs, spans)
        ]

    outs = place(outs, block, me)
    ahead = behind = block
    far = count // 2
    for step in range(1, far + 1):
        if step == far and count % 2 == 0:
            rows = block.shape[0] // 2
            where = order[(my_pos - step) % count]
            front = lax.ppermute(ahead[:rows], "dp", forward)
            back = lax.ppermute(behind[rows:], "dp", backward)
            outs = [
                lax.dynamic_update_slice(
                    lax.dynamic_update_slice(out, front[None, :, lo:hi], (where, 0, 0)),
                    back[None, :, lo:hi],
                    (where, rows, 0),
                )
                for out, (lo, hi) in zip(outs, spans)
            ]
            break
        ahead = lax.ppermute(ahead, "dp", forward)
        outs = place(outs, ahead, order[(my_pos - step) % count])
        if step < far or count % 2 == 1:
            behind = lax.ppermute(behind, "dp", backward)
            outs = place(outs, behind, order[(my_pos + step) % count])
    return outs


def after(token, value):
    return lax.optimization_barrier((token, value))[1]


def attend(projected, seg_all, head_size):
    group_rows = projected.shape[0]
    block_rows = 512
    heads_here = projected.shape[2] // head_size
    split = projected.reshape(group_rows, 3, heads_here, head_size)
    queries = split[:, 0]
    keys = split[:, 1]
    values = split[:, 2]
    blocks = group_rows // block_rows
    scale = 1.0 / head_size**0.5

    def one_block(block_data):
        query_block, seg_block = block_data
        scores = (
            jnp.einsum("qhe,khe->hqk", query_block, keys, preferred_element_type=jnp.float32)
            * scale
        )
        allowed = seg_block[:, None] == seg_all[None, :]
        scores = jnp.where(allowed[None], scores, -1e30)
        top_score = jnp.max(scores, axis=-1, keepdims=True)
        weights = jnp.exp(scores - top_score)
        probs = (weights / jnp.sum(weights, axis=-1, keepdims=True)).astype(jnp.bfloat16)
        mixed = jnp.einsum("hqk,khe->qhe", probs, values, preferred_element_type=jnp.float32)
        return mixed.astype(jnp.bfloat16).reshape(block_rows, heads_here * head_size)

    result = lax.map(
        one_block,
        (
            queries.reshape(blocks, block_rows, heads_here, head_size),
            seg_all.reshape(blocks, block_rows),
        ),
    )
    return result.reshape(group_rows, heads_here * head_size)


def depthwise(padded, kernel, seg_here, seg_near, count):
    total_acc = jnp.zeros((count, padded.shape[1]), jnp.float32)
    for tap_index in range(kernel.shape[0]):
        window = padded[tap_index : tap_index + count].astype(jnp.float32)
        same = (seg_near[tap_index : tap_index + count] == seg_here)[:, None]
        total_acc = total_acc + jnp.where(same, window * kernel[tap_index].astype(jnp.float32), 0.0)
    return jax.nn.silu(total_acc).astype(jnp.bfloat16)


def on_device(ring, paired, frames, lengths, ln1_gain, ln2_gain, w_qkv, w_out, w_glu, dw_kernel, w_proj):
    frame_rows = frames.shape[1]
    model_width = frames.shape[2]
    seq_count = lax.axis_size("seq")
    group_rows = frame_rows * seq_count
    group_width = model_width // seq_count
    kernel_reach = dw_kernel.shape[0] // 2
    qkv_local = w_qkv.reshape(w_qkv.shape[0], 3 * group_width)
    qkv_parts, out_parts = ring_gather(
        jnp.concatenate([qkv_local, w_out.T], axis=1), ring, [3 * group_width]
    )
    qkv_matrix = qkv_parts.reshape(model_width, 3 * group_width)
    out_cols = out_parts.reshape(model_width, w_out.shape[0])
    glu_rows = w_glu.shape[0]
    glu_local = w_glu.reshape(glu_rows, 2 * group_width)
    glu_parts, proj_parts = ring_gather(
        after(out_parts, jnp.concatenate([glu_local, w_proj.T], axis=1)), ring, [2 * group_width]
    )
    glu_matrix = glu_parts.reshape(model_width, 2 * group_width)
    proj_cols = proj_parts.reshape(model_width, w_proj.shape[0])
    inputs = frames[0].astype(jnp.float32)
    record_ends = jnp.cumsum(lengths[0])
    seg_all = segment_of(record_ends, jnp.arange(group_rows, dtype=jnp.int32))
    normed1 = layer_norm(inputs, ln1_gain)
    projected = (
        jnp.dot(seq_gather(normed1, paired).reshape(group_rows, model_width), qkv_matrix, preferred_element_type=jnp.float32)
        .astype(jnp.bfloat16)
        .reshape(group_rows, 3, group_width)
    )
    attended = attend(projected, seg_all, HD)
    attn_sum = seq_scatter_sum(
        jnp.dot(attended, out_cols.T, preferred_element_type=jnp.float32).astype(jnp.bfloat16),
        paired,
    )
    middle = (inputs + attn_sum).astype(jnp.bfloat16)
    normed2 = layer_norm(middle.astype(jnp.float32), ln2_gain)
    shard_piece = seq_gather(normed2, paired).reshape(group_rows, model_width)
    glu_pair = jnp.dot(shard_piece, glu_matrix, preferred_element_type=jnp.float32).reshape(
        shard_piece.shape[0], 2, group_width
    )
    gated = (glu_pair[:, 0] * jax.nn.sigmoid(glu_pair[:, 1])).astype(jnp.bfloat16)
    padded = lax.optimization_barrier(
        jnp.pad(gated, ((kernel_reach, kernel_reach), (0, 0))).astype(jnp.float32)
    )
    near_positions = jnp.arange(-kernel_reach, group_rows + kernel_reach, dtype=jnp.int32)
    activated = depthwise(
        padded, dw_kernel, seg_all, segment_of(record_ends, near_positions), group_rows
    )
    activated = lax.optimization_barrier(activated)
    conv_out = seq_scatter_sum(
        jnp.dot(activated, proj_cols.T, preferred_element_type=jnp.float32).astype(jnp.bfloat16),
        paired,
    )
    results = [(middle.astype(jnp.float32) + conv_out).astype(jnp.bfloat16)]
    return jnp.stack(results, axis=0)


def solution(mesh):
    in_specs = (
        P("dp", "seq", None),
        P("dp", None),
        P(),
        P(),
        P("dp", None, "seq"),
        P("seq", "dp"),
        P("dp", None, "seq"),
        P(None, "seq"),
        P("seq", "dp"),
    )
    out_specs = P("dp", "seq", None)
    return jax.shard_map(
        functools.partial(on_device, dp_ring(mesh), cores_paired(mesh)), mesh=mesh, in_specs=in_specs, out_specs=out_specs, check_vma=False
    )
```

```python
import functools

import jax
import jax.numpy as jnp
from jax import lax
from jax.sharding import PartitionSpec as P

HD = 96


def layer_norm(values, gain_vec):
    mean_value = jnp.mean(values, axis=-1, keepdims=True)
    centered = values - mean_value
    variance = jnp.mean(centered * centered, axis=-1, keepdims=True)
    return (centered * lax.rsqrt(variance + 1e-05) * gain_vec).astype(jnp.bfloat16)


def segment_of(record_ends, positions):
    return jnp.sum((positions[:, None] >= record_ends[None, :]).astype(jnp.int32), axis=1)


def seq_gather(block, paired):
    count = lax.axis_size("seq")
    me = lax.axis_index("seq")
    out = jnp.zeros((count,) + block.shape, block.dtype)
    out = lax.dynamic_update_index_in_dim(out, block, me, 0)
    if not paired:
        for shift in range(1, count):
            got = lax.ppermute(block, "seq", [(i, (i + shift) % count) for i in range(count)])
            out = lax.dynamic_update_index_in_dim(out, got, (me - shift) % count, 0)
        return out
    half = count // 2
    mine = jnp.zeros((half,) + block.shape, block.dtype)
    mine = lax.dynamic_update_index_in_dim(mine, block, me // 2, 0)
    for shift in range(1, half):
        got = lax.ppermute(
            block, "seq", [(i, (i + 2 * shift) % count) for i in range(count)]
        )
        src_dev = (me - 2 * shift) % count
        mine = lax.dynamic_update_index_in_dim(mine, got, src_dev // 2, 0)
        out = lax.dynamic_update_index_in_dim(out, got, src_dev, 0)
    other = lax.ppermute(mine, "seq", [(i, i ^ 1) for i in range(count)])
    partner = me ^ 1
    for k in range(half):
        out = lax.dynamic_update_index_in_dim(out, other[k], 2 * k + partner % 2, 0)
    return out


def cores_paired(mesh):
    count = mesh.shape["seq"]
    if count % 2:
        return False
    try:
        row = mesh.devices[0]
        return all(
            tuple(row[2 * k].coords) == tuple(row[2 * k + 1].coords) for k in range(count // 2)
        )
    except (AttributeError, TypeError, IndexError):
        return False


def seq_scatter_sum(full, paired):
    count = lax.axis_size("seq")
    me = lax.axis_index("seq")
    rows = full.shape[0] // count
    if not paired:
        total = lax.dynamic_slice_in_dim(full, me * rows, rows, axis=0).astype(jnp.float32)
        for shift in range(1, count):
            piece = lax.dynamic_slice_in_dim(full, ((me + shift) % count) * rows, rows, axis=0)
            got = lax.ppermute(piece, "seq", [(i, (i + shift) % count) for i in range(count)])
            total = total + got.astype(jnp.float32)
        return total
    half = count // 2
    core = me % 2
    quads = full.reshape(half, 2, rows, full.shape[1])
    mine = lax.dynamic_index_in_dim(quads, core, axis=1, keepdims=False)
    theirs = lax.dynamic_index_in_dim(quads, 1 - core, axis=1, keepdims=False)
    got = lax.ppermute(theirs, "seq", [(i, i ^ 1) for i in range(count)])
    chip_sum = mine.astype(jnp.float32) + got.astype(jnp.float32)
    here = me // 2
    total = lax.dynamic_index_in_dim(chip_sum, here, axis=0, keepdims=False)
    for shift in range(1, half):
        piece = lax.dynamic_index_in_dim(chip_sum, (here + shift) % half, axis=0, keepdims=False)
        got = lax.ppermute(
            piece.astype(jnp.bfloat16),
            "seq",
            [(i, (i + 2 * shift) % count) for i in range(count)],
        )
        total = total + got.astype(jnp.float32)
    return total


def dp_ring(mesh):
    count = mesh.shape["dp"]
    plain = list(range(count))
    try:
        coords = [tuple(int(c) for c in d.coords) for d in mesh.devices[:, 0]]
    except (AttributeError, TypeError, IndexError):
        return plain
    axes = [k for k in range(len(coords[0])) if len({c[k] for c in coords}) > 1]
    if len(axes) != 2:
        return plain
    low = [min(c[k] for c in coords) for k in axes]
    spots = {(c[axes[0]] - low[0], c[axes[1]] - low[1]): i for i, c in enumerate(coords)}
    sizes = [len({c[k] for c in coords}) for k in axes]
    if sizes[0] * sizes[1] != count or len(spots) != count:
        return plain
    if sizes[0] % 2 == 0:
        first, second, swap = sizes[0], sizes[1], False
    elif sizes[1] % 2 == 0:
        first, second, swap = sizes[1], sizes[0], True
    else:
        return plain
    path = [(0, 0)]
    for a in range(first):
        cols = range(1, second) if a % 2 == 0 else range(second - 1, 0, -1)
        path += [(a, b) for b in cols]
    path += [(a, 0) for a in range(first - 1, 0, -1)]
    if swap:
        path = [(b, a) for a, b in path]
    cycle = [spots.get(p) for p in path]
    if None in cycle or sorted(cycle) != plain:
        return plain
    return cycle


def ring_gather(block, ring, cuts):
    count = len(ring)
    me = lax.axis_index("dp")
    my_pos = jnp.asarray([ring.index(i) for i in range(count)], jnp.int32)[me]
    order = jnp.asarray(ring, jnp.int32)
    forward = [(ring[p], ring[(p + 1) % count]) for p in range(count)]
    backward = [(ring[p], ring[(p - 1) % count]) for p in range(count)]
    edges = [0] + list(cuts) + [block.shape[-1]]
    spans = list(zip(edges[:-1], edges[1:]))
    outs = [jnp.zeros((count,) + block.shape[:-1] + (hi - lo,), block.dtype) for lo, hi in spans]

    def place(outs, piece, where):
        return [
            lax.dynamic_update_index_in_dim(out, piece[..., lo:hi], where, 0)
            for out, (lo, hi) in zip(outs, spans)
        ]

    outs = place(outs, block, me)
    ahead = behind = block
    far = count // 2
    for step in range(1, far + 1):
        if step == far and count % 2 == 0:
            rows = block.shape[0] // 2
            where = order[(my_pos - step) % count]
            front = lax.ppermute(ahead[:rows], "dp", forward)
            back = lax.ppermute(behind[rows:], "dp", backward)
            outs = [
                lax.dynamic_update_slice(
                    lax.dynamic_update_slice(out, front[None, :, lo:hi], (where, 0, 0)),
                    back[None, :, lo:hi],
                    (where, rows, 0),
                )
                for out, (lo, hi) in zip(outs, spans)
            ]
            break
        ahead = lax.ppermute(ahead, "dp", forward)
        outs = place(outs, ahead, order[(my_pos - step) % count])
        if step < far or count % 2 == 1:
            behind = lax.ppermute(behind, "dp", backward)
            outs = place(outs, behind, order[(my_pos + step) % count])
    return outs


def after(token, value):
    return lax.optimization_barrier((token, value))[1]


def attend(projected, seg_all, head_size):
    group_rows = projected.shape[0]
    block_rows = 512
    heads_here = projected.shape[2] // head_size
    split = projected.reshape(group_rows, 3, heads_here, head_size)
    queries = split[:, 0]
    keys = split[:, 1]
    values = split[:, 2]
    blocks = group_rows // block_rows
    scale = 1.0 / head_size**0.5

    def one_block(block_data):
        query_block, seg_block = block_data
        scores = (
            jnp.einsum("qhe,khe->hqk", query_block, keys, preferred_element_type=jnp.float32)
            * scale
        )
        allowed = seg_block[:, None] == seg_all[None, :]
        scores = jnp.where(allowed[None], scores, -1e30)
        top_score = jnp.max(scores, axis=-1, keepdims=True)
        weights = jnp.exp(scores - top_score)
        probs = (weights / jnp.sum(weights, axis=-1, keepdims=True)).astype(jnp.bfloat16)
        mixed = jnp.einsum("hqk,khe->qhe", probs, values, preferred_element_type=jnp.float32)
        return mixed.astype(jnp.bfloat16).reshape(block_rows, heads_here * head_size)

    result = lax.map(
        one_block,
        (
            queries.reshape(blocks, block_rows, heads_here, head_size),
            seg_all.reshape(blocks, block_rows),
        ),
    )
    return result.reshape(group_rows, heads_here * head_size)


def depthwise(padded, kernel, seg_here, seg_near, count):
    total_acc = jnp.zeros((count, padded.shape[1]), jnp.float32)
    for tap_index in range(kernel.shape[0]):
        window = padded[tap_index : tap_index + count].astype(jnp.float32)
        same = (seg_near[tap_index : tap_index + count] == seg_here)[:, None]
        total_acc = total_acc + jnp.where(same, window * kernel[tap_index].astype(jnp.float32), 0.0)
    return jax.nn.silu(total_acc).astype(jnp.bfloat16)


def on_device(ring, paired, frames, lengths, ln1_gain, ln2_gain, w_qkv, w_out, w_glu, dw_kernel, w_proj):
    frame_rows = frames.shape[1]
    model_width = frames.shape[2]
    seq_count = lax.axis_size("seq")
    group_rows = frame_rows * seq_count
    group_width = model_width // seq_count
    kernel_reach = dw_kernel.shape[0] // 2
    qkv_local = w_qkv.reshape(w_qkv.shape[0], 3 * group_width)
    qkv_parts, out_parts = ring_gather(
        jnp.concatenate([qkv_local, w_out.T], axis=1), ring, [3 * group_width]
    )
    qkv_matrix = qkv_parts.reshape(model_width, 3 * group_width)
    out_cols = out_parts.reshape(model_width, w_out.shape[0])
    glu_rows = w_glu.shape[0]
    glu_local = w_glu.reshape(glu_rows, 2 * group_width)
    value_parts, gate_parts, proj_parts = ring_gather(
        after(out_parts, jnp.concatenate([glu_local, w_proj.T], axis=1)),
        ring,
        [group_width, 2 * group_width],
    )
    value_matrix = value_parts.reshape(model_width, group_width)
    gate_matrix = gate_parts.reshape(model_width, group_width)
    proj_cols = proj_parts.reshape(model_width, w_proj.shape[0])
    inputs = frames[0].astype(jnp.float32)
    record_ends = jnp.cumsum(lengths[0])
    seg_all = segment_of(record_ends, jnp.arange(group_rows, dtype=jnp.int32))
    normed1 = layer_norm(inputs, ln1_gain)
    projected = (
        jnp.dot(seq_gather(normed1, paired).reshape(group_rows, model_width), qkv_matrix, preferred_element_type=jnp.float32)
        .astype(jnp.bfloat16)
        .reshape(group_rows, 3, group_width)
    )
    attended = attend(projected, seg_all, HD)
    attn_sum = seq_scatter_sum(
        jnp.dot(attended, out_cols.T, preferred_element_type=jnp.float32).astype(jnp.bfloat16),
        paired,
    )
    middle = (inputs + attn_sum).astype(jnp.bfloat16)
    normed2 = layer_norm(middle.astype(jnp.float32), ln2_gain)
    shard_piece = seq_gather(normed2, paired).reshape(group_rows, model_width)
    glu_value = jnp.dot(shard_piece, value_matrix, preferred_element_type=jnp.float32)
    glu_gate = jnp.dot(shard_piece, gate_matrix, preferred_element_type=jnp.float32)
    gated = (glu_value * jax.nn.sigmoid(glu_gate)).astype(jnp.bfloat16)
    padded = jnp.pad(gated, ((kernel_reach, kernel_reach), (0, 0)))
    near_positions = jnp.arange(-kernel_reach, group_rows + kernel_reach, dtype=jnp.int32)
    activated = depthwise(
        padded, dw_kernel, seg_all, segment_of(record_ends, near_positions), group_rows
    )
    activated = lax.optimization_barrier(activated)
    conv_out = seq_scatter_sum(
        jnp.dot(activated, proj_cols.T, preferred_element_type=jnp.float32).astype(jnp.bfloat16),
        paired,
    )
    results = [(middle.astype(jnp.float32) + conv_out).astype(jnp.bfloat16)]
    return jnp.stack(results, axis=0)


def solution(mesh):
    in_specs = (
        P("dp", "seq", None),
        P("dp", None),
        P(),
        P(),
        P("dp", None, "seq"),
        P("seq", "dp"),
        P("dp", None, "seq"),
        P(None, "seq"),
        P("seq", "dp"),
    )
    out_specs = P("dp", "seq", None)
    return jax.shard_map(
        functools.partial(on_device, dp_ring(mesh), cores_paired(mesh)), mesh=mesh, in_specs=in_specs, out_specs=out_specs, check_vma=False
    )
```

```python
import functools

import jax
import jax.numpy as jnp
from jax import lax
from jax.sharding import PartitionSpec as P

HD = 96


def layer_norm(values, gain_vec):
    mean_value = jnp.mean(values, axis=-1, keepdims=True)
    centered = values - mean_value
    variance = jnp.mean(centered * centered, axis=-1, keepdims=True)
    return (centered * lax.rsqrt(variance + 1e-05) * gain_vec).astype(jnp.bfloat16)


def segment_of(record_ends, positions):
    return jnp.sum((positions[:, None] >= record_ends[None, :]).astype(jnp.int32), axis=1)


def seq_gather(block, paired):
    count = lax.axis_size("seq")
    me = lax.axis_index("seq")
    out = jnp.zeros((count,) + block.shape, block.dtype)
    out = lax.dynamic_update_index_in_dim(out, block, me, 0)
    if not paired:
        for shift in range(1, count):
            got = lax.ppermute(block, "seq", [(i, (i + shift) % count) for i in range(count)])
            out = lax.dynamic_update_index_in_dim(out, got, (me - shift) % count, 0)
        return out
    half = count // 2
    mine = jnp.zeros((half,) + block.shape, block.dtype)
    mine = lax.dynamic_update_index_in_dim(mine, block, me // 2, 0)
    for shift in range(1, half):
        got = lax.ppermute(
            block, "seq", [(i, (i + 2 * shift) % count) for i in range(count)]
        )
        src_dev = (me - 2 * shift) % count
        mine = lax.dynamic_update_index_in_dim(mine, got, src_dev // 2, 0)
        out = lax.dynamic_update_index_in_dim(out, got, src_dev, 0)
    other = lax.ppermute(mine, "seq", [(i, i ^ 1) for i in range(count)])
    partner = me ^ 1
    for k in range(half):
        out = lax.dynamic_update_index_in_dim(out, other[k], 2 * k + partner % 2, 0)
    return out


def cores_paired(mesh):
    count = mesh.shape["seq"]
    if count % 2:
        return False
    try:
        row = mesh.devices[0]
        return all(
            tuple(row[2 * k].coords) == tuple(row[2 * k + 1].coords) for k in range(count // 2)
        )
    except (AttributeError, TypeError, IndexError):
        return False


def seq_scatter_sum(full, paired):
    count = lax.axis_size("seq")
    me = lax.axis_index("seq")
    rows = full.shape[0] // count
    if not paired:
        total = lax.dynamic_slice_in_dim(full, me * rows, rows, axis=0).astype(jnp.float32)
        for shift in range(1, count):
            piece = lax.dynamic_slice_in_dim(full, ((me + shift) % count) * rows, rows, axis=0)
            got = lax.ppermute(piece, "seq", [(i, (i + shift) % count) for i in range(count)])
            total = total + got.astype(jnp.float32)
        return total
    half = count // 2
    core = me % 2
    quads = full.reshape(half, 2, rows, full.shape[1])
    mine = lax.dynamic_index_in_dim(quads, core, axis=1, keepdims=False)
    theirs = lax.dynamic_index_in_dim(quads, 1 - core, axis=1, keepdims=False)
    got = lax.ppermute(theirs, "seq", [(i, i ^ 1) for i in range(count)])
    chip_sum = mine.astype(jnp.float32) + got.astype(jnp.float32)
    here = me // 2
    total = lax.dynamic_index_in_dim(chip_sum, here, axis=0, keepdims=False)
    for shift in range(1, half):
        piece = lax.dynamic_index_in_dim(chip_sum, (here + shift) % half, axis=0, keepdims=False)
        got = lax.ppermute(
            piece.astype(jnp.bfloat16),
            "seq",
            [(i, (i + 2 * shift) % count) for i in range(count)],
        )
        total = total + got.astype(jnp.float32)
    return total


def dp_ring(mesh):
    count = mesh.shape["dp"]
    plain = list(range(count))
    try:
        coords = [tuple(int(c) for c in d.coords) for d in mesh.devices[:, 0]]
    except (AttributeError, TypeError, IndexError):
        return plain
    axes = [k for k in range(len(coords[0])) if len({c[k] for c in coords}) > 1]
    if len(axes) != 2:
        return plain
    low = [min(c[k] for c in coords) for k in axes]
    spots = {(c[axes[0]] - low[0], c[axes[1]] - low[1]): i for i, c in enumerate(coords)}
    sizes = [len({c[k] for c in coords}) for k in axes]
    if sizes[0] * sizes[1] != count or len(spots) != count:
        return plain
    if sizes[0] % 2 == 0:
        first, second, swap = sizes[0], sizes[1], False
    elif sizes[1] % 2 == 0:
        first, second, swap = sizes[1], sizes[0], True
    else:
        return plain
    path = [(0, 0)]
    for a in range(first):
        cols = range(1, second) if a % 2 == 0 else range(second - 1, 0, -1)
        path += [(a, b) for b in cols]
    path += [(a, 0) for a in range(first - 1, 0, -1)]
    if swap:
        path = [(b, a) for a, b in path]
    cycle = [spots.get(p) for p in path]
    if None in cycle or sorted(cycle) != plain:
        return plain
    return cycle


def ring_gather(block, ring, cuts):
    count = len(ring)
    me = lax.axis_index("dp")
    my_pos = jnp.asarray([ring.index(i) for i in range(count)], jnp.int32)[me]
    order = jnp.asarray(ring, jnp.int32)
    forward = [(ring[p], ring[(p + 1) % count]) for p in range(count)]
    backward = [(ring[p], ring[(p - 1) % count]) for p in range(count)]
    edges = [0] + list(cuts) + [block.shape[-1]]
    spans = list(zip(edges[:-1], edges[1:]))
    outs = [jnp.zeros((count,) + block.shape[:-1] + (hi - lo,), block.dtype) for lo, hi in spans]

    def place(outs, piece, where):
        return [
            lax.dynamic_update_index_in_dim(out, piece[..., lo:hi], where, 0)
            for out, (lo, hi) in zip(outs, spans)
        ]

    outs = place(outs, block, me)
    ahead = behind = block
    far = count // 2
    for step in range(1, far + 1):
        if step == far and count % 2 == 0:
            rows = block.shape[0] // 2
            where = order[(my_pos - step) % count]
            front = lax.ppermute(ahead[:rows], "dp", forward)
            back = lax.ppermute(behind[rows:], "dp", backward)
            outs = [
                lax.dynamic_update_slice(
                    lax.dynamic_update_slice(out, front[None, :, lo:hi], (where, 0, 0)),
                    back[None, :, lo:hi],
                    (where, rows, 0),
                )
                for out, (lo, hi) in zip(outs, spans)
            ]
            break
        ahead = lax.ppermute(ahead, "dp", forward)
        outs = place(outs, ahead, order[(my_pos - step) % count])
        if step < far or count % 2 == 1:
            behind = lax.ppermute(behind, "dp", backward)
            outs = place(outs, behind, order[(my_pos + step) % count])
    return outs


def after(token, value):
    return lax.optimization_barrier((token, value))[1]


def attend(query_rows, key_rows, value_rows, seg_all, head_size):
    group_rows = query_rows.shape[0]
    block_rows = 512
    heads_here = query_rows.shape[1] // head_size
    queries = query_rows.reshape(group_rows, heads_here, head_size)
    keys = key_rows.reshape(group_rows, heads_here, head_size)
    values = value_rows.reshape(group_rows, heads_here, head_size)
    blocks = group_rows // block_rows
    scale = 1.0 / head_size**0.5

    def one_block(block_data):
        query_block, seg_block = block_data
        scores = (
            jnp.einsum("qhe,khe->hqk", query_block, keys, preferred_element_type=jnp.float32)
            * scale
        )
        allowed = seg_block[:, None] == seg_all[None, :]
        scores = jnp.where(allowed[None], scores, -1e30)
        top_score = jnp.max(scores, axis=-1, keepdims=True)
        weights = jnp.exp(scores - top_score)
        probs = (weights / jnp.sum(weights, axis=-1, keepdims=True)).astype(jnp.bfloat16)
        mixed = jnp.einsum("hqk,khe->qhe", probs, values, preferred_element_type=jnp.float32)
        return mixed.astype(jnp.bfloat16).reshape(block_rows, heads_here * head_size)

    result = lax.map(
        one_block,
        (
            queries.reshape(blocks, block_rows, heads_here, head_size),
            seg_all.reshape(blocks, block_rows),
        ),
    )
    return result.reshape(group_rows, heads_here * head_size)


def depthwise(padded, kernel, seg_here, seg_near, count):
    total_acc = jnp.zeros((count, padded.shape[1]), jnp.float32)
    for tap_index in range(kernel.shape[0]):
        window = padded[tap_index : tap_index + count].astype(jnp.float32)
        same = (seg_near[tap_index : tap_index + count] == seg_here)[:, None]
        total_acc = total_acc + jnp.where(same, window * kernel[tap_index].astype(jnp.float32), 0.0)
    return jax.nn.silu(total_acc).astype(jnp.bfloat16)


def on_device(ring, paired, frames, lengths, ln1_gain, ln2_gain, w_qkv, w_out, w_glu, dw_kernel, w_proj):
    frame_rows = frames.shape[1]
    model_width = frames.shape[2]
    seq_count = lax.axis_size("seq")
    group_rows = frame_rows * seq_count
    group_width = model_width // seq_count
    kernel_reach = dw_kernel.shape[0] // 2
    qkv_local = w_qkv.reshape(w_qkv.shape[0], 3 * group_width)
    query_parts, key_parts, value_parts_a, out_parts = ring_gather(
        jnp.concatenate([qkv_local, w_out.T], axis=1),
        ring,
        [group_width, 2 * group_width, 3 * group_width],
    )
    query_matrix = query_parts.reshape(model_width, group_width)
    kv_matrices = [p.reshape(model_width, group_width) for p in (key_parts, value_parts_a)]
    out_cols = out_parts.reshape(model_width, w_out.shape[0])
    glu_rows = w_glu.shape[0]
    glu_local = w_glu.reshape(glu_rows, 2 * group_width)
    value_parts, gate_parts, proj_parts = ring_gather(
        after(out_parts, jnp.concatenate([glu_local, w_proj.T], axis=1)),
        ring,
        [group_width, 2 * group_width],
    )
    value_matrix = value_parts.reshape(model_width, group_width)
    gate_matrix = gate_parts.reshape(model_width, group_width)
    proj_cols = proj_parts.reshape(model_width, w_proj.shape[0])
    inputs = frames[0].astype(jnp.float32)
    record_ends = jnp.cumsum(lengths[0])
    seg_all = segment_of(record_ends, jnp.arange(group_rows, dtype=jnp.int32))
    normed1 = layer_norm(inputs, ln1_gain)
    group_normed = seq_gather(normed1, paired).reshape(group_rows, model_width)
    query_rows, key_rows, value_rows = [
        jnp.dot(group_normed, m, preferred_element_type=jnp.float32).astype(jnp.bfloat16)
        for m in [query_matrix] + kv_matrices
    ]
    attended = attend(query_rows, key_rows, value_rows, seg_all, HD)
    attn_sum = seq_scatter_sum(
        jnp.dot(attended, out_cols.T, preferred_element_type=jnp.float32).astype(jnp.bfloat16),
        paired,
    )
    middle = (inputs + attn_sum).astype(jnp.bfloat16)
    normed2 = layer_norm(middle.astype(jnp.float32), ln2_gain)
    shard_piece = seq_gather(normed2, paired).reshape(group_rows, model_width)
    glu_value = jnp.dot(shard_piece, value_matrix, preferred_element_type=jnp.float32)
    glu_gate = jnp.dot(shard_piece, gate_matrix, preferred_element_type=jnp.float32)
    gated = (glu_value * jax.nn.sigmoid(glu_gate)).astype(jnp.bfloat16)
    padded = jnp.pad(gated, ((kernel_reach, kernel_reach), (0, 0)))
    near_positions = jnp.arange(-kernel_reach, group_rows + kernel_reach, dtype=jnp.int32)
    activated = depthwise(
        padded, dw_kernel, seg_all, segment_of(record_ends, near_positions), group_rows
    )
    activated = lax.optimization_barrier(activated)
    conv_out = seq_scatter_sum(
        jnp.dot(activated, proj_cols.T, preferred_element_type=jnp.float32).astype(jnp.bfloat16),
        paired,
    )
    results = [(middle.astype(jnp.float32) + conv_out).astype(jnp.bfloat16)]
    return jnp.stack(results, axis=0)


def solution(mesh):
    in_specs = (
        P("dp", "seq", None),
        P("dp", None),
        P(),
        P(),
        P("dp", None, "seq"),
        P("seq", "dp"),
        P("dp", None, "seq"),
        P(None, "seq"),
        P("seq", "dp"),
    )
    out_specs = P("dp", "seq", None)
    return jax.shard_map(
        functools.partial(on_device, dp_ring(mesh), cores_paired(mesh)), mesh=mesh, in_specs=in_specs, out_specs=out_specs, check_vma=False
    )
```

```python
import functools

import jax
import jax.numpy as jnp
from jax import lax
from jax.sharding import PartitionSpec as P

HD = 96


def layer_norm(values, gain_vec):
    mean_value = jnp.mean(values, axis=-1, keepdims=True)
    centered = values - mean_value
    variance = jnp.mean(centered * centered, axis=-1, keepdims=True)
    return (centered * lax.rsqrt(variance + 1e-05) * gain_vec).astype(jnp.bfloat16)


def segment_of(record_ends, positions):
    return jnp.sum((positions[:, None] >= record_ends[None, :]).astype(jnp.int32), axis=1)


def seq_gather(block, paired):
    count = lax.axis_size("seq")
    me = lax.axis_index("seq")
    out = jnp.zeros((count,) + block.shape, block.dtype)
    out = lax.dynamic_update_index_in_dim(out, block, me, 0)
    if not paired:
        for shift in range(1, count):
            got = lax.ppermute(block, "seq", [(i, (i + shift) % count) for i in range(count)])
            out = lax.dynamic_update_index_in_dim(out, got, (me - shift) % count, 0)
        return out
    half = count // 2
    mine = jnp.zeros((half,) + block.shape, block.dtype)
    mine = lax.dynamic_update_index_in_dim(mine, block, me // 2, 0)
    for shift in range(1, half):
        got = lax.ppermute(
            block, "seq", [(i, (i + 2 * shift) % count) for i in range(count)]
        )
        src_dev = (me - 2 * shift) % count
        mine = lax.dynamic_update_index_in_dim(mine, got, src_dev // 2, 0)
        out = lax.dynamic_update_index_in_dim(out, got, src_dev, 0)
    other = lax.ppermute(mine, "seq", [(i, i ^ 1) for i in range(count)])
    partner = me ^ 1
    for k in range(half):
        out = lax.dynamic_update_index_in_dim(out, other[k], 2 * k + partner % 2, 0)
    return out


def cores_paired(mesh):
    count = mesh.shape["seq"]
    if count % 2:
        return False
    try:
        row = mesh.devices[0]
        return all(
            tuple(row[2 * k].coords) == tuple(row[2 * k + 1].coords) for k in range(count // 2)
        )
    except (AttributeError, TypeError, IndexError):
        return False


def seq_scatter_sum(full, paired):
    count = lax.axis_size("seq")
    me = lax.axis_index("seq")
    rows = full.shape[0] // count
    if not paired:
        total = lax.dynamic_slice_in_dim(full, me * rows, rows, axis=0).astype(jnp.float32)
        for shift in range(1, count):
            piece = lax.dynamic_slice_in_dim(full, ((me + shift) % count) * rows, rows, axis=0)
            got = lax.ppermute(piece, "seq", [(i, (i + shift) % count) for i in range(count)])
            total = total + got.astype(jnp.float32)
        return total
    half = count // 2
    core = me % 2
    quads = full.reshape(half, 2, rows, full.shape[1])
    mine = lax.dynamic_index_in_dim(quads, core, axis=1, keepdims=False)
    theirs = lax.dynamic_index_in_dim(quads, 1 - core, axis=1, keepdims=False)
    got = lax.ppermute(theirs, "seq", [(i, i ^ 1) for i in range(count)])
    chip_sum = mine.astype(jnp.float32) + got.astype(jnp.float32)
    here = me // 2
    total = lax.dynamic_index_in_dim(chip_sum, here, axis=0, keepdims=False)
    for shift in range(1, half):
        piece = lax.dynamic_index_in_dim(chip_sum, (here + shift) % half, axis=0, keepdims=False)
        got = lax.ppermute(
            piece.astype(jnp.bfloat16),
            "seq",
            [(i, (i + 2 * shift) % count) for i in range(count)],
        )
        total = total + got.astype(jnp.float32)
    return total


def dp_ring(mesh):
    count = mesh.shape["dp"]
    plain = list(range(count))
    try:
        coords = [tuple(int(c) for c in d.coords) for d in mesh.devices[:, 0]]
    except (AttributeError, TypeError, IndexError):
        return plain
    axes = [k for k in range(len(coords[0])) if len({c[k] for c in coords}) > 1]
    if len(axes) != 2:
        return plain
    low = [min(c[k] for c in coords) for k in axes]
    spots = {(c[axes[0]] - low[0], c[axes[1]] - low[1]): i for i, c in enumerate(coords)}
    sizes = [len({c[k] for c in coords}) for k in axes]
    if sizes[0] * sizes[1] != count or len(spots) != count:
        return plain
    if sizes[0] % 2 == 0:
        first, second, swap = sizes[0], sizes[1], False
    elif sizes[1] % 2 == 0:
        first, second, swap = sizes[1], sizes[0], True
    else:
        return plain
    path = [(0, 0)]
    for a in range(first):
        cols = range(1, second) if a % 2 == 0 else range(second - 1, 0, -1)
        path += [(a, b) for b in cols]
    path += [(a, 0) for a in range(first - 1, 0, -1)]
    if swap:
        path = [(b, a) for a, b in path]
    cycle = [spots.get(p) for p in path]
    if None in cycle or sorted(cycle) != plain:
        return plain
    return cycle


def ring_gather(block, ring, cuts):
    count = len(ring)
    me = lax.axis_index("dp")
    my_pos = jnp.asarray([ring.index(i) for i in range(count)], jnp.int32)[me]
    order = jnp.asarray(ring, jnp.int32)
    forward = [(ring[p], ring[(p + 1) % count]) for p in range(count)]
    backward = [(ring[p], ring[(p - 1) % count]) for p in range(count)]
    edges = [0] + list(cuts) + [block.shape[-1]]
    spans = list(zip(edges[:-1], edges[1:]))
    outs = [jnp.zeros((count,) + block.shape[:-1] + (hi - lo,), block.dtype) for lo, hi in spans]

    def place(outs, piece, where):
        return [
            lax.dynamic_update_index_in_dim(out, piece[..., lo:hi], where, 0)
            for out, (lo, hi) in zip(outs, spans)
        ]

    outs = place(outs, block, me)
    ahead = behind = block
    far = count // 2
    for step in range(1, far + 1):
        if step == far and count % 2 == 0:
            rows = block.shape[0] // 2
            where = order[(my_pos - step) % count]
            front = lax.ppermute(ahead[:rows], "dp", forward)
            back = lax.ppermute(behind[rows:], "dp", backward)
            outs = [
                lax.dynamic_update_slice(
                    lax.dynamic_update_slice(out, front[None, :, lo:hi], (where, 0, 0)),
                    back[None, :, lo:hi],
                    (where, rows, 0),
                )
                for out, (lo, hi) in zip(outs, spans)
            ]
            break
        ahead = lax.ppermute(ahead, "dp", forward)
        outs = place(outs, ahead, order[(my_pos - step) % count])
        if step < far or count % 2 == 1:
            behind = lax.ppermute(behind, "dp", backward)
            outs = place(outs, behind, order[(my_pos + step) % count])
    return outs


def after(token, value):
    return lax.optimization_barrier((token, value))[1]


def attend(query_rows, key_rows, value_rows, seg_all, head_size):
    group_rows = query_rows.shape[0]
    block_rows = 512
    heads_here = query_rows.shape[1] // head_size
    queries = query_rows.reshape(group_rows, heads_here, head_size)
    keys = key_rows.reshape(group_rows, heads_here, head_size)
    values = value_rows.reshape(group_rows, heads_here, head_size)
    blocks = group_rows // block_rows
    scale = 1.0 / head_size**0.5

    def one_block(block_data):
        query_block, seg_block = block_data
        scores = (
            jnp.einsum("qhe,khe->hqk", query_block, keys, preferred_element_type=jnp.float32)
            * scale
        )
        allowed = seg_block[:, None] == seg_all[None, :]
        scores = jnp.where(allowed[None], scores, -1e30)
        top_score = jnp.max(scores, axis=-1, keepdims=True)
        weights = jnp.exp(scores - top_score)
        probs = (weights / jnp.sum(weights, axis=-1, keepdims=True)).astype(jnp.bfloat16)
        mixed = jnp.einsum("hqk,khe->qhe", probs, values, preferred_element_type=jnp.float32)
        return mixed.astype(jnp.bfloat16).reshape(block_rows, heads_here * head_size)

    result = lax.map(
        one_block,
        (
            queries.reshape(blocks, block_rows, heads_here, head_size),
            seg_all.reshape(blocks, block_rows),
        ),
    )
    return result.reshape(group_rows, heads_here * head_size)


def depthwise(padded, kernel, seg_here, seg_near, count):
    total_acc = jnp.zeros((count, padded.shape[1]), jnp.float32)
    for tap_index in range(kernel.shape[0]):
        window = padded[tap_index : tap_index + count].astype(jnp.float32)
        same = (seg_near[tap_index : tap_index + count] == seg_here)[:, None]
        total_acc = total_acc + window * kernel[tap_index].astype(jnp.float32) * same.astype(
            jnp.float32
        )
    return jax.nn.silu(total_acc).astype(jnp.bfloat16)


def on_device(ring, paired, frames, lengths, ln1_gain, ln2_gain, w_qkv, w_out, w_glu, dw_kernel, w_proj):
    frame_rows = frames.shape[1]
    model_width = frames.shape[2]
    seq_count = lax.axis_size("seq")
    group_rows = frame_rows * seq_count
    group_width = model_width // seq_count
    kernel_reach = dw_kernel.shape[0] // 2
    qkv_local = w_qkv.reshape(w_qkv.shape[0], 3 * group_width)
    query_parts, key_parts, value_parts_a, out_parts = ring_gather(
        jnp.concatenate([qkv_local, w_out.T], axis=1),
        ring,
        [group_width, 2 * group_width, 3 * group_width],
    )
    query_matrix = query_parts.reshape(model_width, group_width)
    kv_matrices = [p.reshape(model_width, group_width) for p in (key_parts, value_parts_a)]
    out_cols = out_parts.reshape(model_width, w_out.shape[0])
    glu_rows = w_glu.shape[0]
    glu_local = w_glu.reshape(glu_rows, 2 * group_width)
    value_parts, gate_parts, proj_parts = ring_gather(
        after(out_parts, jnp.concatenate([glu_local, w_proj.T], axis=1)),
        ring,
        [group_width, 2 * group_width],
    )
    value_matrix = value_parts.reshape(model_width, group_width)
    gate_matrix = gate_parts.reshape(model_width, group_width)
    proj_cols = proj_parts.reshape(model_width, w_proj.shape[0])
    inputs = frames[0].astype(jnp.float32)
    record_ends = jnp.cumsum(lengths[0])
    seg_all = segment_of(record_ends, jnp.arange(group_rows, dtype=jnp.int32))
    normed1 = layer_norm(inputs, ln1_gain)
    group_normed = seq_gather(normed1, paired).reshape(group_rows, model_width)
    query_rows, key_rows, value_rows = [
        jnp.dot(group_normed, m, preferred_element_type=jnp.float32).astype(jnp.bfloat16)
        for m in [query_matrix] + kv_matrices
    ]
    attended = attend(query_rows, key_rows, value_rows, seg_all, HD)
    attn_sum = seq_scatter_sum(
        jnp.dot(attended, out_cols.T, preferred_element_type=jnp.float32).astype(jnp.bfloat16),
        paired,
    )
    middle = (inputs + attn_sum).astype(jnp.bfloat16)
    normed2 = layer_norm(middle.astype(jnp.float32), ln2_gain)
    shard_piece = seq_gather(normed2, paired).reshape(group_rows, model_width)
    glu_value = jnp.dot(shard_piece, value_matrix, preferred_element_type=jnp.float32)
    glu_gate = jnp.dot(shard_piece, gate_matrix, preferred_element_type=jnp.float32)
    gated = (glu_value * jax.nn.sigmoid(glu_gate)).astype(jnp.bfloat16)
    padded = jnp.pad(gated, ((kernel_reach, kernel_reach), (0, 0)))
    near_positions = jnp.arange(-kernel_reach, group_rows + kernel_reach, dtype=jnp.int32)
    activated = depthwise(
        padded, dw_kernel, seg_all, segment_of(record_ends, near_positions), group_rows
    )
    activated = lax.optimization_barrier(activated)
    conv_out = seq_scatter_sum(
        jnp.dot(activated, proj_cols.T, preferred_element_type=jnp.float32).astype(jnp.bfloat16),
        paired,
    )
    results = [(middle.astype(jnp.float32) + conv_out).astype(jnp.bfloat16)]
    return jnp.stack(results, axis=0)


def solution(mesh):
    in_specs = (
        P("dp", "seq", None),
        P("dp", None),
        P(),
        P(),
        P("dp", None, "seq"),
        P("seq", "dp"),
        P("dp", None, "seq"),
        P(None, "seq"),
        P("seq", "dp"),
    )
    out_specs = P("dp", "seq", None)
    return jax.shard_map(
        functools.partial(on_device, dp_ring(mesh), cores_paired(mesh)), mesh=mesh, in_specs=in_specs, out_specs=out_specs, check_vma=False
    )
```

```python
import functools

import jax
import jax.numpy as jnp
from jax import lax
from jax.sharding import PartitionSpec as P

HD = 96


def layer_norm(values, gain_vec):
    mean_value = jnp.mean(values, axis=-1, keepdims=True)
    centered = values - mean_value
    variance = jnp.mean(centered * centered, axis=-1, keepdims=True)
    return (centered * lax.rsqrt(variance + 1e-05) * gain_vec).astype(jnp.bfloat16)


def segment_of(record_ends, positions):
    return jnp.sum((positions[:, None] >= record_ends[None, :]).astype(jnp.int32), axis=1)


def seq_gather(block, paired):
    count = lax.axis_size("seq")
    me = lax.axis_index("seq")
    out = jnp.zeros((count,) + block.shape, block.dtype)
    out = lax.dynamic_update_index_in_dim(out, block, me, 0)
    if not paired:
        for shift in range(1, count):
            got = lax.ppermute(block, "seq", [(i, (i + shift) % count) for i in range(count)])
            out = lax.dynamic_update_index_in_dim(out, got, (me - shift) % count, 0)
        return out
    half = count // 2
    mine = jnp.zeros((half,) + block.shape, block.dtype)
    mine = lax.dynamic_update_index_in_dim(mine, block, me // 2, 0)
    for shift in range(1, half):
        got = lax.ppermute(
            block, "seq", [(i, (i + 2 * shift) % count) for i in range(count)]
        )
        src_dev = (me - 2 * shift) % count
        mine = lax.dynamic_update_index_in_dim(mine, got, src_dev // 2, 0)
        out = lax.dynamic_update_index_in_dim(out, got, src_dev, 0)
    other = lax.ppermute(mine, "seq", [(i, i ^ 1) for i in range(count)])
    partner = me ^ 1
    for k in range(half):
        out = lax.dynamic_update_index_in_dim(out, other[k], 2 * k + partner % 2, 0)
    return out


def cores_paired(mesh):
    count = mesh.shape["seq"]
    if count % 2:
        return False
    try:
        row = mesh.devices[0]
        return all(
            tuple(row[2 * k].coords) == tuple(row[2 * k + 1].coords) for k in range(count // 2)
        )
    except (AttributeError, TypeError, IndexError):
        return False


def seq_scatter_sum(full, paired):
    count = lax.axis_size("seq")
    me = lax.axis_index("seq")
    rows = full.shape[0] // count
    if not paired:
        total = lax.dynamic_slice_in_dim(full, me * rows, rows, axis=0).astype(jnp.float32)
        for shift in range(1, count):
            piece = lax.dynamic_slice_in_dim(full, ((me + shift) % count) * rows, rows, axis=0)
            got = lax.ppermute(piece, "seq", [(i, (i + shift) % count) for i in range(count)])
            total = total + got.astype(jnp.float32)
        return total
    half = count // 2
    core = me % 2
    quads = full.reshape(half, 2, rows, full.shape[1])
    mine = lax.dynamic_index_in_dim(quads, core, axis=1, keepdims=False)
    theirs = lax.dynamic_index_in_dim(quads, 1 - core, axis=1, keepdims=False)
    got = lax.ppermute(theirs, "seq", [(i, i ^ 1) for i in range(count)])
    chip_sum = mine.astype(jnp.float32) + got.astype(jnp.float32)
    here = me // 2
    total = lax.dynamic_index_in_dim(chip_sum, here, axis=0, keepdims=False)
    for shift in range(1, half):
        piece = lax.dynamic_index_in_dim(chip_sum, (here + shift) % half, axis=0, keepdims=False)
        got = lax.ppermute(
            piece.astype(jnp.bfloat16),
            "seq",
            [(i, (i + 2 * shift) % count) for i in range(count)],
        )
        total = total + got.astype(jnp.float32)
    return total


def dp_ring(mesh):
    count = mesh.shape["dp"]
    plain = list(range(count))
    try:
        coords = [tuple(int(c) for c in d.coords) for d in mesh.devices[:, 0]]
    except (AttributeError, TypeError, IndexError):
        return plain
    axes = [k for k in range(len(coords[0])) if len({c[k] for c in coords}) > 1]
    if len(axes) != 2:
        return plain
    low = [min(c[k] for c in coords) for k in axes]
    spots = {(c[axes[0]] - low[0], c[axes[1]] - low[1]): i for i, c in enumerate(coords)}
    sizes = [len({c[k] for c in coords}) for k in axes]
    if sizes[0] * sizes[1] != count or len(spots) != count:
        return plain
    if sizes[0] % 2 == 0:
        first, second, swap = sizes[0], sizes[1], False
    elif sizes[1] % 2 == 0:
        first, second, swap = sizes[1], sizes[0], True
    else:
        return plain
    path = [(0, 0)]
    for a in range(first):
        cols = range(1, second) if a % 2 == 0 else range(second - 1, 0, -1)
        path += [(a, b) for b in cols]
    path += [(a, 0) for a in range(first - 1, 0, -1)]
    if swap:
        path = [(b, a) for a, b in path]
    cycle = [spots.get(p) for p in path]
    if None in cycle or sorted(cycle) != plain:
        return plain
    return cycle


def ring_gather(block, ring, cuts):
    count = len(ring)
    me = lax.axis_index("dp")
    my_pos = jnp.asarray([ring.index(i) for i in range(count)], jnp.int32)[me]
    order = jnp.asarray(ring, jnp.int32)
    forward = [(ring[p], ring[(p + 1) % count]) for p in range(count)]
    backward = [(ring[p], ring[(p - 1) % count]) for p in range(count)]
    edges = [0] + list(cuts) + [block.shape[-1]]
    spans = list(zip(edges[:-1], edges[1:]))
    outs = [jnp.zeros((count,) + block.shape[:-1] + (hi - lo,), block.dtype) for lo, hi in spans]

    def place(outs, piece, where):
        return [
            lax.dynamic_update_index_in_dim(out, piece[..., lo:hi], where, 0)
            for out, (lo, hi) in zip(outs, spans)
        ]

    outs = place(outs, block, me)
    ahead = behind = block
    early = block
    far = count // 2
    for step in range(1, far + 1):
        if step == far and count % 2 == 0:
            early = ahead
            rows = block.shape[0] // 2
            where = order[(my_pos - step) % count]
            front = lax.ppermute(ahead[:rows], "dp", forward)
            back = lax.ppermute(behind[rows:], "dp", backward)
            outs = [
                lax.dynamic_update_slice(
                    lax.dynamic_update_slice(out, front[None, :, lo:hi], (where, 0, 0)),
                    back[None, :, lo:hi],
                    (where, rows, 0),
                )
                for out, (lo, hi) in zip(outs, spans)
            ]
            break
        ahead = lax.ppermute(ahead, "dp", forward)
        outs = place(outs, ahead, order[(my_pos - step) % count])
        if step < far or count % 2 == 1:
            behind = lax.ppermute(behind, "dp", backward)
            outs = place(outs, behind, order[(my_pos + step) % count])
        early = ahead
    return outs, early


def after(token, value):
    return lax.optimization_barrier((token, value))[1]


def attend(query_rows, key_rows, value_rows, seg_all, head_size):
    group_rows = query_rows.shape[0]
    block_rows = 512
    heads_here = query_rows.shape[1] // head_size
    queries = query_rows.reshape(group_rows, heads_here, head_size)
    keys = key_rows.reshape(group_rows, heads_here, head_size)
    values = value_rows.reshape(group_rows, heads_here, head_size)
    blocks = group_rows // block_rows
    scale = 1.0 / head_size**0.5

    def one_block(block_data):
        query_block, seg_block = block_data
        scores = (
            jnp.einsum("qhe,khe->hqk", query_block, keys, preferred_element_type=jnp.float32)
            * scale
        )
        allowed = seg_block[:, None] == seg_all[None, :]
        scores = jnp.where(allowed[None], scores, -1e30)
        top_score = jnp.max(scores, axis=-1, keepdims=True)
        weights = jnp.exp(scores - top_score)
        probs = (weights / jnp.sum(weights, axis=-1, keepdims=True)).astype(jnp.bfloat16)
        mixed = jnp.einsum("hqk,khe->qhe", probs, values, preferred_element_type=jnp.float32)
        return mixed.astype(jnp.bfloat16).reshape(block_rows, heads_here * head_size)

    result = lax.map(
        one_block,
        (
            queries.reshape(blocks, block_rows, heads_here, head_size),
            seg_all.reshape(blocks, block_rows),
        ),
    )
    return result.reshape(group_rows, heads_here * head_size)


def depthwise(padded, kernel, seg_here, seg_near, count):
    total_acc = jnp.zeros((count, padded.shape[1]), jnp.float32)
    for tap_index in range(kernel.shape[0]):
        window = padded[tap_index : tap_index + count].astype(jnp.float32)
        same = (seg_near[tap_index : tap_index + count] == seg_here)[:, None]
        total_acc = total_acc + window * kernel[tap_index].astype(jnp.float32) * same.astype(
            jnp.float32
        )
    return jax.nn.silu(total_acc).astype(jnp.bfloat16)


def on_device(ring, paired, frames, lengths, ln1_gain, ln2_gain, w_qkv, w_out, w_glu, dw_kernel, w_proj):
    frame_rows = frames.shape[1]
    model_width = frames.shape[2]
    seq_count = lax.axis_size("seq")
    group_rows = frame_rows * seq_count
    group_width = model_width // seq_count
    kernel_reach = dw_kernel.shape[0] // 2
    qkv_local = w_qkv.reshape(w_qkv.shape[0], 3 * group_width)
    (query_parts, key_parts, value_parts_a, out_parts), first_early = ring_gather(
        jnp.concatenate([qkv_local, w_out.T], axis=1),
        ring,
        [group_width, 2 * group_width, 3 * group_width],
    )
    query_matrix = query_parts.reshape(model_width, group_width)
    kv_matrices = [p.reshape(model_width, group_width) for p in (key_parts, value_parts_a)]
    out_cols = out_parts.reshape(model_width, w_out.shape[0])
    glu_rows = w_glu.shape[0]
    glu_local = w_glu.reshape(glu_rows, 2 * group_width)
    (value_parts, gate_parts, proj_parts), _ = ring_gather(
        after(first_early, jnp.concatenate([glu_local, w_proj.T], axis=1)),
        ring,
        [group_width, 2 * group_width],
    )
    value_matrix = value_parts.reshape(model_width, group_width)
    gate_matrix = gate_parts.reshape(model_width, group_width)
    proj_cols = proj_parts.reshape(model_width, w_proj.shape[0])
    inputs = frames[0].astype(jnp.float32)
    record_ends = jnp.cumsum(lengths[0])
    seg_all = segment_of(record_ends, jnp.arange(group_rows, dtype=jnp.int32))
    normed1 = layer_norm(inputs, ln1_gain)
    group_normed = seq_gather(normed1, paired).reshape(group_rows, model_width)
    query_rows, key_rows, value_rows = [
        jnp.dot(group_normed, m, preferred_element_type=jnp.float32).astype(jnp.bfloat16)
        for m in [query_matrix] + kv_matrices
    ]
    attended = attend(query_rows, key_rows, value_rows, seg_all, HD)
    attn_sum = seq_scatter_sum(
        jnp.dot(attended, out_cols.T, preferred_element_type=jnp.float32).astype(jnp.bfloat16),
        paired,
    )
    middle = (inputs + attn_sum).astype(jnp.bfloat16)
    normed2 = layer_norm(middle.astype(jnp.float32), ln2_gain)
    shard_piece = seq_gather(normed2, paired).reshape(group_rows, model_width)
    glu_value = jnp.dot(shard_piece, value_matrix, preferred_element_type=jnp.float32)
    glu_gate = jnp.dot(shard_piece, gate_matrix, preferred_element_type=jnp.float32)
    gated = (glu_value * jax.nn.sigmoid(glu_gate)).astype(jnp.bfloat16)
    padded = jnp.pad(gated, ((kernel_reach, kernel_reach), (0, 0)))
    near_positions = jnp.arange(-kernel_reach, group_rows + kernel_reach, dtype=jnp.int32)
    activated = depthwise(
        padded, dw_kernel, seg_all, segment_of(record_ends, near_positions), group_rows
    )
    activated = lax.optimization_barrier(activated)
    conv_out = seq_scatter_sum(
        jnp.dot(activated, proj_cols.T, preferred_element_type=jnp.float32).astype(jnp.bfloat16),
        paired,
    )
    results = [(middle.astype(jnp.float32) + conv_out).astype(jnp.bfloat16)]
    return jnp.stack(results, axis=0)


def solution(mesh):
    in_specs = (
        P("dp", "seq", None),
        P("dp", None),
        P(),
        P(),
        P("dp", None, "seq"),
        P("seq", "dp"),
        P("dp", None, "seq"),
        P(None, "seq"),
        P("seq", "dp"),
    )
    out_specs = P("dp", "seq", None)
    return jax.shard_map(
        functools.partial(on_device, dp_ring(mesh), cores_paired(mesh)), mesh=mesh, in_specs=in_specs, out_specs=out_specs, check_vma=False
    )
```
